32 devices in a mesh: groups: 2 (over y), replica: 4 (over z), tensor: 4 (over x, core).
Axes of the slice: x: 2, y: 2, z: 4, core: 2. Of those that a mesh axis runs over, the one named last changes fastest.
Arguments:
- queries: bfloat16 [8, 128, 8192], P(('groups', 'replica'), None, 'tensor'), parts along dimension 0, may hold values from -12 to 12
- suffix_kv: bfloat16 [8, 2, 128, 1024], P(('groups', 'replica'), None, None, 'tensor'), parts along dimension 0, may hold values from -12 to 12
- page_pool: bfloat16 [96, 2, 128, 1024], P(('groups', 'replica'), None, 'tensor'), parts along dimension 0, may hold values from -6 to 6
- offsets: int32 [8, 8], P('groups'), parts along dimension 0, may hold values from 1 to 3, as said below
- slots: int32 [8, 8], P('groups'), parts along dimension 0, may hold values from 0 to 11, as said below
- prefix_len: int32 [8], P('groups'), parts along dimension 0, may hold values from 1 to 1024, 2048 in all
Outputs:
- attended: bfloat16 [8, 128, 8192], P(('groups', 'replica'), None, 'tensor'), parts along dimension 0
The draws below stay inside these ranges and needn't reach their ends.
There are 2 independent parts, one for each index of `groups`. The reference program is written for one: setup_inputs(seed, part) draws one part's arguments, and reference() takes and returns one part's arrays. A program takes and returns all parts, laid end to end along the dimension named above; each array names one. Nothing has to cross between parts.
Inputs may be any that keep to these rules, and one draw needn't show every extreme that they name: Page p of request r is held by replica (r - offsets[r, p]) mod 4; one request takes at most 4 pages from one holder, and exactly 4 from some holder. `slots`: the prefix pages of one request are distinct pool entries. `prefix_len`: the longest prefix fills all 8 pages.
All inputs are finite; a program needn't handle non-finite values.
Results may differ from the reference program's by a relative error of at most 0.0034.
Values may be sent and summed in bfloat16 or wider, within the bound.
No kernel may reach another device: no remote copies, remote signals or barrier semaphores. Data moves between devices by JAX's collectives and lax.ppermute only.
A program may use at most 64 MiB of HBM per device.

```python
import math
import jax
import jax.numpy as jnp
import numpy as np
from jax import lax

HEADS = 64
KV_HEADS = 8
HEAD_DIM = 128
PAGE = 128
SUF = 128
PAGES = 8
REPLICAS = 4
SPAN = 3
CAP = 4
POOL = 12


def draw_suffix_kv(key, part):
    shape = (REPLICAS, 2, SUF, KV_HEADS * HEAD_DIM)
    base = jax.random.truncated_normal(jax.random.fold_in(key, 1), -6.0, 6.0, shape, jnp.float32)
    return base.astype(jnp.bfloat16)


def draw_queries(key, part):
    shape = (REPLICAS, SUF, HEADS * HEAD_DIM)
    base = 2.0 * jax.random.truncated_normal(jax.random.fold_in(key, 2), -5.0, 5.0, shape, jnp.float32)
    return base.astype(jnp.bfloat16)


def draw_offsets(key, part):
    total_slots = SPAN * CAP
    counter = jnp.arange(total_slots, dtype=jnp.int32)
    ranked = jax.random.randint(jax.random.fold_in(key, 3), (REPLICAS, total_slots), 0, 65536, jnp.int32) * total_slots + counter[None, :]
    filled = jax.random.randint(jax.random.fold_in(key, 4), (REPLICAS, 1), 0, SPAN, jnp.int32)
    boosted = ranked + (counter[None, :] // CAP == filled).astype(jnp.int32) * (1 << 24)
    unused, picked = lax.top_k(boosted, PAGES)
    return (picked // CAP + 1).astype(jnp.int32)


def draw_slots(key, part):
    offsets = draw_offsets(key, part)
    counter = jnp.arange(PAGES, dtype=jnp.int32)
    same_holder = offsets[:, :, None] == offsets[:, None, :]
    earlier = counter[None, None, :] < counter[None, :, None]
    ranking = jnp.sum((same_holder & earlier).astype(jnp.int32), axis=2)
    places = (offsets - 1) * CAP + ranking
    pool_counter = jnp.arange(POOL, dtype=jnp.int32)
    scores = jax.random.randint(jax.random.fold_in(key, 11), (REPLICAS, POOL), 0, 65536, jnp.int32) * POOL + pool_counter[None, :]
    unused, perm = lax.top_k(scores, POOL)
    chosen = jnp.take_along_axis(perm, places, axis=1)
    first = chosen[:, :1]
    return ((chosen - first + POOL - 1) % POOL).astype(jnp.int32)


def level_of(stream_key, extent, pieces, low, largest):
    level, own = 1.0, jax.random.fold_in(stream_key, 6)
    for dim, shards_of in pieces:
        steps = jnp.exp(jax.random.uniform(jax.random.fold_in(own, dim), (shards_of,), jnp.float32, low / len(pieces), largest / len(pieces)))
        level = level * jnp.repeat(steps, extent[dim] // shards_of).reshape([-1 if axis == dim else 1 for axis in range(len(extent))])
    return level


def profile(amount, total, bound, slope):
    portions = [(1 << 20) // math.isqrt(grade ** slope) + 1 for grade in range(2, amount + 1)]
    rest, counts = total - bound - (amount - 1), [1] * (amount - 1)
    while rest > 0:
        movable = [i for i in range(amount - 1) if counts[i] < bound]
        mass, budget = sum([portions[i] for i in movable]), rest
        for i in movable:
            extra = min(bound - counts[i], max(1, budget * portions[i] // mass), rest)
            counts[i] = counts[i] + extra
            rest = rest - extra
    return np.array([bound] + counts)


def uneven(stream_key, number_of, total, reach, skew):
    if number_of == 2:
        one = jax.random.randint(stream_key, (), max(1, total - reach), min(reach, total - 1) + 1)
        return jnp.stack([one, total - one])
    lengths = jnp.asarray(profile(number_of, total, reach, skew), jnp.int32)
    pairs = (number_of - 1) // 2
    source_of, taker = lengths[1:1 + 2 * pairs:2], lengths[2:2 + 2 * pairs:2]
    slack = jnp.minimum(source_of - 1, reach - taker)
    moved = jax.random.randint(jax.random.fold_in(stream_key, 1), (pairs,), 0, 1 << 20) % (slack + 1)
    lengths = lengths.at[1:1 + 2 * pairs:2].set(source_of - moved).at[2:2 + 2 * pairs:2].set(taker + moved)
    return lengths[jax.random.permutation(jax.random.fold_in(stream_key, 2), number_of)]


def bell_draw(key, dims, width, limit, pieces=(), kind=jnp.bfloat16):
    drawn = jax.random.normal(key, dims, jnp.float32) * width
    if len(pieces) > 0:
        drawn = level_of(key, dims, pieces, -0.22, 0.18) * drawn
    return jnp.clip(drawn, min=-limit, max=limit).astype(kind)


def setup_inputs(seed: int = 0, part: int = 0) -> dict:
    key_list = jax.random.split(jax.random.key(seed), 7)
    own_keys = jax.random.split(jax.random.fold_in(key_list[6], part), 7)
    queries = draw_queries(jax.random.fold_in(jax.random.fold_in(key_list[6], part), 71), part)
    suffix_kv = draw_suffix_kv(jax.random.fold_in(jax.random.fold_in(key_list[6], part), 71), part)
    page_pool = bell_draw(own_keys[2], (REPLICAS * POOL, 2, PAGE, KV_HEADS * HEAD_DIM), 1.0, 6.0, ((0, 4), (2, 4)))
    offsets = draw_offsets(jax.random.fold_in(jax.random.fold_in(key_list[6], part), 71), part)
    slots = draw_slots(jax.random.fold_in(jax.random.fold_in(key_list[6], part), 71), part)
    prefix_len = uneven(own_keys[5], REPLICAS, REPLICAS * PAGES * PAGE // 2, PAGES * PAGE, 2).astype(jnp.int32)
    return dict(queries=queries, suffix_kv=suffix_kv, page_pool=page_pool, offsets=offsets, slots=slots, prefix_len=prefix_len)


def reference(queries, suffix_kv, page_pool, offsets, slots, prefix_len):
    group = HEADS // KV_HEADS
    prefix_rows = PAGES * PAGE

    def one_request(items):
        request, query_rows, suffix_rows, own_offsets, own_slots, own_length = items
        holders = (request - own_offsets) % REPLICAS
        fetched = jnp.take(page_pool, (holders * POOL + own_slots).astype(jnp.int32), axis=0)
        prefix_keys = fetched[:, 0].reshape(prefix_rows, KV_HEADS, HEAD_DIM)
        prefix_vals = fetched[:, 1].reshape(prefix_rows, KV_HEADS, HEAD_DIM)
        suffix_keys = suffix_rows[0].reshape(SUF, KV_HEADS, HEAD_DIM)
        suffix_vals = suffix_rows[1].reshape(SUF, KV_HEADS, HEAD_DIM)
        all_keys = jnp.concatenate([prefix_keys, suffix_keys], axis=0).astype(jnp.float32)
        all_vals = jnp.concatenate([prefix_vals, suffix_vals], axis=0).astype(jnp.float32)
        query_f = query_rows.reshape(SUF, KV_HEADS, group, HEAD_DIM).astype(jnp.float32)
        scores = jnp.einsum("qkgd,ckd->kgqc", query_f, all_keys) * (HEAD_DIM ** -0.5)
        positions = jnp.arange(prefix_rows + SUF, dtype=jnp.int32)[None, :]
        query_pos = jnp.arange(SUF, dtype=jnp.int32)[:, None]
        visible = jnp.where(positions < prefix_rows, positions < own_length, positions - prefix_rows <= query_pos)
        masked = jnp.where(visible, scores, -1.0e30)
        row_top = jnp.max(masked, axis=-1, keepdims=True)
        weights = jnp.where(visible, jnp.exp(masked - row_top), 0.0)
        denominator = jnp.sum(weights, axis=-1, keepdims=True)
        rounded = lax.optimization_barrier(weights.astype(jnp.bfloat16)).astype(jnp.float32)
        summed = jnp.einsum("kgqc,ckd->kgqd", rounded, all_vals) / denominator
        return summed.transpose(2, 0, 1, 3).reshape(SUF, HEADS * HEAD_DIM).astype(jnp.bfloat16)

    requests = jnp.arange(REPLICAS, dtype=jnp.int32)
    return lax.map(one_request, (requests, queries, suffix_kv, offsets, slots, prefix_len))
```

```python
import math

import jax
import jax.numpy as jnp
from jax import lax
from jax.sharding import PartitionSpec as P

HEADS = 64
KV_HEADS = 8
HEAD_DIM = 128


NEG_FILL = -1e30


def passed_along(value, axis, steps):
    count = lax.axis_size(axis)
    pairs = [(source, (source + steps) % count) for source in range(count)]
    return lax.ppermute(value, axis, pairs)


def absorb(state_now, scores, visible, values):
    run_max, run_sum, run_acc = state_now
    masked = jnp.where(visible, scores, NEG_FILL)
    new_max = jnp.maximum(run_max, jnp.max(masked, axis=-1))
    weights = jnp.where(visible, jnp.exp(masked - new_max[..., None]), 0.0)
    rescale = jnp.exp(run_max - new_max)
    run_sum = run_sum * rescale + jnp.sum(weights, axis=-1)
    update = jnp.einsum(
        "kgqc,kcd->kgqd", weights.astype(jnp.bfloat16), values, preferred_element_type=jnp.float32
    )
    run_acc = run_acc * rescale[..., None] + update
    return (new_max, run_sum, run_acc)


def slot_choice(offsets_rows, distances, slot_cap):
    matched = (offsets_rows == distances[:, None]).astype(jnp.int32)
    ranking = jnp.cumsum(matched, axis=1) - 1
    places = jnp.arange(slot_cap, dtype=jnp.int32)
    picked = matched[:, None, :] * (ranking[:, None, :] == places[None, :, None]).astype(jnp.int32)
    return picked


def pack_pages(pool_part, offsets, slots, holder, replicas, span_count, slot_cap, tensor_count):
    distances = jnp.arange(1, span_count + 1, dtype=jnp.int32)
    readers = (holder + distances) % replicas
    off_rows = jnp.take(offsets, readers, axis=0)
    slot_rows = jnp.take(slots, readers, axis=0)
    picked = slot_choice(off_rows, distances, slot_cap)
    chosen = jnp.sum(picked * slot_rows[:, None, :], axis=2)
    gathered = jnp.take(pool_part, chosen.reshape(-1), axis=0)
    pages, kv, rows, width = gathered.shape
    split = gathered.reshape(span_count, slot_cap, kv, rows, tensor_count, width // tensor_count)
    return split.transpose(0, 4, 1, 2, 3, 5)


def on_device(queries, suffix_kv, page_pool, offsets, slots, prefix_len):
    replicas = lax.axis_size("replica")
    tensor_count = lax.axis_size("tensor")
    reader = lax.axis_index("replica")
    span_count = min(8, replicas - 1)
    page_count = offsets.shape[1]
    slot_cap = (page_count + span_count - 1) // span_count + 1
    own_offsets = lax.dynamic_index_in_dim(offsets, reader, 0, keepdims=False)
    own_length = lax.dynamic_index_in_dim(prefix_len, reader, 0, keepdims=False)
    payload = pack_pages(
        page_pool, offsets, slots, reader, replicas, span_count, slot_cap, tensor_count
    )
    arrivals = []
    for distance in range(1, span_count + 1):
        arrivals.append(passed_along(payload[distance - 1], "replica", distance))

    page_rows = page_pool.shape[2] * tensor_count
    quarter = page_pool.shape[2]
    width = suffix_kv.shape[3]
    kv_local = width // HEAD_DIM
    group = HEADS // KV_HEADS
    suffix_rows = queries.shape[1]
    scale = HEAD_DIM ** (-0.5)
    query_heads = queries[0].reshape(suffix_rows, kv_local, group, HEAD_DIM)
    suffix_keys = suffix_kv[0, 0].reshape(suffix_rows, kv_local, HEAD_DIM).transpose(1, 0, 2)
    suffix_vals = suffix_kv[0, 1].reshape(suffix_rows, kv_local, HEAD_DIM).transpose(1, 0, 2)
    initial = (
        jnp.full((kv_local, group, suffix_rows), NEG_FILL, jnp.float32),
        jnp.zeros((kv_local, group, suffix_rows), jnp.float32),
        jnp.zeros((kv_local, group, suffix_rows, HEAD_DIM), jnp.float32),
    )
    suffix_scores = (
        jnp.einsum("qkgd,kcd->kgqc", query_heads, suffix_keys, preferred_element_type=jnp.float32)
        * scale
    )
    query_pos = jnp.arange(suffix_rows, dtype=jnp.int32)
    causal = query_pos[:, None] >= query_pos[None, :]
    state_now = absorb(initial, suffix_scores, causal, suffix_vals)

    distances = jnp.arange(1, span_count + 1, dtype=jnp.int32)
    own_picked = slot_choice(own_offsets[None, :], distances, slot_cap)
    page_ids = jnp.arange(page_count, dtype=jnp.int32)
    slot_page = jnp.sum(own_picked * page_ids[None, None, :], axis=2)
    slot_used = jnp.sum(own_picked, axis=2) > 0
    chunk_ids = jnp.arange(tensor_count, dtype=jnp.int32)
    row_ids = jnp.arange(quarter, dtype=jnp.int32)
    for distance in range(1, span_count + 1):
        local = lax.all_to_all(
            arrivals[distance - 1], "tensor", split_axis=0, concat_axis=0, tiled=True
        )
        keys_block = local[:, :, 0].reshape(tensor_count * slot_cap * quarter, kv_local, HEAD_DIM)
        vals_block = local[:, :, 1].reshape(tensor_count * slot_cap * quarter, kv_local, HEAD_DIM)
        position = (
            slot_page[distance - 1][None, :, None] * page_rows
            + chunk_ids[:, None, None] * quarter
            + row_ids[None, None, :]
        )
        visible = slot_used[distance - 1][None, :, None] & (position < own_length)
        visible = visible.reshape(-1)
        block_scores = (
            jnp.einsum(
                "qkgd,ckd->kgqc", query_heads, keys_block, preferred_element_type=jnp.float32
            )
            * scale
        )
        state_now = absorb(
            state_now, block_scores, visible[None, None, None, :], vals_block.transpose(1, 0, 2)
        )
    run_max, run_sum, run_acc = state_now
    result = run_acc / run_sum[..., None]
    result = result.transpose(2, 0, 1, 3).reshape(1, suffix_rows, kv_local * group * HEAD_DIM)
    return result.astype(jnp.bfloat16)


def solution(mesh):
    in_specs = (
        P(("groups", "replica"), None, "tensor"),
        P(("groups", "replica"), None, None, "tensor"),
        P(("groups", "replica"), None, "tensor", None),
        P("groups", None),
        P("groups", None),
        P("groups"),
    )
    out_specs = P(("groups", "replica"), None, "tensor")
    return jax.shard_map(
        on_device, mesh=mesh, in_specs=in_specs, out_specs=out_specs, check_vma=False
    )
```

```python
import functools
import math

import jax
import jax.numpy as jnp
from jax import lax
from jax.experimental import pallas as pl
from jax.sharding import PartitionSpec as P

HEADS = 64
KV_HEADS = 8
HEAD_DIM = 128


NEG_FILL = -1e30


def passed_along(value, axis, steps):
    count = lax.axis_size(axis)
    pairs = [(source, (source + steps) % count) for source in range(count)]
    return lax.ppermute(value, axis, pairs)


def absorb(state_now, scores, visible, values):
    run_max, run_sum, run_acc = state_now
    masked = jnp.where(visible, scores, NEG_FILL)
    new_max = jnp.maximum(run_max, jnp.max(masked, axis=-1))
    weights = jnp.where(visible, jnp.exp(masked - new_max[..., None]), 0.0)
    rescale = jnp.exp(run_max - new_max)
    run_sum = run_sum * rescale + jnp.sum(weights, axis=-1)
    update = jnp.einsum(
        "kgqc,kcd->kgqd", weights.astype(jnp.bfloat16), values, preferred_element_type=jnp.float32
    )
    run_acc = run_acc * rescale[..., None] + update
    return (new_max, run_sum, run_acc)


def slot_choice(offsets_rows, distances, slot_cap):
    matched = (offsets_rows == distances[:, None]).astype(jnp.int32)
    ranking = jnp.cumsum(matched, axis=1) - 1
    places = jnp.arange(slot_cap, dtype=jnp.int32)
    picked = matched[:, None, :] * (ranking[:, None, :] == places[None, :, None]).astype(jnp.int32)
    return picked


def pack_pages(pool_part, offsets, slots, holder, replicas, span_count, slot_cap, tensor_count):
    distances = jnp.arange(1, span_count + 1, dtype=jnp.int32)
    readers = (holder + distances) % replicas
    off_rows = jnp.take(offsets, readers, axis=0)
    slot_rows = jnp.take(slots, readers, axis=0)
    picked = slot_choice(off_rows, distances, slot_cap)
    chosen = jnp.sum(picked * slot_rows[:, None, :], axis=2)
    gathered = jnp.take(pool_part, chosen.reshape(-1), axis=0)
    pages, kv, rows, width = gathered.shape
    split = gathered.reshape(span_count, slot_cap, kv, rows, tensor_count, width // tensor_count)
    return split.transpose(0, 4, 1, 2, 3, 5)


def on_device(queries, suffix_kv, page_pool, offsets, slots, prefix_len):
    replicas = lax.axis_size("replica")
    tensor_count = lax.axis_size("tensor")
    reader = lax.axis_index("replica")
    span_count = min(8, replicas - 1)
    page_count = offsets.shape[1]
    slot_cap = (page_count + span_count - 1) // span_count + 1
    own_offsets = lax.dynamic_index_in_dim(offsets, reader, 0, keepdims=False)
    own_length = lax.dynamic_index_in_dim(prefix_len, reader, 0, keepdims=False)
    payload = pack_pages(
        page_pool, offsets, slots, reader, replicas, span_count, slot_cap, tensor_count
    )
    arrivals = []
    for distance in range(1, span_count + 1):
        arrivals.append(passed_along(payload[distance - 1], "replica", distance))

    page_rows = page_pool.shape[2] * tensor_count
    quarter = page_pool.shape[2]
    suffix_rows = queries.shape[1]

    distances = jnp.arange(1, span_count + 1, dtype=jnp.int32)
    own_picked = slot_choice(own_offsets[None, :], distances, slot_cap)
    page_ids = jnp.arange(page_count, dtype=jnp.int32)
    slot_page = jnp.sum(own_picked * page_ids[None, None, :], axis=2)
    slot_used = jnp.sum(own_picked, axis=2) > 0
    chunk_ids = jnp.arange(tensor_count, dtype=jnp.int32)
    row_ids = jnp.arange(quarter, dtype=jnp.int32)
    position = (
        slot_page[:, None, :, None] * page_rows
        + chunk_ids[None, :, None, None] * quarter
        + row_ids[None, None, None, :]
    )
    visible = slot_used[:, None, :, None] & (position < own_length)
    visible = visible.astype(jnp.int32).reshape(span_count, 1, -1)
    chunks = []
    for distance in range(1, span_count + 1):
        chunks.append(
            lax.all_to_all(arrivals[distance - 1], "tensor", split_axis=0, concat_axis=0, tiled=True)
        )
    result = attend(queries[0], suffix_kv[0], visible, chunks)
    return result.reshape(1, suffix_rows, result.shape[1])


def attention_kernel(chunk_count, q_ref, suf_ref, vis_ref, *rest):
    chunk_refs, o_ref = rest[:chunk_count], rest[chunk_count]
    rows, width = q_ref.shape
    kv_local = suf_ref.shape[2] // HEAD_DIM
    group = width // (kv_local * HEAD_DIM)
    scale = HEAD_DIM ** (-0.5)
    dims = (((1,), (1,)), ((), ()))
    row_pos = lax.broadcasted_iota(jnp.int32, (group * rows, rows), 0) % rows
    col_pos = lax.broadcasted_iota(jnp.int32, (group * rows, rows), 1)
    causal = col_pos <= row_pos
    for head in range(kv_local):
        lanes = pl.ds(head * HEAD_DIM, HEAD_DIM)
        q_all = jnp.concatenate(
            [q_ref[:, pl.ds((head * group + g) * HEAD_DIM, HEAD_DIM)] for g in range(group)], axis=0
        )
        keys = [suf_ref[0, :, lanes]]
        vals = [suf_ref[1, :, lanes]]
        masks = [causal]
        for c in range(chunk_count):
            ref = chunk_refs[c]
            keys.append(ref[:, :, 0, :, lanes].reshape(-1, HEAD_DIM))
            vals.append(ref[:, :, 1, :, lanes].reshape(-1, HEAD_DIM))
            masks.append(vis_ref[c] > 0)
        scores = []
        top = None
        for key, mask in zip(keys, masks):
            s = lax.dot_general(q_all, key, dims, preferred_element_type=jnp.float32) * scale
            s = jnp.where(mask, s, NEG_FILL)
            scores.append(s)
            part = jnp.max(s, axis=-1, keepdims=True)
            top = part if top is None else jnp.maximum(top, part)
        total = None
        acc = None
        for s, val, mask in zip(scores, vals, masks):
            w = jnp.where(mask, jnp.exp(s - top), 0.0)
            part = jnp.sum(w, axis=-1, keepdims=True)
            total = part if total is None else total + part
            pv = jnp.dot(w.astype(jnp.bfloat16), val, preferred_element_type=jnp.float32)
            acc = pv if acc is None else acc + pv
        out = (acc / total).astype(o_ref.dtype)
        for g in range(group):
            o_ref[:, pl.ds((head * group + g) * HEAD_DIM, HEAD_DIM)] = out[g * rows:(g + 1) * rows]


def attend(q, suf, visible, chunks):
    rows, width = q.shape
    keys_total = suf.shape[1] + sum(c.size // (2 * suf.shape[2]) for c in chunks)
    flops = 4 * rows * width * keys_total
    nbytes = 2 * (q.size * 2 + suf.size + sum(c.size for c in chunks))
    return pl.pallas_call(
        functools.partial(attention_kernel, len(chunks)),
        out_shape=jax.ShapeDtypeStruct((rows, width), jnp.bfloat16),
        cost_estimate=pl.CostEstimate(
            flops=flops, transcendentals=rows * (width // HEAD_DIM) * keys_total, bytes_accessed=nbytes
        ),
    )(q, suf, visible, *chunks)


def solution(mesh):
    in_specs = (
        P(("groups", "replica"), None, "tensor"),
        P(("groups", "replica"), None, None, "tensor"),
        P(("groups", "replica"), None, "tensor", None),
        P("groups", None),
        P("groups", None),
        P("groups"),
    )
    out_specs = P(("groups", "replica"), None, "tensor")
    return jax.shard_map(
        on_device, mesh=mesh, in_specs=in_specs, out_specs=out_specs, check_vma=False
    )
```

```python
import functools

import jax
import jax.numpy as jnp
from jax import lax
from jax.experimental import pallas as pl
from jax.experimental.pallas import tpu as pltpu
from jax.sharding import PartitionSpec as P

HEADS = 64
KV_HEADS = 8
HEAD_DIM = 128


NEG_FILL = -1e30


def slot_choice(offsets_rows, distances, slot_cap):
    matched = (offsets_rows == distances[:, None]).astype(jnp.int32)
    page_count = offsets_rows.shape[1]
    page_ids = jnp.arange(page_count, dtype=jnp.int32)
    earlier = (page_ids[None, :] < page_ids[:, None]).astype(jnp.int32)
    ranking = jnp.sum(matched[:, None, :] * earlier[None, :, :], axis=2)
    places = jnp.arange(slot_cap, dtype=jnp.int32)
    return matched[:, None, :] * (ranking[:, None, :] == places[None, :, None]).astype(jnp.int32)


def gather_kernel(cap, tensor_count, idx_ref, pool_ref, o_ref):
    me = idx_ref[idx_ref.shape[0] - 1]
    lanes = o_ref.shape[-1]
    for shift in range(tensor_count):
        start = pl.multiple_of(((me + shift) % tensor_count) * lanes, lanes)
        o_ref[0, shift, 0] = pool_ref[0, :, :, pl.ds(start, lanes)]


def pack_pages(pool_part, chosen, me, span_count, slot_cap, tensor_count):
    pages, kv, rows, width = pool_part.shape
    lanes = width // tensor_count
    table = jnp.concatenate([chosen.reshape(-1), me.reshape(1)]).astype(jnp.int32)
    grid_spec = pltpu.PrefetchScalarGridSpec(
        num_scalar_prefetch=1,
        grid=(span_count * slot_cap,),
        in_specs=[pl.BlockSpec((1, kv, rows, width), lambda i, idx: (idx[i], 0, 0, 0))],
        out_specs=pl.BlockSpec(
            (1, tensor_count, 1, kv, rows, lanes),
            lambda i, idx: (i // slot_cap, 0, i % slot_cap, 0, 0, 0),
        ),
    )
    nbytes = 2 * 2 * span_count * slot_cap * kv * rows * width
    return pl.pallas_call(
        functools.partial(gather_kernel, slot_cap, tensor_count),
        grid_spec=grid_spec,
        out_shape=jax.ShapeDtypeStruct(
            (span_count, tensor_count, slot_cap, kv, rows, lanes), pool_part.dtype
        ),
        cost_estimate=pl.CostEstimate(flops=0, transcendentals=0, bytes_accessed=nbytes),
    )(table, pool_part)


def on_device(queries, suffix_kv, page_pool, offsets, slots, prefix_len):
    replicas = lax.axis_size("replica")
    tensor_count = lax.axis_size("tensor")
    reader = lax.axis_index("replica")
    me = lax.axis_index("tensor")
    span_count = min(8, replicas - 1)
    page_count = offsets.shape[1]
    slot_cap = (page_count + span_count - 1) // span_count + 1
    distances = jnp.arange(1, span_count + 1, dtype=jnp.int32)

    off_twice = jnp.concatenate([offsets, offsets], axis=0)
    slots_twice = jnp.concatenate([slots, slots], axis=0)
    off_rows = lax.dynamic_slice_in_dim(off_twice, reader + 1, span_count, 0)
    slot_rows = lax.dynamic_slice_in_dim(slots_twice, reader + 1, span_count, 0)
    picked = slot_choice(off_rows, distances, slot_cap)
    chosen = jnp.sum(picked * slot_rows[:, None, :], axis=2)
    payload = pack_pages(page_pool, chosen, me, span_count, slot_cap, tensor_count)

    arrivals = []
    for distance in range(1, span_count + 1):
        for shift in range(tensor_count):
            pairs = []
            for source in range(replicas):
                for peer in range(tensor_count):
                    target = ((source + distance) % replicas) * tensor_count + (peer + shift) % tensor_count
                    pairs.append((source * tensor_count + peer, target))
            arrivals.append(lax.ppermute(payload[distance - 1, shift], ("replica", "tensor"), pairs))

    quarter = page_pool.shape[2]
    page_rows = quarter * tensor_count
    suffix_rows = queries.shape[1]
    own_offsets = lax.dynamic_index_in_dim(offsets, reader, 0, keepdims=False)
    own_length = lax.dynamic_index_in_dim(prefix_len, reader, 0, keepdims=False)
    own_picked = slot_choice(own_offsets[None, :], distances, slot_cap)
    page_ids = jnp.arange(page_count, dtype=jnp.int32)
    slot_page = jnp.sum(own_picked * page_ids[None, None, :], axis=2)
    slot_used = jnp.sum(own_picked, axis=2) > 0
    shifts = jnp.arange(tensor_count, dtype=jnp.int32)
    row_ids = jnp.arange(quarter, dtype=jnp.int32)
    position = (
        slot_page[:, None, :, None] * page_rows
        + ((me - shifts + tensor_count) % tensor_count)[None, :, None, None] * quarter
        + row_ids[None, None, None, :]
    )
    visible = slot_used[:, None, :, None] & (position < own_length)
    visible = visible.astype(jnp.int32).reshape(span_count * tensor_count, 1, -1)
    result = attend(queries[0], suffix_kv[0], visible, arrivals)
    return result.reshape(1, suffix_rows, result.shape[1])


def attention_kernel(chunk_count, q_ref, suf_ref, vis_ref, *rest):
    chunk_refs, o_ref = rest[:chunk_count], rest[chunk_count]
    rows, width = q_ref.shape
    kv_local = suf_ref.shape[2] // HEAD_DIM
    group = width // (kv_local * HEAD_DIM)
    scale = HEAD_DIM ** (-0.5)
    dims = (((1,), (1,)), ((), ()))
    row_pos = lax.broadcasted_iota(jnp.int32, (group * rows, rows), 0) % rows
    col_pos = lax.broadcasted_iota(jnp.int32, (group * rows, rows), 1)
    causal = col_pos <= row_pos
    for head in range(kv_local):
        lanes = pl.ds(head * HEAD_DIM, HEAD_DIM)
        q_all = jnp.concatenate(
            [q_ref[:, pl.ds((head * group + g) * HEAD_DIM, HEAD_DIM)] for g in range(group)], axis=0
        )
        keys = [suf_ref[0, :, lanes]]
        vals = [suf_ref[1, :, lanes]]
        masks = [causal]
        for c in range(chunk_count):
            ref = chunk_refs[c]
            keys.append(ref[:, 0, :, lanes].reshape(-1, HEAD_DIM))
            vals.append(ref[:, 1, :, lanes].reshape(-1, HEAD_DIM))
            masks.append(vis_ref[c] > 0)
        scores = []
        top = None
        for key, mask in zip(keys, masks):
            s = lax.dot_general(q_all, key, dims, preferred_element_type=jnp.float32) * scale
            s = jnp.where(mask, s, NEG_FILL)
            scores.append(s)
            part = jnp.max(s, axis=-1, keepdims=True)
            top = part if top is None else jnp.maximum(top, part)
        total = None
        acc = None
        for s, val, mask in zip(scores, vals, masks):
            w = jnp.where(mask, jnp.exp(s - top), 0.0)
            part = jnp.sum(w, axis=-1, keepdims=True)
            total = part if total is None else total + part
            pv = jnp.dot(w.astype(jnp.bfloat16), val, preferred_element_type=jnp.float32)
            acc = pv if acc is None else acc + pv
        out = (acc / total).astype(o_ref.dtype)
        for g in range(group):
            o_ref[:, pl.ds((head * group + g) * HEAD_DIM, HEAD_DIM)] = out[g * rows:(g + 1) * rows]


def attend(q, suf, visible, chunks):
    rows, width = q.shape
    keys_total = suf.shape[1] + sum(c.size // (2 * suf.shape[2]) for c in chunks)
    flops = 4 * rows * width * keys_total
    nbytes = 2 * (q.size * 2 + suf.size + sum(c.size for c in chunks))
    return pl.pallas_call(
        functools.partial(attention_kernel, len(chunks)),
        out_shape=jax.ShapeDtypeStruct((rows, width), jnp.bfloat16),
        cost_estimate=pl.CostEstimate(
            flops=flops, transcendentals=rows * (width // HEAD_DIM) * keys_total, bytes_accessed=nbytes
        ),
    )(q, suf, visible, *chunks)


def solution(mesh):
    in_specs = (
        P(("groups", "replica"), None, "tensor"),
        P(("groups", "replica"), None, None, "tensor"),
        P(("groups", "replica"), None, "tensor", None),
        P("groups", None),
        P("groups", None),
        P("groups"),
    )
    out_specs = P(("groups", "replica"), None, "tensor")
    return jax.shard_map(
        on_device, mesh=mesh, in_specs=in_specs, out_specs=out_specs, check_vma=False
    )
```

```python
import functools

import jax
import jax.numpy as jnp
from jax import lax
from jax.experimental import pallas as pl
from jax.experimental.pallas import tpu as pltpu
from jax.sharding import PartitionSpec as P

HEADS = 64
KV_HEADS = 8
HEAD_DIM = 128


NEG_FILL = -1e30


def slot_choice(offsets_rows, distances, slot_cap):
    matched = (offsets_rows == distances[:, None]).astype(jnp.int32)
    page_count = offsets_rows.shape[1]
    page_ids = jnp.arange(page_count, dtype=jnp.int32)
    earlier = (page_ids[None, :] < page_ids[:, None]).astype(jnp.int32)
    ranking = jnp.sum(matched[:, None, :] * earlier[None, :, :], axis=2)
    places = jnp.arange(slot_cap, dtype=jnp.int32)
    return matched[:, None, :] * (ranking[:, None, :] == places[None, :, None]).astype(jnp.int32)


def gather_kernel(span_count, slot_cap, tensor_count, idx_ref, pool_ref, *out_refs):
    me = idx_ref[span_count * slot_cap]
    lanes = out_refs[0].shape[-1]
    starts = [
        pl.multiple_of(((me + shift) % tensor_count) * lanes, lanes) for shift in range(tensor_count)
    ]
    for distance in range(span_count):
        for slot in range(slot_cap):
            page = idx_ref[distance * slot_cap + slot]
            for shift in range(tensor_count):
                out_refs[distance * tensor_count + shift][slot] = pool_ref[
                    page, :, :, pl.ds(starts[shift], lanes)
                ]


def pack_pages(pool_part, chosen, me, span_count, slot_cap, tensor_count):
    pages, kv, rows, width = pool_part.shape
    lanes = width // tensor_count
    table = jnp.concatenate([chosen.reshape(-1), me.reshape(1)]).astype(jnp.int32)
    piece = (slot_cap, kv, rows, lanes)
    count = span_count * tensor_count
    grid_spec = pltpu.PrefetchScalarGridSpec(
        num_scalar_prefetch=1,
        grid=(1,),
        in_specs=[pl.BlockSpec((pages, kv, rows, width), lambda i, idx: (0, 0, 0, 0))],
        out_specs=[pl.BlockSpec(piece, lambda i, idx: (0, 0, 0, 0)) for _ in range(count)],
    )
    nbytes = 2 * (pool_part.size + span_count * slot_cap * kv * rows * width)
    return pl.pallas_call(
        functools.partial(gather_kernel, span_count, slot_cap, tensor_count),
        grid_spec=grid_spec,
        out_shape=[jax.ShapeDtypeStruct(piece, pool_part.dtype) for _ in range(count)],
        cost_estimate=pl.CostEstimate(flops=0, transcendentals=0, bytes_accessed=nbytes),
    )(table, pool_part)


def on_device(queries, suffix_kv, page_pool, offsets, slots, prefix_len):
    replicas = lax.axis_size("replica")
    tensor_count = lax.axis_size("tensor")
    reader = lax.axis_index("replica")
    me = lax.axis_index("tensor")
    span_count = min(8, replicas - 1)
    page_count = offsets.shape[1]
    slot_cap = (page_count + span_count - 1) // span_count + 1
    distances = jnp.arange(1, span_count + 1, dtype=jnp.int32)

    off_twice = jnp.concatenate([offsets, offsets], axis=0)
    slots_twice = jnp.concatenate([slots, slots], axis=0)
    off_rows = lax.dynamic_slice_in_dim(off_twice, reader + 1, span_count, 0)
    slot_rows = lax.dynamic_slice_in_dim(slots_twice, reader + 1, span_count, 0)
    picked = slot_choice(off_rows, distances, slot_cap)
    chosen = jnp.sum(picked * slot_rows[:, None, :], axis=2)
    payload = pack_pages(page_pool, chosen, me, span_count, slot_cap, tensor_count)

    arrivals = []
    for distance in range(1, span_count + 1):
        for shift in range(tensor_count):
            pairs = []
            for source in range(replicas):
                for peer in range(tensor_count):
                    target = ((source + distance) % replicas) * tensor_count + (peer + shift) % tensor_count
                    pairs.append((source * tensor_count + peer, target))
            arrivals.append(lax.ppermute(payload[(distance - 1) * tensor_count + shift], ("replica", "tensor"), pairs))

    quarter = page_pool.shape[2]
    page_rows = quarter * tensor_count
    suffix_rows = queries.shape[1]
    own_offsets = lax.dynamic_index_in_dim(offsets, reader, 0, keepdims=False)
    own_length = lax.dynamic_index_in_dim(prefix_len, reader, 0, keepdims=False)
    own_picked = slot_choice(own_offsets[None, :], distances, slot_cap)
    page_ids = jnp.arange(page_count, dtype=jnp.int32)
    slot_page = jnp.sum(own_picked * page_ids[None, None, :], axis=2)
    slot_used = jnp.sum(own_picked, axis=2) > 0
    shifts = jnp.arange(tensor_count, dtype=jnp.int32)
    row_ids = jnp.arange(quarter, dtype=jnp.int32)
    position = (
        slot_page[:, None, :, None] * page_rows
        + ((me - shifts + tensor_count) % tensor_count)[None, :, None, None] * quarter
        + row_ids[None, None, None, :]
    )
    visible = slot_used[:, None, :, None] & (position < own_length)
    visible = visible.astype(jnp.int32).reshape(span_count * tensor_count, 1, -1)
    result = attend(queries[0], suffix_kv[0], visible, arrivals)
    return result.reshape(1, suffix_rows, result.shape[1])


def attention_kernel(chunk_count, q_ref, suf_ref, vis_ref, *rest):
    chunk_refs, o_ref = rest[:chunk_count], rest[chunk_count]
    rows, width = q_ref.shape
    kv_local = suf_ref.shape[2] // HEAD_DIM
    group = width // (kv_local * HEAD_DIM)
    scale = HEAD_DIM ** (-0.5)
    dims = (((1,), (1,)), ((), ()))
    row_pos = lax.broadcasted_iota(jnp.int32, (group * rows, rows), 0) % rows
    col_pos = lax.broadcasted_iota(jnp.int32, (group * rows, rows), 1)
    causal = col_pos <= row_pos
    for head in range(kv_local):
        lanes = pl.ds(head * HEAD_DIM, HEAD_DIM)
        q_all = jnp.concatenate(
            [q_ref[:, pl.ds((head * group + g) * HEAD_DIM, HEAD_DIM)] for g in range(group)], axis=0
        )
        keys = [suf_ref[0, :, lanes]]
        vals = [suf_ref[1, :, lanes]]
        masks = [causal]
        for c in range(chunk_count):
            ref = chunk_refs[c]
            keys.append(ref[:, 0, :, lanes].reshape(-1, HEAD_DIM))
            vals.append(ref[:, 1, :, lanes].reshape(-1, HEAD_DIM))
            masks.append(vis_ref[c] > 0)
        scores = []
        top = None
        for key, mask in zip(keys, masks):
            s = lax.dot_general(q_all, key, dims, preferred_element_type=jnp.float32) * scale
            s = jnp.where(mask, s, NEG_FILL)
            scores.append(s)
            part = jnp.max(s, axis=-1, keepdims=True)
            top = part if top is None else jnp.maximum(top, part)
        total = None
        acc = None
        for s, val, mask in zip(scores, vals, masks):
            w = jnp.where(mask, jnp.exp(s - top), 0.0)
            part = jnp.sum(w, axis=-1, keepdims=True)
            total = part if total is None else total + part
            pv = jnp.dot(w.astype(jnp.bfloat16), val, preferred_element_type=jnp.float32)
            acc = pv if acc is None else acc + pv
        out = (acc / total).astype(o_ref.dtype)
        for g in range(group):
            o_ref[:, pl.ds((head * group + g) * HEAD_DIM, HEAD_DIM)] = out[g * rows:(g + 1) * rows]


def attend(q, suf, visible, chunks):
    rows, width = q.shape
    keys_total = suf.shape[1] + sum(c.size // (2 * suf.shape[2]) for c in chunks)
    flops = 4 * rows * width * keys_total
    nbytes = 2 * (q.size * 2 + suf.size + sum(c.size for c in chunks))
    return pl.pallas_call(
        functools.partial(attention_kernel, len(chunks)),
        out_shape=jax.ShapeDtypeStruct((rows, width), jnp.bfloat16),
        cost_estimate=pl.CostEstimate(
            flops=flops, transcendentals=rows * (width // HEAD_DIM) * keys_total, bytes_accessed=nbytes
        ),
    )(q, suf, visible, *chunks)


def solution(mesh):
    in_specs = (
        P(("groups", "replica"), None, "tensor"),
        P(("groups", "replica"), None, None, "tensor"),
        P(("groups", "replica"), None, "tensor", None),
        P("groups", None),
        P("groups", None),
        P("groups"),
    )
    out_specs = P(("groups", "replica"), None, "tensor")
    return jax.shard_map(
        on_device, mesh=mesh, in_specs=in_specs, out_specs=out_specs, check_vma=False
    )
```

```python
import functools

import jax
import jax.numpy as jnp
from jax import lax
from jax.experimental import pallas as pl
from jax.experimental.pallas import tpu as pltpu
from jax.sharding import PartitionSpec as P

HEADS = 64
KV_HEADS = 8
HEAD_DIM = 128


NEG_FILL = -1e30


def slot_choice(offsets_rows, distances, slot_cap):
    matched = (offsets_rows == distances[:, None]).astype(jnp.int32)
    page_count = offsets_rows.shape[1]
    page_ids = jnp.arange(page_count, dtype=jnp.int32)
    earlier = (page_ids[None, :] < page_ids[:, None]).astype(jnp.int32)
    ranking = jnp.sum(matched[:, None, :] * earlier[None, :, :], axis=2)
    places = jnp.arange(slot_cap, dtype=jnp.int32)
    return matched[:, None, :] * (ranking[:, None, :] == places[None, :, None]).astype(jnp.int32)


def gather_kernel(span_count, slot_cap, tensor_count, idx_ref, pool_ref, *out_refs):
    me = idx_ref[span_count * slot_cap]
    lanes = out_refs[0].shape[-1]
    starts = [
        pl.multiple_of(((me + shift) % tensor_count) * lanes, lanes) for shift in range(tensor_count)
    ]
    for distance in range(span_count):
        for slot in range(slot_cap):
            page = idx_ref[distance * slot_cap + slot]
            for shift in range(tensor_count):
                out_refs[distance * tensor_count + shift][slot] = pool_ref[
                    page, :, :, pl.ds(starts[shift], lanes)
                ]


def pack_pages(pool_part, chosen, me, span_count, slot_cap, tensor_count):
    pages, kv, rows, width = pool_part.shape
    lanes = width // tensor_count
    table = jnp.concatenate([chosen.reshape(-1), me.reshape(1)]).astype(jnp.int32)
    piece = (slot_cap, kv, rows, lanes)
    count = span_count * tensor_count
    grid_spec = pltpu.PrefetchScalarGridSpec(
        num_scalar_prefetch=1,
        grid=(1,),
        in_specs=[pl.BlockSpec((pages, kv, rows, width), lambda i, idx: (0, 0, 0, 0))],
        out_specs=[pl.BlockSpec(piece, lambda i, idx: (0, 0, 0, 0)) for _ in range(count)],
    )
    nbytes = 2 * (pool_part.size + span_count * slot_cap * kv * rows * width)
    return pl.pallas_call(
        functools.partial(gather_kernel, span_count, slot_cap, tensor_count),
        grid_spec=grid_spec,
        out_shape=[jax.ShapeDtypeStruct(piece, pool_part.dtype) for _ in range(count)],
        cost_estimate=pl.CostEstimate(flops=0, transcendentals=0, bytes_accessed=nbytes),
    )(table, pool_part)


def on_device(queries, suffix_kv, page_pool, offsets, slots, prefix_len):
    replicas = lax.axis_size("replica")
    tensor_count = lax.axis_size("tensor")
    reader = lax.axis_index("replica")
    me = lax.axis_index("tensor")
    span_count = min(8, replicas - 1)
    page_count = offsets.shape[1]
    slot_cap = (page_count + span_count - 1) // span_count + 1
    distances = jnp.arange(1, span_count + 1, dtype=jnp.int32)

    off_twice = jnp.concatenate([offsets, offsets], axis=0)
    slots_twice = jnp.concatenate([slots, slots], axis=0)
    off_rows = lax.dynamic_slice_in_dim(off_twice, reader + 1, span_count, 0)
    slot_rows = lax.dynamic_slice_in_dim(slots_twice, reader + 1, span_count, 0)
    picked = slot_choice(off_rows, distances, slot_cap)
    chosen = jnp.sum(picked * slot_rows[:, None, :], axis=2)
    payload = pack_pages(page_pool, chosen, me, span_count, slot_cap, tensor_count)

    arrivals = []
    for distance in range(1, span_count + 1):
        for shift in range(tensor_count):
            pairs = []
            for source in range(replicas):
                for peer in range(tensor_count):
                    target = ((source + distance) % replicas) * tensor_count + (peer + shift) % tensor_count
                    pairs.append((source * tensor_count + peer, target))
            arrivals.append(lax.ppermute(payload[(distance - 1) * tensor_count + shift], ("replica", "tensor"), pairs))

    quarter = page_pool.shape[2]
    page_rows = quarter * tensor_count
    suffix_rows = queries.shape[1]
    own_offsets = lax.dynamic_index_in_dim(offsets, reader, 0, keepdims=False)
    own_length = lax.dynamic_index_in_dim(prefix_len, reader, 0, keepdims=False)
    own_picked = slot_choice(own_offsets[None, :], distances, slot_cap)
    page_ids = jnp.arange(page_count, dtype=jnp.int32)
    slot_page = jnp.sum(own_picked * page_ids[None, None, :], axis=2)
    slot_used = jnp.sum(own_picked, axis=2) > 0
    shifts = jnp.arange(tensor_count, dtype=jnp.int32)
    row_ids = jnp.arange(quarter, dtype=jnp.int32)
    position = (
        slot_page[:, :, None, None] * page_rows
        + ((me - shifts + tensor_count) % tensor_count)[None, None, :, None] * quarter
        + row_ids[None, None, None, :]
    )
    visible = slot_used[:, :, None, None] & (position < own_length)
    visible = visible.astype(jnp.int32).reshape(span_count * slot_cap, 1, -1)
    live = (slot_used & (slot_page * page_rows < own_length)).astype(jnp.int32).reshape(-1)
    result = attend(queries[0], suffix_kv[0], live, visible, arrivals, slot_cap, tensor_count)
    return result.reshape(1, suffix_rows, result.shape[1])


def attention_kernel(
    chunk_count, slot_cap, tensor_count, live_ref, q_ref, suf_ref, vis_ref, *rest
):
    chunk_refs = rest[:chunk_count]
    o_ref, top_ref, sum_ref, acc_ref = rest[chunk_count:]
    rows, width = q_ref.shape
    kv_local = suf_ref.shape[2] // HEAD_DIM
    group = width // (kv_local * HEAD_DIM)
    scale = HEAD_DIM ** (-0.5)
    dims = (((1,), (1,)), ((), ()))
    row_pos = lax.broadcasted_iota(jnp.int32, (group * rows, rows), 0) % rows
    col_pos = lax.broadcasted_iota(jnp.int32, (group * rows, rows), 1)
    causal = col_pos <= row_pos
    tile_count = chunk_count // tensor_count * slot_cap
    for head in range(kv_local):
        lanes = pl.ds(head * HEAD_DIM, HEAD_DIM)
        q_all = jnp.concatenate(
            [q_ref[:, pl.ds((head * group + g) * HEAD_DIM, HEAD_DIM)] for g in range(group)], axis=0
        )

        def tile(c, part):
            distance, slot = c // slot_cap, c % slot_cap
            return jnp.concatenate(
                [
                    chunk_refs[distance * tensor_count + s][slot, part, :, lanes]
                    for s in range(tensor_count)
                ],
                axis=0,
            )

        def raw_scores(key):
            return lax.dot_general(q_all, key, dims, preferred_element_type=jnp.float32)

        top_ref[...] = jnp.where(causal, raw_scores(suf_ref[0, :, lanes]), NEG_FILL)
        for c in range(tile_count):

            @pl.when(live_ref[c] > 0)
            def _():
                s = jnp.where(vis_ref[c] > 0, raw_scores(tile(c, 0)), NEG_FILL)
                top_ref[...] = jnp.maximum(top_ref[...], s)

        top = jnp.max(top_ref[...], axis=-1, keepdims=True) * scale

        def weights(raw, mask):
            return jnp.where(mask, jnp.exp(raw * scale - top), 0.0)

        w = weights(raw_scores(suf_ref[0, :, lanes]), causal)
        sum_ref[...] = w
        acc_ref[...] = jnp.dot(
            w.astype(jnp.bfloat16), suf_ref[1, :, lanes], preferred_element_type=jnp.float32
        )
        for c in range(tile_count):

            @pl.when(live_ref[c] > 0)
            def _():
                w = weights(raw_scores(tile(c, 0)), vis_ref[c] > 0)
                sum_ref[...] += w
                acc_ref[...] += jnp.dot(
                    w.astype(jnp.bfloat16), tile(c, 1), preferred_element_type=jnp.float32
                )

        total = jnp.sum(sum_ref[...], axis=-1, keepdims=True)
        out = (acc_ref[...] / total).astype(o_ref.dtype)
        for g in range(group):
            o_ref[:, pl.ds((head * group + g) * HEAD_DIM, HEAD_DIM)] = out[g * rows:(g + 1) * rows]


def attend(q, suf, live, visible, chunks, slot_cap, tensor_count):
    rows, width = q.shape
    kv_local = suf.shape[2] // HEAD_DIM
    group = width // (kv_local * HEAD_DIM)
    keys_total = suf.shape[1] + sum(c.size // (2 * suf.shape[2]) for c in chunks)
    flops = 6 * rows * width * keys_total
    nbytes = 2 * (q.size * 2 + suf.size + sum(c.size for c in chunks))

    def whole(a):
        return pl.BlockSpec(a.shape, lambda i, flags: (0,) * a.ndim)

    grid_spec = pltpu.PrefetchScalarGridSpec(
        num_scalar_prefetch=1,
        grid=(1,),
        in_specs=[whole(q), whole(suf), whole(visible)] + [whole(c) for c in chunks],
        out_specs=pl.BlockSpec((rows, width), lambda i, flags: (0, 0)),
        scratch_shapes=[pltpu.VMEM((group * rows, rows), jnp.float32)] * 2
        + [pltpu.VMEM((group * rows, HEAD_DIM), jnp.float32)],
    )
    return pl.pallas_call(
        functools.partial(attention_kernel, len(chunks), slot_cap, tensor_count),
        grid_spec=grid_spec,
        out_shape=jax.ShapeDtypeStruct((rows, width), jnp.bfloat16),
        cost_estimate=pl.CostEstimate(
            flops=flops, transcendentals=rows * (width // HEAD_DIM) * keys_total, bytes_accessed=nbytes
        ),
    )(live, q, suf, visible, *chunks)


def solution(mesh):
    in_specs = (
        P(("groups", "replica"), None, "tensor"),
        P(("groups", "replica"), None, None, "tensor"),
        P(("groups", "replica"), None, "tensor", None),
        P("groups", None),
        P("groups", None),
        P("groups"),
    )
    out_specs = P(("groups", "replica"), None, "tensor")
    return jax.shard_map(
        on_device, mesh=mesh, in_specs=in_specs, out_specs=out_specs, check_vma=False
    )
```

```python
import functools

import jax
import jax.numpy as jnp
from jax import lax
from jax.experimental import pallas as pl
from jax.experimental.pallas import tpu as pltpu
from jax.sharding import PartitionSpec as P

HEADS = 64
KV_HEADS = 8
HEAD_DIM = 128


NEG_FILL = -1e30


def slot_choice(offsets_rows, distances, slot_cap):
    matched = (offsets_rows == distances[:, None]).astype(jnp.int32)
    page_count = offsets_rows.shape[1]
    page_ids = jnp.arange(page_count, dtype=jnp.int32)
    earlier = (page_ids[None, :] < page_ids[:, None]).astype(jnp.int32)
    ranking = jnp.sum(matched[:, None, :] * earlier[None, :, :], axis=2)
    places = jnp.arange(slot_cap, dtype=jnp.int32)
    return matched[:, None, :] * (ranking[:, None, :] == places[None, :, None]).astype(jnp.int32)


def gather_kernel(span_count, slot_cap, tensor_count, off_ref, slot_ref, pool_ref, *out_refs):
    replicas, page_count = off_ref.shape
    holder = lax.axis_index("replica")
    me = lax.axis_index("tensor")
    lanes = out_refs[0].shape[-1]
    starts = [
        pl.multiple_of(((me + shift) % tensor_count) * lanes, lanes) for shift in range(tensor_count)
    ]
    for distance in range(1, span_count + 1):
        reader = (holder + distance) % replicas
        chosen = [jnp.int32(0)] * slot_cap
        count = jnp.int32(0)
        for page in range(page_count):
            matched = off_ref[reader, page] == distance
            place = slot_ref[reader, page]
            chosen = [
                jnp.where(matched & (count == slot), place, chosen[slot]) for slot in range(slot_cap)
            ]
            count = count + matched.astype(jnp.int32)
        for slot in range(slot_cap):
            for shift in range(tensor_count):
                out_refs[(distance - 1) * tensor_count + shift][slot] = pool_ref[
                    chosen[slot], :, :, pl.ds(starts[shift], lanes)
                ]


def pack_pages(pool_part, offsets, slots, span_count, slot_cap, tensor_count):
    pages, kv, rows, width = pool_part.shape
    lanes = width // tensor_count
    piece = (slot_cap, kv, rows, lanes)
    count = span_count * tensor_count
    grid_spec = pltpu.PrefetchScalarGridSpec(
        num_scalar_prefetch=2,
        grid=(1,),
        in_specs=[pl.BlockSpec((pages, kv, rows, width), lambda i, o, s: (0, 0, 0, 0))],
        out_specs=[pl.BlockSpec(piece, lambda i, o, s: (0, 0, 0, 0)) for _ in range(count)],
    )
    nbytes = 2 * (pool_part.size + span_count * slot_cap * kv * rows * width)
    return pl.pallas_call(
        functools.partial(gather_kernel, span_count, slot_cap, tensor_count),
        grid_spec=grid_spec,
        out_shape=[jax.ShapeDtypeStruct(piece, pool_part.dtype) for _ in range(count)],
        cost_estimate=pl.CostEstimate(flops=0, transcendentals=0, bytes_accessed=nbytes),
    )(offsets, slots, pool_part)


def on_device(queries, suffix_kv, page_pool, offsets, slots, prefix_len):
    replicas = lax.axis_size("replica")
    tensor_count = lax.axis_size("tensor")
    reader = lax.axis_index("replica")
    me = lax.axis_index("tensor")
    span_count = min(8, replicas - 1)
    page_count = offsets.shape[1]
    slot_cap = (page_count + span_count - 1) // span_count + 1
    distances = jnp.arange(1, span_count + 1, dtype=jnp.int32)

    payload = pack_pages(page_pool, offsets, slots, span_count, slot_cap, tensor_count)

    arrivals = []
    for distance in range(1, span_count + 1):
        for shift in range(tensor_count):
            pairs = []
            for source in range(replicas):
                for peer in range(tensor_count):
                    target = ((source + distance) % replicas) * tensor_count + (peer + shift) % tensor_count
                    pairs.append((source * tensor_count + peer, target))
            arrivals.append(lax.ppermute(payload[(distance - 1) * tensor_count + shift], ("replica", "tensor"), pairs))

    quarter = page_pool.shape[2]
    page_rows = quarter * tensor_count
    suffix_rows = queries.shape[1]
    own_offsets = lax.dynamic_index_in_dim(offsets, reader, 0, keepdims=False)
    own_length = lax.dynamic_index_in_dim(prefix_len, reader, 0, keepdims=False)
    own_picked = slot_choice(own_offsets[None, :], distances, slot_cap)
    page_ids = jnp.arange(page_count, dtype=jnp.int32)
    slot_page = jnp.sum(own_picked * page_ids[None, None, :], axis=2)
    slot_used = jnp.sum(own_picked, axis=2) > 0
    shifts = jnp.arange(tensor_count, dtype=jnp.int32)
    row_ids = jnp.arange(quarter, dtype=jnp.int32)
    position = (
        slot_page[:, None, :, None] * page_rows
        + ((me - shifts + tensor_count) % tensor_count)[None, :, None, None] * quarter
        + row_ids[None, None, None, :]
    )
    visible = slot_used[:, None, :, None] & (position < own_length)
    visible = visible.astype(jnp.int32).reshape(span_count * tensor_count, 1, -1)
    result = attend(queries[0], suffix_kv[0], visible, arrivals)
    return result.reshape(1, suffix_rows, result.shape[1])


def attention_kernel(chunk_count, q_ref, suf_ref, vis_ref, *rest):
    chunk_refs, o_ref = rest[:chunk_count], rest[chunk_count]
    rows, width = q_ref.shape
    kv_local = suf_ref.shape[2] // HEAD_DIM
    group = width // (kv_local * HEAD_DIM)
    scale = HEAD_DIM ** (-0.5)
    dims = (((1,), (1,)), ((), ()))
    row_pos = lax.broadcasted_iota(jnp.int32, (group * rows, rows), 0) % rows
    col_pos = lax.broadcasted_iota(jnp.int32, (group * rows, rows), 1)
    causal = col_pos <= row_pos
    for head in range(kv_local):
        lanes = pl.ds(head * HEAD_DIM, HEAD_DIM)
        q_all = jnp.concatenate(
            [q_ref[:, pl.ds((head * group + g) * HEAD_DIM, HEAD_DIM)] for g in range(group)], axis=0
        )
        keys = [suf_ref[0, :, lanes]]
        vals = [suf_ref[1, :, lanes]]
        masks = [causal]
        for c in range(chunk_count):
            ref = chunk_refs[c]
            keys.append(ref[:, 0, :, lanes].reshape(-1, HEAD_DIM))
            vals.append(ref[:, 1, :, lanes].reshape(-1, HEAD_DIM))
            masks.append(vis_ref[c] > 0)
        scores = []
        for key, mask in zip(keys, masks):
            s = lax.dot_general(q_all, key, dims, preferred_element_type=jnp.float32) * scale
            scores.append(jnp.where(mask, s, NEG_FILL))
        even = all(s.shape == scores[0].shape for s in scores)
        if even:
            running = scores[0]
            for s in scores[1:]:
                running = jnp.maximum(running, s)
            top = jnp.max(running, axis=-1, keepdims=True)
        else:
            top = functools.reduce(jnp.maximum, [jnp.max(s, axis=-1, keepdims=True) for s in scores])
        total = None
        acc = None
        for s, val, mask in zip(scores, vals, masks):
            w = jnp.where(mask, jnp.exp(s - top), 0.0)
            part = w if even else jnp.sum(w, axis=-1, keepdims=True)
            total = part if total is None else total + part
            pv = jnp.dot(w.astype(jnp.bfloat16), val, preferred_element_type=jnp.float32)
            acc = pv if acc is None else acc + pv
        if even:
            total = jnp.sum(total, axis=-1, keepdims=True)
        out = (acc / total).astype(o_ref.dtype)
        for g in range(group):
            o_ref[:, pl.ds((head * group + g) * HEAD_DIM, HEAD_DIM)] = out[g * rows:(g + 1) * rows]


def attend(q, suf, visible, chunks):
    rows, width = q.shape
    keys_total = suf.shape[1] + sum(c.size // (2 * suf.shape[2]) for c in chunks)
    flops = 4 * rows * width * keys_total
    nbytes = 2 * (q.size * 2 + suf.size + sum(c.size for c in chunks))
    return pl.pallas_call(
        functools.partial(attention_kernel, len(chunks)),
        out_shape=jax.ShapeDtypeStruct((rows, width), jnp.bfloat16),
        cost_estimate=pl.CostEstimate(
            flops=flops, transcendentals=rows * (width // HEAD_DIM) * keys_total, bytes_accessed=nbytes
        ),
    )(q, suf, visible, *chunks)


def solution(mesh):
    in_specs = (
        P(("groups", "replica"), None, "tensor"),
        P(("groups", "replica"), None, None, "tensor"),
        P(("groups", "replica"), None, "tensor", None),
        P("groups", None),
        P("groups", None),
        P("groups"),
    )
    out_specs = P(("groups", "replica"), None, "tensor")
    return jax.shard_map(
        on_device, mesh=mesh, in_specs=in_specs, out_specs=out_specs, check_vma=False
    )
```

```python
import functools

import jax
import jax.numpy as jnp
from jax import lax
from jax.experimental import pallas as pl
from jax.experimental.pallas import tpu as pltpu
from jax.sharding import PartitionSpec as P

HEADS = 64
KV_HEADS = 8
HEAD_DIM = 128


NEG_FILL = -1e30


def slot_choice(offsets_rows, distances, slot_cap):
    matched = (offsets_rows == distances[:, None]).astype(jnp.int32)
    page_count = offsets_rows.shape[1]
    page_ids = jnp.arange(page_count, dtype=jnp.int32)
    earlier = (page_ids[None, :] < page_ids[:, None]).astype(jnp.int32)
    ranking = jnp.sum(matched[:, None, :] * earlier[None, :, :], axis=2)
    places = jnp.arange(slot_cap, dtype=jnp.int32)
    return matched[:, None, :] * (ranking[:, None, :] == places[None, :, None]).astype(jnp.int32)


def gather_kernel(span_count, slot_cap, tensor_count, off_ref, slot_ref, pool_ref, *out_refs):
    replicas, page_count = off_ref.shape
    holder = lax.axis_index("replica")
    me = lax.axis_index("tensor")
    lanes = out_refs[0].shape[-1]
    starts = [
        pl.multiple_of(((me + shift) % tensor_count) * lanes, lanes) for shift in range(tensor_count)
    ]
    for distance in range(1, span_count + 1):
        reader = (holder + distance) % replicas
        chosen = [jnp.int32(0)] * slot_cap
        count = jnp.int32(0)
        for page in range(page_count):
            matched = off_ref[reader, page] == distance
            place = slot_ref[reader, page]
            chosen = [
                jnp.where(matched & (count == slot), place, chosen[slot]) for slot in range(slot_cap)
            ]
            count = count + matched.astype(jnp.int32)
        for slot in range(slot_cap):
            for shift in range(tensor_count):
                out_refs[(distance - 1) * tensor_count + shift][slot] = pool_ref[
                    chosen[slot], :, :, pl.ds(starts[shift], lanes)
                ]


def pack_pages(pool_part, offsets, slots, span_count, slot_cap, tensor_count):
    pages, kv, rows, width = pool_part.shape
    lanes = width // tensor_count
    piece = (slot_cap, kv, rows, lanes)
    count = span_count * tensor_count
    grid_spec = pltpu.PrefetchScalarGridSpec(
        num_scalar_prefetch=2,
        grid=(1,),
        in_specs=[pl.BlockSpec((pages, kv, rows, width), lambda i, o, s: (0, 0, 0, 0))],
        out_specs=[pl.BlockSpec(piece, lambda i, o, s: (0, 0, 0, 0)) for _ in range(count)],
    )
    nbytes = 2 * (pool_part.size + span_count * slot_cap * kv * rows * width)
    return pl.pallas_call(
        functools.partial(gather_kernel, span_count, slot_cap, tensor_count),
        grid_spec=grid_spec,
        out_shape=[jax.ShapeDtypeStruct(piece, pool_part.dtype) for _ in range(count)],
        cost_estimate=pl.CostEstimate(flops=0, transcendentals=0, bytes_accessed=nbytes),
    )(offsets, slots, pool_part)


def on_device(queries, suffix_kv, page_pool, offsets, slots, prefix_len):
    replicas = lax.axis_size("replica")
    tensor_count = lax.axis_size("tensor")
    reader = lax.axis_index("replica")
    me = lax.axis_index("tensor")
    span_count = min(8, replicas - 1)
    page_count = offsets.shape[1]
    slot_cap = (page_count + span_count - 1) // span_count + 1
    distances = jnp.arange(1, span_count + 1, dtype=jnp.int32)

    payload = pack_pages(page_pool, offsets, slots, span_count, slot_cap, tensor_count)

    arrivals = []
    for distance in range(1, span_count + 1):
        for shift in range(tensor_count):
            pairs = []
            for source in range(replicas):
                for peer in range(tensor_count):
                    target = ((source + distance) % replicas) * tensor_count + (peer + shift) % tensor_count
                    pairs.append((source * tensor_count + peer, target))
            arrivals.append(lax.ppermute(payload[(distance - 1) * tensor_count + shift], ("replica", "tensor"), pairs))

    quarter = page_pool.shape[2]
    page_rows = quarter * tensor_count
    suffix_rows = queries.shape[1]
    own_offsets = lax.dynamic_index_in_dim(offsets, reader, 0, keepdims=False)
    own_length = lax.dynamic_index_in_dim(prefix_len, reader, 0, keepdims=False)
    own_picked = slot_choice(own_offsets[None, :], distances, slot_cap)
    page_ids = jnp.arange(page_count, dtype=jnp.int32)
    slot_page = jnp.sum(own_picked * page_ids[None, None, :], axis=2)
    slot_used = jnp.sum(own_picked, axis=2) > 0
    shifts = jnp.arange(tensor_count, dtype=jnp.int32)
    row_ids = jnp.arange(quarter, dtype=jnp.int32)
    position = (
        slot_page[:, None, :, None] * page_rows
        + ((me - shifts + tensor_count) % tensor_count)[None, :, None, None] * quarter
        + row_ids[None, None, None, :]
    )
    visible = slot_used[:, None, :, None] & (position < own_length)
    visible = visible.astype(jnp.int32).reshape(span_count * tensor_count, 1, -1)
    result = attend(queries[0], suffix_kv[0], visible, arrivals, tensor_count)
    return result.reshape(1, suffix_rows, result.shape[1])


def attention_kernel(chunk_count, with_suffix, carry_in, final, *refs):
    refs = list(refs)
    q_ref = refs.pop(0)
    suf_ref = refs.pop(0) if with_suffix else None
    vis_ref = refs.pop(0)
    chunk_refs = [refs.pop(0) for _ in range(chunk_count)]
    if carry_in:
        top_in, sum_in, acc_in = refs.pop(0), refs.pop(0), refs.pop(0)
    rows, width = q_ref.shape
    group = HEADS // KV_HEADS
    kv_local = width // (group * HEAD_DIM)
    scale = HEAD_DIM ** (-0.5)
    dims = (((1,), (1,)), ((), ()))
    row_pos = lax.broadcasted_iota(jnp.int32, (group * rows, rows), 0) % rows
    col_pos = lax.broadcasted_iota(jnp.int32, (group * rows, rows), 1)
    causal = col_pos <= row_pos
    for head in range(kv_local):
        lanes = pl.ds(head * HEAD_DIM, HEAD_DIM)
        q_all = jnp.concatenate(
            [q_ref[:, pl.ds((head * group + g) * HEAD_DIM, HEAD_DIM)] for g in range(group)], axis=0
        )
        keys, vals, masks = [], [], []
        if with_suffix:
            keys.append(suf_ref[0, :, lanes])
            vals.append(suf_ref[1, :, lanes])
            masks.append(causal)
        for c in range(chunk_count):
            ref = chunk_refs[c]
            keys.append(ref[:, 0, :, lanes].reshape(-1, HEAD_DIM))
            vals.append(ref[:, 1, :, lanes].reshape(-1, HEAD_DIM))
            masks.append(vis_ref[c] > 0)
        scores = []
        for key, mask in zip(keys, masks):
            s = lax.dot_general(q_all, key, dims, preferred_element_type=jnp.float32) * scale
            scores.append(jnp.where(mask, s, NEG_FILL))
        even = all(s.shape == scores[0].shape for s in scores)
        if even:
            running = scores[0]
            for s in scores[1:]:
                running = jnp.maximum(running, s)
            top = jnp.max(running, axis=-1, keepdims=True)
        else:
            top = functools.reduce(jnp.maximum, [jnp.max(s, axis=-1, keepdims=True) for s in scores])
        if carry_in:
            before = top_in[head]
            top = jnp.maximum(top, before)
        total = None
        acc = None
        for s, val, mask in zip(scores, vals, masks):
            w = jnp.where(mask, jnp.exp(s - top), 0.0)
            part = w if even else jnp.sum(w, axis=-1, keepdims=True)
            total = part if total is None else total + part
            pv = jnp.dot(w.astype(jnp.bfloat16), val, preferred_element_type=jnp.float32)
            acc = pv if acc is None else acc + pv
        if even:
            total = jnp.sum(total, axis=-1, keepdims=True)
        if carry_in:
            rescale = jnp.exp(before - top)
            total = total + sum_in[head] * rescale
            acc = acc + acc_in[head] * rescale
        if final:
            o_ref = refs[0]
            out = (acc / total).astype(o_ref.dtype)
            for g in range(group):
                o_ref[:, pl.ds((head * group + g) * HEAD_DIM, HEAD_DIM)] = out[g * rows:(g + 1) * rows]
        else:
            top_out, sum_out, acc_out = refs
            top_out[head] = top
            sum_out[head] = total
            acc_out[head] = acc


def attend_part(q, suf, visible, chunks, carry, final):
    rows, width = q.shape
    group = HEADS // KV_HEADS
    kv_local = width // (group * HEAD_DIM)
    lanes = kv_local * HEAD_DIM
    keys_total = sum(c.size // (2 * lanes) for c in chunks) + (0 if suf is None else suf.shape[1])
    flops = 4 * rows * width * keys_total
    nbytes = 2 * (q.size * 2 + sum(c.size for c in chunks)) + (0 if suf is None else 2 * suf.size)
    state = [
        jax.ShapeDtypeStruct((kv_local, group * rows, 1), jnp.float32),
        jax.ShapeDtypeStruct((kv_local, group * rows, 1), jnp.float32),
        jax.ShapeDtypeStruct((kv_local, group * rows, HEAD_DIM), jnp.float32),
    ]
    out_shape = jax.ShapeDtypeStruct((rows, width), jnp.bfloat16) if final else state
    operands = [q] + ([] if suf is None else [suf]) + [visible] + list(chunks) + list(carry)
    return pl.pallas_call(
        functools.partial(attention_kernel, len(chunks), suf is not None, len(carry) > 0, final),
        out_shape=out_shape,
        cost_estimate=pl.CostEstimate(
            flops=flops, transcendentals=rows * (width // HEAD_DIM) * keys_total, bytes_accessed=nbytes
        ),
    )(*operands)


def attend(q, suf, visible, chunks, first_count):
    carry = attend_part(q, suf, visible[:first_count], chunks[:first_count], (), False)
    return attend_part(q, None, visible[first_count:], chunks[first_count:], carry, True)


def solution(mesh):
    in_specs = (
        P(("groups", "replica"), None, "tensor"),
        P(("groups", "replica"), None, None, "tensor"),
        P(("groups", "replica"), None, "tensor", None),
        P("groups", None),
        P("groups", None),
        P("groups"),
    )
    out_specs = P(("groups", "replica"), None, "tensor")
    return jax.shard_map(
        on_device, mesh=mesh, in_specs=in_specs, out_specs=out_specs, check_vma=False
    )
```

```python
import functools

import jax
import jax.numpy as jnp
from jax import lax
from jax.experimental import pallas as pl
from jax.experimental.pallas import tpu as pltpu
from jax.sharding import PartitionSpec as P

HEADS = 64
KV_HEADS = 8
HEAD_DIM = 128


NEG_FILL = -1e30


def slot_choice(offsets_rows, distances, slot_cap):
    matched = (offsets_rows == distances[:, None]).astype(jnp.int32)
    page_count = offsets_rows.shape[1]
    page_ids = jnp.arange(page_count, dtype=jnp.int32)
    earlier = (page_ids[None, :] < page_ids[:, None]).astype(jnp.int32)
    ranking = jnp.sum(matched[:, None, :] * earlier[None, :, :], axis=2)
    places = jnp.arange(slot_cap, dtype=jnp.int32)
    return matched[:, None, :] * (ranking[:, None, :] == places[None, :, None]).astype(jnp.int32)


def gather_kernel(span_count, slot_cap, tensor_count, off_ref, slot_ref, pool_ref, *out_refs):
    replicas, page_count = off_ref.shape
    holder = lax.axis_index("replica")
    me = lax.axis_index("tensor")
    lanes = out_refs[0].shape[-1]
    starts = [
        pl.multiple_of(((me + shift) % tensor_count) * lanes, lanes) for shift in range(tensor_count)
    ]
    for distance in range(1, span_count + 1):
        reader = (holder + distance) % replicas
        chosen = [jnp.int32(0)] * slot_cap
        count = jnp.int32(0)
        for page in range(page_count):
            matched = off_ref[reader, page] == distance
            place = slot_ref[reader, page]
            chosen = [
                jnp.where(matched & (count == slot), place, chosen[slot]) for slot in range(slot_cap)
            ]
            count = count + matched.astype(jnp.int32)
        for slot in range(slot_cap):
            for shift in range(tensor_count):
                out_refs[(distance - 1) * tensor_count + shift][slot] = pool_ref[
                    chosen[slot], :, :, pl.ds(starts[shift], lanes)
                ]


def pack_pages(pool_part, offsets, slots, span_count, slot_cap, tensor_count):
    pages, kv, rows, width = pool_part.shape
    lanes = width // tensor_count
    piece = (slot_cap, kv, rows, lanes)
    count = span_count * tensor_count
    grid_spec = pltpu.PrefetchScalarGridSpec(
        num_scalar_prefetch=2,
        grid=(1,),
        in_specs=[pl.BlockSpec((pages, kv, rows, width), lambda i, o, s: (0, 0, 0, 0))],
        out_specs=[pl.BlockSpec(piece, lambda i, o, s: (0, 0, 0, 0)) for _ in range(count)],
    )
    nbytes = 2 * (pool_part.size + span_count * slot_cap * kv * rows * width)
    return pl.pallas_call(
        functools.partial(gather_kernel, span_count, slot_cap, tensor_count),
        grid_spec=grid_spec,
        out_shape=[jax.ShapeDtypeStruct(piece, pool_part.dtype) for _ in range(count)],
        cost_estimate=pl.CostEstimate(flops=0, transcendentals=0, bytes_accessed=nbytes),
    )(offsets, slots, pool_part)


def on_device(queries, suffix_kv, page_pool, offsets, slots, prefix_len):
    replicas = lax.axis_size("replica")
    tensor_count = lax.axis_size("tensor")
    reader = lax.axis_index("replica")
    me = lax.axis_index("tensor")
    span_count = min(8, replicas - 1)
    page_count = offsets.shape[1]
    slot_cap = (page_count + span_count - 1) // span_count + 1
    distances = jnp.arange(1, span_count + 1, dtype=jnp.int32)

    payload = pack_pages(page_pool, offsets, slots, span_count, slot_cap, tensor_count)

    arrivals = []
    for distance in range(1, span_count + 1):
        for shift in range(tensor_count):
            pairs = []
            for source in range(replicas):
                for peer in range(tensor_count):
                    target = ((source + distance) % replicas) * tensor_count + (peer + shift) % tensor_count
                    pairs.append((source * tensor_count + peer, target))
            arrivals.append(lax.ppermute(payload[(distance - 1) * tensor_count + shift], ("replica", "tensor"), pairs))

    quarter = page_pool.shape[2]
    page_rows = quarter * tensor_count
    suffix_rows = queries.shape[1]
    own_offsets = lax.dynamic_index_in_dim(offsets, reader, 0, keepdims=False)
    own_length = lax.dynamic_index_in_dim(prefix_len, reader, 0, keepdims=False)
    own_picked = slot_choice(own_offsets[None, :], distances, slot_cap)
    page_ids = jnp.arange(page_count, dtype=jnp.int32)
    slot_page = jnp.sum(own_picked * page_ids[None, None, :], axis=2)
    slot_used = jnp.sum(own_picked, axis=2) > 0
    shifts = jnp.arange(tensor_count, dtype=jnp.int32)
    row_ids = jnp.arange(quarter, dtype=jnp.int32)
    position = (
        slot_page[:, None, :, None] * page_rows
        + ((me - shifts + tensor_count) % tensor_count)[None, :, None, None] * quarter
        + row_ids[None, None, None, :]
    )
    visible = slot_used[:, None, :, None] & (position < own_length)
    visible = visible.astype(jnp.int32).reshape(span_count * tensor_count, 1, -1)
    result = attend(queries[0], suffix_kv[0], visible, arrivals)
    return result.reshape(1, suffix_rows, result.shape[1])


def attention_kernel(chunk_count, q_ref, suf_ref, vis_ref, *rest):
    chunk_refs, o_ref = rest[:chunk_count], rest[chunk_count]
    rows, width = q_ref.shape
    kv_local = suf_ref.shape[2] // HEAD_DIM
    group = width // (kv_local * HEAD_DIM)
    scale = HEAD_DIM ** (-0.5)
    dims = (((1,), (1,)), ((), ()))
    row_pos = lax.broadcasted_iota(jnp.int32, (group * rows, rows), 0) % rows
    col_pos = lax.broadcasted_iota(jnp.int32, (group * rows, rows), 1)
    causal = col_pos <= row_pos
    for head in range(kv_local):
        lanes = pl.ds(head * HEAD_DIM, HEAD_DIM)
        q_all = jnp.concatenate(
            [q_ref[:, pl.ds((head * group + g) * HEAD_DIM, HEAD_DIM)] for g in range(group)], axis=0
        )
        keys = [suf_ref[0, :, lanes]]
        vals = [suf_ref[1, :, lanes]]
        masks = [causal]
        pieces = [
            (
                chunk_refs[c][:, 0, :, lanes].reshape(-1, HEAD_DIM),
                chunk_refs[c][:, 1, :, lanes].reshape(-1, HEAD_DIM),
                vis_ref[c],
            )
            for c in range(chunk_count)
        ]
        join = 2 if chunk_count % 2 == 0 else 1
        for c in range(0, chunk_count, join):
            part = pieces[c:c + join]
            keys.append(jnp.concatenate([p[0] for p in part], axis=0))
            vals.append(jnp.concatenate([p[1] for p in part], axis=0))
            masks.append(jnp.concatenate([p[2] for p in part], axis=-1) > 0)
        scores = []
        for key, mask in zip(keys, masks):
            s = lax.dot_general(q_all, key, dims, preferred_element_type=jnp.float32) * scale
            scores.append(jnp.where(mask, s, NEG_FILL))
        widths = sorted(set(s.shape[-1] for s in scores))
        top = None
        for width_now in widths:
            same = [s for s in scores if s.shape[-1] == width_now]
            part = functools.reduce(jnp.maximum, same)
            part = jnp.max(part, axis=-1, keepdims=True)
            top = part if top is None else jnp.maximum(top, part)
        sums = {}
        acc = None
        for s, val, mask in zip(scores, vals, masks):
            w = jnp.where(mask, jnp.exp(s - top), 0.0)
            width_now = s.shape[-1]
            sums[width_now] = w if width_now not in sums else sums[width_now] + w
            pv = jnp.dot(w.astype(jnp.bfloat16), val, preferred_element_type=jnp.float32)
            acc = pv if acc is None else acc + pv
        total = None
        for width_now in widths:
            part = jnp.sum(sums[width_now], axis=-1, keepdims=True)
            total = part if total is None else total + part
        out = (acc / total).astype(o_ref.dtype)
        for g in range(group):
            o_ref[:, pl.ds((head * group + g) * HEAD_DIM, HEAD_DIM)] = out[g * rows:(g + 1) * rows]


def attend(q, suf, visible, chunks):
    rows, width = q.shape
    keys_total = suf.shape[1] + sum(c.size // (2 * suf.shape[2]) for c in chunks)
    flops = 4 * rows * width * keys_total
    nbytes = 2 * (q.size * 2 + suf.size + sum(c.size for c in chunks))
    return pl.pallas_call(
        functools.partial(attention_kernel, len(chunks)),
        out_shape=jax.ShapeDtypeStruct((rows, width), jnp.bfloat16),
        cost_estimate=pl.CostEstimate(
            flops=flops, transcendentals=rows * (width // HEAD_DIM) * keys_total, bytes_accessed=nbytes
        ),
    )(q, suf, visible, *chunks)


def solution(mesh):
    in_specs = (
        P(("groups", "replica"), None, "tensor"),
        P(("groups", "replica"), None, None, "tensor"),
        P(("groups", "replica"), None, "tensor", None),
        P("groups", None),
        P("groups", None),
        P("groups"),
    )
    out_specs = P(("groups", "replica"), None, "tensor")
    return jax.shard_map(
        on_device, mesh=mesh, in_specs=in_specs, out_specs=out_specs, check_vma=False
    )
```

```python
import functools

import jax
import jax.numpy as jnp
from jax import lax
from jax.experimental import pallas as pl
from jax.experimental.pallas import tpu as pltpu
from jax.sharding import PartitionSpec as P

HEADS = 64
KV_HEADS = 8
HEAD_DIM = 128


NEG_FILL = -1e30


def slot_choice(offsets_rows, distances, slot_cap):
    matched = (offsets_rows == distances[:, None]).astype(jnp.int32)
    page_count = offsets_rows.shape[1]
    page_ids = jnp.arange(page_count, dtype=jnp.int32)
    earlier = (page_ids[None, :] < page_ids[:, None]).astype(jnp.int32)
    ranking = jnp.sum(matched[:, None, :] * earlier[None, :, :], axis=2)
    places = jnp.arange(slot_cap, dtype=jnp.int32)
    return matched[:, None, :] * (ranking[:, None, :] == places[None, :, None]).astype(jnp.int32)


def gather_kernel(span_count, slot_cap, tensor_count, off_ref, slot_ref, pool_ref, *out_refs):
    replicas, page_count = off_ref.shape
    holder = lax.axis_index("replica")
    me = lax.axis_index("tensor")
    (out_ref,) = out_refs
    lanes = out_ref.shape[-1]
    starts = [
        pl.multiple_of(((me + shift) % tensor_count) * lanes, lanes) for shift in range(tensor_count)
    ]
    for distance in range(1, span_count + 1):
        reader = (holder + distance) % replicas
        chosen = [jnp.int32(0)] * slot_cap
        count = jnp.int32(0)
        for page in range(page_count):
            matched = off_ref[reader, page] == distance
            place = slot_ref[reader, page]
            chosen = [
                jnp.where(matched & (count == slot), place, chosen[slot]) for slot in range(slot_cap)
            ]
            count = count + matched.astype(jnp.int32)
        for slot in range(slot_cap):
            for shift in range(tensor_count):
                target = reader * tensor_count + (me + shift) % tensor_count
                out_ref[target, slot] = pool_ref[chosen[slot], :, :, pl.ds(starts[shift], lanes)]


def pack_pages(pool_part, offsets, slots, span_count, slot_cap, tensor_count):
    pages, kv, rows, width = pool_part.shape
    lanes = width // tensor_count
    piece = (offsets.shape[0] * tensor_count, slot_cap, kv, rows, lanes)
    grid_spec = pltpu.PrefetchScalarGridSpec(
        num_scalar_prefetch=2,
        grid=(1,),
        in_specs=[pl.BlockSpec((pages, kv, rows, width), lambda i, o, s: (0, 0, 0, 0))],
        out_specs=pl.BlockSpec(piece, lambda i, o, s: (0, 0, 0, 0, 0)),
    )
    nbytes = 2 * (pool_part.size + span_count * slot_cap * kv * rows * width)
    return pl.pallas_call(
        functools.partial(gather_kernel, span_count, slot_cap, tensor_count),
        grid_spec=grid_spec,
        out_shape=jax.ShapeDtypeStruct(piece, pool_part.dtype),
        cost_estimate=pl.CostEstimate(flops=0, transcendentals=0, bytes_accessed=nbytes),
    )(offsets, slots, pool_part)


def on_device(queries, suffix_kv, page_pool, offsets, slots, prefix_len):
    replicas = lax.axis_size("replica")
    tensor_count = lax.axis_size("tensor")
    reader = lax.axis_index("replica")
    me = lax.axis_index("tensor")
    span_count = min(8, replicas - 1)
    page_count = offsets.shape[1]
    slot_cap = (page_count + span_count - 1) // span_count + 1
    distances = jnp.arange(1, span_count + 1, dtype=jnp.int32)

    payload = pack_pages(page_pool, offsets, slots, span_count, slot_cap, tensor_count)

    got = lax.all_to_all(payload, ("replica", "tensor"), split_axis=0, concat_axis=0, tiled=True)

    quarter = page_pool.shape[2]
    page_rows = quarter * tensor_count
    suffix_rows = queries.shape[1]
    own_offsets = lax.dynamic_index_in_dim(offsets, reader, 0, keepdims=False)
    own_length = lax.dynamic_index_in_dim(prefix_len, reader, 0, keepdims=False)
    own_picked = slot_choice(own_offsets[None, :], distances, slot_cap)
    page_ids = jnp.arange(page_count, dtype=jnp.int32)
    slot_page = jnp.sum(own_picked * page_ids[None, None, :], axis=2)
    slot_used = jnp.sum(own_picked, axis=2) > 0
    shifts = jnp.arange(tensor_count, dtype=jnp.int32)
    row_ids = jnp.arange(quarter, dtype=jnp.int32)
    position = (
        slot_page[:, None, :, None] * page_rows
        + shifts[None, :, None, None] * quarter
        + row_ids[None, None, None, :]
    )
    visible = slot_used[:, None, :, None] & (position < own_length)
    visible = visible.astype(jnp.int32).reshape(span_count * tensor_count, 1, -1)
    result = attend(queries[0], suffix_kv[0], visible, got, span_count, tensor_count)
    return result.reshape(1, suffix_rows, result.shape[1])


def attention_kernel(span_count, tensor_count, q_ref, suf_ref, vis_ref, got_ref, o_ref):
    chunk_count = span_count * tensor_count
    replicas = got_ref.shape[0] // tensor_count
    reader = lax.axis_index("replica")
    blocks = [
        ((reader - distance + replicas) % replicas) * tensor_count + peer
        for distance in range(1, span_count + 1)
        for peer in range(tensor_count)
    ]
    rows, width = q_ref.shape
    kv_local = suf_ref.shape[2] // HEAD_DIM
    group = width // (kv_local * HEAD_DIM)
    scale = HEAD_DIM ** (-0.5)
    dims = (((1,), (1,)), ((), ()))
    row_pos = lax.broadcasted_iota(jnp.int32, (group * rows, rows), 0) % rows
    col_pos = lax.broadcasted_iota(jnp.int32, (group * rows, rows), 1)
    causal = col_pos <= row_pos
    for head in range(kv_local):
        lanes = pl.ds(head * HEAD_DIM, HEAD_DIM)
        q_all = jnp.concatenate(
            [q_ref[:, pl.ds((head * group + g) * HEAD_DIM, HEAD_DIM)] for g in range(group)], axis=0
        )
        keys = [suf_ref[0, :, lanes]]
        vals = [suf_ref[1, :, lanes]]
        masks = [causal]
        pieces = [
            (
                got_ref[blocks[c], :, 0, :, lanes].reshape(-1, HEAD_DIM),
                got_ref[blocks[c], :, 1, :, lanes].reshape(-1, HEAD_DIM),
                vis_ref[c],
            )
            for c in range(chunk_count)
        ]
        join = 2 if chunk_count % 2 == 0 else 1
        for c in range(0, chunk_count, join):
            part = pieces[c:c + join]
            keys.append(jnp.concatenate([p[0] for p in part], axis=0))
            vals.append(jnp.concatenate([p[1] for p in part], axis=0))
            masks.append(jnp.concatenate([p[2] for p in part], axis=-1) > 0)
        scores = []
        for key, mask in zip(keys, masks):
            s = lax.dot_general(q_all, key, dims, preferred_element_type=jnp.float32) * scale
            scores.append(jnp.where(mask, s, NEG_FILL))
        widths = sorted(set(s.shape[-1] for s in scores))
        top = None
        for width_now in widths:
            same = [s for s in scores if s.shape[-1] == width_now]
            part = functools.reduce(jnp.maximum, same)
            part = jnp.max(part, axis=-1, keepdims=True)
            top = part if top is None else jnp.maximum(top, part)
        sums = {}
        acc = None
        for s, val, mask in zip(scores, vals, masks):
            w = jnp.where(mask, jnp.exp(s - top), 0.0)
            width_now = s.shape[-1]
            sums[width_now] = w if width_now not in sums else sums[width_now] + w
            pv = jnp.dot(w.astype(jnp.bfloat16), val, preferred_element_type=jnp.float32)
            acc = pv if acc is None else acc + pv
        total = None
        for width_now in widths:
            part = jnp.sum(sums[width_now], axis=-1, keepdims=True)
            total = part if total is None else total + part
        out = (acc / total).astype(o_ref.dtype)
        for g in range(group):
            o_ref[:, pl.ds((head * group + g) * HEAD_DIM, HEAD_DIM)] = out[g * rows:(g + 1) * rows]


def attend(q, suf, visible, got, span_count, tensor_count):
    rows, width = q.shape
    chunk_keys = got.shape[1] * got.shape[3]
    keys_total = suf.shape[1] + span_count * tensor_count * chunk_keys
    flops = 4 * rows * width * keys_total
    nbytes = 2 * (q.size * 2 + suf.size + got.size)
    return pl.pallas_call(
        functools.partial(attention_kernel, span_count, tensor_count),
        out_shape=jax.ShapeDtypeStruct((rows, width), jnp.bfloat16),
        cost_estimate=pl.CostEstimate(
            flops=flops, transcendentals=rows * (width // HEAD_DIM) * keys_total, bytes_accessed=nbytes
        ),
    )(q, suf, visible, got)


def solution(mesh):
    in_specs = (
        P(("groups", "replica"), None, "tensor"),
        P(("groups", "replica"), None, None, "tensor"),
        P(("groups", "replica"), None, "tensor", None),
        P("groups", None),
        P("groups", None),
        P("groups"),
    )
    out_specs = P(("groups", "replica"), None, "tensor")
    return jax.shard_map(
        on_device, mesh=mesh, in_specs=in_specs, out_specs=out_specs, check_vma=False
    )
```

```python
import functools

import jax
import jax.numpy as jnp
from jax import lax
from jax.experimental import pallas as pl
from jax.experimental.pallas import tpu as pltpu
from jax.sharding import PartitionSpec as P

HEADS = 64
KV_HEADS = 8
HEAD_DIM = 128


NEG_FILL = -1e30


def slot_choice(offsets_rows, distances, slot_cap):
    matched = (offsets_rows == distances[:, None]).astype(jnp.int32)
    page_count = offsets_rows.shape[1]
    page_ids = jnp.arange(page_count, dtype=jnp.int32)
    earlier = (page_ids[None, :] < page_ids[:, None]).astype(jnp.int32)
    ranking = jnp.sum(matched[:, None, :] * earlier[None, :, :], axis=2)
    places = jnp.arange(slot_cap, dtype=jnp.int32)
    return matched[:, None, :] * (ranking[:, None, :] == places[None, :, None]).astype(jnp.int32)


def gather_kernel(span_count, slot_cap, tensor_count, off_ref, slot_ref, pool_ref, *out_refs):
    replicas, page_count = off_ref.shape
    holder = lax.axis_index("replica")
    me = lax.axis_index("tensor")
    lanes = out_refs[0].shape[-1]
    starts = [
        pl.multiple_of(((me + shift) % tensor_count) * lanes, lanes) for shift in range(tensor_count)
    ]
    for distance in range(1, span_count + 1):
        reader = (holder + distance) % replicas
        chosen = [jnp.int32(0)] * slot_cap
        count = jnp.int32(0)
        for page in range(page_count):
            matched = off_ref[reader, page] == distance
            place = slot_ref[reader, page]
            chosen = [
                jnp.where(matched & (count == slot), place, chosen[slot]) for slot in range(slot_cap)
            ]
            count = count + matched.astype(jnp.int32)
        for slot in range(slot_cap):
            for shift in range(tensor_count):
                out_refs[(distance - 1) * tensor_count + shift][slot] = pool_ref[
                    chosen[slot], :, :, pl.ds(starts[shift], lanes)
                ]


def pack_pages(pool_part, offsets, slots, span_count, slot_cap, tensor_count):
    pages, kv, rows, width = pool_part.shape
    lanes = width // tensor_count
    piece = (slot_cap, kv, rows, lanes)
    count = span_count * tensor_count
    grid_spec = pltpu.PrefetchScalarGridSpec(
        num_scalar_prefetch=2,
        grid=(1,),
        in_specs=[pl.BlockSpec((pages, kv, rows, width), lambda i, o, s: (0, 0, 0, 0))],
        out_specs=[pl.BlockSpec(piece, lambda i, o, s: (0, 0, 0, 0)) for _ in range(count)],
    )
    nbytes = 2 * (pool_part.size + span_count * slot_cap * kv * rows * width)
    return pl.pallas_call(
        functools.partial(gather_kernel, span_count, slot_cap, tensor_count),
        grid_spec=grid_spec,
        out_shape=[jax.ShapeDtypeStruct(piece, pool_part.dtype) for _ in range(count)],
        cost_estimate=pl.CostEstimate(flops=0, transcendentals=0, bytes_accessed=nbytes),
    )(offsets, slots, pool_part)


def on_device(queries, suffix_kv, page_pool, offsets, slots, prefix_len):
    replicas = lax.axis_size("replica")
    tensor_count = lax.axis_size("tensor")
    reader = lax.axis_index("replica")
    me = lax.axis_index("tensor")
    span_count = min(8, replicas - 1)
    page_count = offsets.shape[1]
    slot_cap = (page_count + span_count - 1) // span_count + 1
    distances = jnp.arange(1, span_count + 1, dtype=jnp.int32)

    payload = pack_pages(page_pool, offsets, slots, span_count, slot_cap, tensor_count)

    arrivals = []
    for distance in range(1, span_count + 1):
        for shift in range(tensor_count):
            pairs = []
            for source in range(replicas):
                for peer in range(tensor_count):
                    target = ((source + distance) % replicas) * tensor_count + (peer + shift) % tensor_count
                    pairs.append((source * tensor_count + peer, target))
            arrivals.append(lax.ppermute(payload[(distance - 1) * tensor_count + shift], ("replica", "tensor"), pairs))

    quarter = page_pool.shape[2]
    page_rows = quarter * tensor_count
    suffix_rows = queries.shape[1]
    own_offsets = lax.dynamic_index_in_dim(offsets, reader, 0, keepdims=False)
    own_length = lax.dynamic_index_in_dim(prefix_len, reader, 0, keepdims=False)
    own_picked = slot_choice(own_offsets[None, :], distances, slot_cap)
    page_ids = jnp.arange(page_count, dtype=jnp.int32)
    slot_page = jnp.sum(own_picked * page_ids[None, None, :], axis=2)
    slot_used = jnp.sum(own_picked, axis=2) > 0
    shifts = jnp.arange(tensor_count, dtype=jnp.int32)
    row_ids = jnp.arange(quarter, dtype=jnp.int32)
    position = (
        slot_page[:, None, :, None] * page_rows
        + ((me - shifts + tensor_count) % tensor_count)[None, :, None, None] * quarter
        + row_ids[None, None, None, :]
    )
    visible = slot_used[:, None, :, None] & (position < own_length)
    visible = visible.astype(jnp.int32).reshape(span_count * tensor_count, 1, -1)
    result = attend(queries[0], suffix_kv[0], visible, arrivals)
    return result.reshape(1, suffix_rows, result.shape[1])


def attention_kernel(chunk_count, q_ref, suf_ref, vis_ref, *rest):
    chunk_refs, o_ref = rest[:chunk_count], rest[chunk_count]
    rows, width = q_ref.shape
    kv_local = suf_ref.shape[2] // HEAD_DIM
    group = width // (kv_local * HEAD_DIM)
    scale = HEAD_DIM ** (-0.5)
    dims = (((1,), (1,)), ((), ()))
    row_pos = lax.broadcasted_iota(jnp.int32, (group * rows, rows), 0) % rows
    col_pos = lax.broadcasted_iota(jnp.int32, (group * rows, rows), 1)
    causal = col_pos <= row_pos
    for head in range(kv_local):
        lanes = pl.ds(head * HEAD_DIM, HEAD_DIM)
        q_all = jnp.concatenate(
            [q_ref[:, pl.ds((head * group + g) * HEAD_DIM, HEAD_DIM)] for g in range(group)], axis=0
        )
        keys = [suf_ref[0, :, lanes]]
        vals = [suf_ref[1, :, lanes]]
        masks = [causal]
        pieces = [
            (
                chunk_refs[c][:, 0, :, lanes].reshape(-1, HEAD_DIM),
                chunk_refs[c][:, 1, :, lanes].reshape(-1, HEAD_DIM),
                vis_ref[c],
            )
            for c in range(chunk_count)
        ]
        join = 2 if chunk_count % 2 == 0 else 1
        for c in range(0, chunk_count, join):
            part = pieces[c:c + join]
            keys.append(jnp.concatenate([p[0] for p in part], axis=0))
            vals.append(jnp.concatenate([p[1] for p in part], axis=0))
            masks.append(jnp.concatenate([p[2] for p in part], axis=-1) > 0)
        scores = []
        for key, mask in zip(keys, masks):
            s = lax.dot_general(q_all, key, dims, preferred_element_type=jnp.float32)
            scores.append(jnp.where(mask, s, NEG_FILL))
        widths = sorted(set(s.shape[-1] for s in scores))
        top = None
        for width_now in widths:
            same = [s for s in scores if s.shape[-1] == width_now]
            part = functools.reduce(jnp.maximum, same)
            part = jnp.max(part, axis=-1, keepdims=True)
            top = part if top is None else jnp.maximum(top, part)
        top = top * scale
        sums = {}
        acc = None
        for s, val, mask in zip(scores, vals, masks):
            w = jnp.exp(s * scale - top)
            width_now = s.shape[-1]
            sums[width_now] = w if width_now not in sums else sums[width_now] + w
            pv = jnp.dot(w.astype(jnp.bfloat16), val, preferred_element_type=jnp.float32)
            acc = pv if acc is None else acc + pv
        total = None
        for width_now in widths:
            part = jnp.sum(sums[width_now], axis=-1, keepdims=True)
            total = part if total is None else total + part
        out = (acc / total).astype(o_ref.dtype)
        for g in range(group):
            o_ref[:, pl.ds((head * group + g) * HEAD_DIM, HEAD_DIM)] = out[g * rows:(g + 1) * rows]


def attend(q, suf, visible, chunks):
    rows, width = q.shape
    keys_total = suf.shape[1] + sum(c.size // (2 * suf.shape[2]) for c in chunks)
    flops = 4 * rows * width * keys_total
    nbytes = 2 * (q.size * 2 + suf.size + sum(c.size for c in chunks))
    return pl.pallas_call(
        functools.partial(attention_kernel, len(chunks)),
        out_shape=jax.ShapeDtypeStruct((rows, width), jnp.bfloat16),
        cost_estimate=pl.CostEstimate(
            flops=flops, transcendentals=rows * (width // HEAD_DIM) * keys_total, bytes_accessed=nbytes
        ),
    )(q, suf, visible, *chunks)


def solution(mesh):
    in_specs = (
        P(("groups", "replica"), None, "tensor"),
        P(("groups", "replica"), None, None, "tensor"),
        P(("groups", "replica"), None, "tensor", None),
        P("groups", None),
        P("groups", None),
        P("groups"),
    )
    out_specs = P(("groups", "replica"), None, "tensor")
    return jax.shard_map(
        on_device, mesh=mesh, in_specs=in_specs, out_specs=out_specs, check_vma=False
    )
```

```python
import functools

import jax
import jax.numpy as jnp
from jax import lax
from jax.experimental import pallas as pl
from jax.experimental.pallas import tpu as pltpu
from jax.sharding import PartitionSpec as P

HEADS = 64
KV_HEADS = 8
HEAD_DIM = 128


NEG_FILL = -1e30


def slot_choice(offsets_rows, distances, slot_cap):
    matched = (offsets_rows == distances[:, None]).astype(jnp.int32)
    page_count = offsets_rows.shape[1]
    page_ids = jnp.arange(page_count, dtype=jnp.int32)
    earlier = (page_ids[None, :] < page_ids[:, None]).astype(jnp.int32)
    ranking = jnp.sum(matched[:, None, :] * earlier[None, :, :], axis=2)
    places = jnp.arange(slot_cap, dtype=jnp.int32)
    return matched[:, None, :] * (ranking[:, None, :] == places[None, :, None]).astype(jnp.int32)


def gather_kernel(span_count, slot_cap, tensor_count, off_ref, slot_ref, pool_ref, *out_refs):
    replicas, page_count = off_ref.shape
    holder = lax.axis_index("replica")
    me = lax.axis_index("tensor")
    lanes = out_refs[0].shape[-1]
    starts = [
        pl.multiple_of(((me + shift) % tensor_count) * lanes, lanes) for shift in range(tensor_count)
    ]
    for distance in range(1, span_count + 1):
        reader = (holder + distance) % replicas
        chosen = [jnp.int32(0)] * slot_cap
        count = jnp.int32(0)
        for page in range(page_count):
            matched = off_ref[reader, page] == distance
            place = slot_ref[reader, page]
            chosen = [
                jnp.where(matched & (count == slot), place, chosen[slot]) for slot in range(slot_cap)
            ]
            count = count + matched.astype(jnp.int32)
        for slot in range(slot_cap):
            for shift in range(tensor_count):
                out_refs[(distance - 1) * tensor_count + shift][slot] = pool_ref[
                    chosen[slot], :, :, pl.ds(starts[shift], lanes)
                ]


def pack_pages(pool_part, offsets, slots, span_count, slot_cap, tensor_count):
    pages, kv, rows, width = pool_part.shape
    lanes = width // tensor_count
    piece = (slot_cap, kv, rows, lanes)
    count = span_count * tensor_count
    grid_spec = pltpu.PrefetchScalarGridSpec(
        num_scalar_prefetch=2,
        grid=(1,),
        in_specs=[pl.BlockSpec((pages, kv, rows, width), lambda i, o, s: (0, 0, 0, 0))],
        out_specs=[pl.BlockSpec(piece, lambda i, o, s: (0, 0, 0, 0)) for _ in range(count)],
    )
    nbytes = 2 * (pool_part.size + span_count * slot_cap * kv * rows * width)
    return pl.pallas_call(
        functools.partial(gather_kernel, span_count, slot_cap, tensor_count),
        grid_spec=grid_spec,
        out_shape=[jax.ShapeDtypeStruct(piece, pool_part.dtype) for _ in range(count)],
        cost_estimate=pl.CostEstimate(flops=0, transcendentals=0, bytes_accessed=nbytes),
    )(offsets, slots, pool_part)


def on_device(queries, suffix_kv, page_pool, offsets, slots, prefix_len):
    replicas = lax.axis_size("replica")
    tensor_count = lax.axis_size("tensor")
    reader = lax.axis_index("replica")
    me = lax.axis_index("tensor")
    span_count = min(8, replicas - 1)
    page_count = offsets.shape[1]
    slot_cap = (page_count + span_count - 1) // span_count + 1
    distances = jnp.arange(1, span_count + 1, dtype=jnp.int32)

    payload = pack_pages(page_pool, offsets, slots, span_count, slot_cap, tensor_count)

    arrivals = []
    for distance in range(1, span_count + 1):
        for shift in range(tensor_count):
            pairs = []
            for source in range(replicas):
                for peer in range(tensor_count):
                    target = ((source + distance) % replicas) * tensor_count + (peer + shift) % tensor_count
                    pairs.append((source * tensor_count + peer, target))
            arrivals.append(lax.ppermute(payload[(distance - 1) * tensor_count + shift], ("replica", "tensor"), pairs))

    quarter = page_pool.shape[2]
    page_rows = quarter * tensor_count
    suffix_rows = queries.shape[1]
    own_offsets = lax.dynamic_index_in_dim(offsets, reader, 0, keepdims=False)
    own_length = lax.dynamic_index_in_dim(prefix_len, reader, 0, keepdims=False)
    page_ids = jnp.arange(page_count, dtype=jnp.int32)
    earlier = (page_ids[None, :] < page_ids[:, None]).astype(jnp.int32)
    same = (own_offsets[:, None] == own_offsets[None, :]).astype(jnp.int32)
    rank = jnp.sum(same * earlier, axis=1)
    table = jnp.concatenate([own_offsets, rank]).astype(jnp.int32)
    shifts = jnp.arange(tensor_count, dtype=jnp.int32)
    row_ids = jnp.arange(quarter, dtype=jnp.int32)
    position = (
        page_ids[:, None, None] * page_rows
        + ((me - shifts + tensor_count) % tensor_count)[None, :, None] * quarter
        + row_ids[None, None, :]
    )
    visible = (position < own_length).astype(jnp.int32).reshape(page_count, 1, -1)
    result = attend(queries[0], suffix_kv[0], table, visible, arrivals, span_count, tensor_count)
    return result.reshape(1, suffix_rows, result.shape[1])


def attention_kernel(span_count, tensor_count, tab_ref, q_ref, suf_ref, vis_ref, *rest):
    chunk_refs, o_ref = rest[:-1], rest[-1]
    page_count = vis_ref.shape[0]
    rows, width = q_ref.shape
    group = HEADS // KV_HEADS
    kv_local = width // (group * HEAD_DIM)
    scale = HEAD_DIM ** (-0.5)
    dims = (((1,), (1,)), ((), ()))
    row_pos = lax.broadcasted_iota(jnp.int32, (group * rows, rows), 0) % rows
    col_pos = lax.broadcasted_iota(jnp.int32, (group * rows, rows), 1)
    causal = col_pos <= row_pos
    for head in range(kv_local):
        lanes = pl.ds(head * HEAD_DIM, HEAD_DIM)
        q_all = jnp.concatenate(
            [q_ref[:, pl.ds((head * group + g) * HEAD_DIM, HEAD_DIM)] for g in range(group)], axis=0
        )

        def page_part(page, part):
            distance, slot = tab_ref[page], tab_ref[page_count + page]
            pieces = []
            for shift in range(tensor_count):
                piece = chunk_refs[shift][slot, part, :, lanes]
                for d in range(2, span_count + 1):
                    other = chunk_refs[(d - 1) * tensor_count + shift][slot, part, :, lanes]
                    piece = jnp.where(distance == d, other, piece)
                pieces.append(piece)
            return jnp.concatenate(pieces, axis=0)

        keys = [suf_ref[0, :, lanes]]
        vals = [suf_ref[1, :, lanes]]
        masks = [causal]
        join = 2 if page_count % 2 == 0 else 1
        for page in range(0, page_count, join):
            keys.append(jnp.concatenate([page_part(p, 0) for p in range(page, page + join)], axis=0))
            vals.append(jnp.concatenate([page_part(p, 1) for p in range(page, page + join)], axis=0))
            masks.append(
                jnp.concatenate([vis_ref[p] for p in range(page, page + join)], axis=-1) > 0
            )
        scores = []
        for key, mask in zip(keys, masks):
            s = lax.dot_general(q_all, key, dims, preferred_element_type=jnp.float32)
            scores.append(jnp.where(mask, s, NEG_FILL))
        widths = sorted(set(s.shape[-1] for s in scores))
        top = None
        for width_now in widths:
            same = [s for s in scores if s.shape[-1] == width_now]
            part = functools.reduce(jnp.maximum, same)
            part = jnp.max(part, axis=-1, keepdims=True)
            top = part if top is None else jnp.maximum(top, part)
        top = top * scale
        sums = {}
        acc = None
        for s, val in zip(scores, vals):
            w = jnp.exp(s * scale - top)
            width_now = s.shape[-1]
            sums[width_now] = w if width_now not in sums else sums[width_now] + w
            pv = jnp.dot(w.astype(jnp.bfloat16), val, preferred_element_type=jnp.float32)
            acc = pv if acc is None else acc + pv
        total = None
        for width_now in widths:
            part = jnp.sum(sums[width_now], axis=-1, keepdims=True)
            total = part if total is None else total + part
        out = (acc / total).astype(o_ref.dtype)
        for g in range(group):
            o_ref[:, pl.ds((head * group + g) * HEAD_DIM, HEAD_DIM)] = out[g * rows:(g + 1) * rows]


def attend(q, suf, table, visible, chunks, span_count, tensor_count):
    rows, width = q.shape
    keys_total = suf.shape[1] + visible.shape[0] * visible.shape[2]
    flops = 4 * rows * width * keys_total
    nbytes = 2 * (q.size * 2 + suf.size + sum(c.size for c in chunks))

    def whole(a):
        return pl.BlockSpec(a.shape, lambda i, t: (0,) * a.ndim)

    grid_spec = pltpu.PrefetchScalarGridSpec(
        num_scalar_prefetch=1,
        grid=(1,),
        in_specs=[whole(q), whole(suf), whole(visible)] + [whole(c) for c in chunks],
        out_specs=pl.BlockSpec((rows, width), lambda i, t: (0, 0)),
    )
    return pl.pallas_call(
        functools.partial(attention_kernel, span_count, tensor_count),
        grid_spec=grid_spec,
        out_shape=jax.ShapeDtypeStruct((rows, width), jnp.bfloat16),
        cost_estimate=pl.CostEstimate(
            flops=flops, transcendentals=rows * (width // HEAD_DIM) * keys_total, bytes_accessed=nbytes
        ),
    )(table, q, suf, visible, *chunks)


def solution(mesh):
    in_specs = (
        P(("groups", "replica"), None, "tensor"),
        P(("groups", "replica"), None, None, "tensor"),
        P(("groups", "replica"), None, "tensor", None),
        P("groups", None),
        P("groups", None),
        P("groups"),
    )
    out_specs = P(("groups", "replica"), None, "tensor")
    return jax.shard_map(
        on_device, mesh=mesh, in_specs=in_specs, out_specs=out_specs, check_vma=False
    )
```

```python
import functools

import jax
import jax.numpy as jnp
from jax import lax
from jax.experimental import pallas as pl
from jax.experimental.pallas import tpu as pltpu
from jax.sharding import PartitionSpec as P

HEADS = 64
KV_HEADS = 8
HEAD_DIM = 128


NEG_FILL = -1e30


def slot_choice(offsets_rows, distances, slot_cap):
    matched = (offsets_rows == distances[:, None]).astype(jnp.int32)
    page_count = offsets_rows.shape[1]
    page_ids = jnp.arange(page_count, dtype=jnp.int32)
    earlier = (page_ids[None, :] < page_ids[:, None]).astype(jnp.int32)
    ranking = jnp.sum(matched[:, None, :] * earlier[None, :, :], axis=2)
    places = jnp.arange(slot_cap, dtype=jnp.int32)
    return matched[:, None, :] * (ranking[:, None, :] == places[None, :, None]).astype(jnp.int32)


def gather_kernel(first, last, slot_cap, tensor_count, off_ref, slot_ref, pool_ref, *out_refs):
    replicas, page_count = off_ref.shape
    holder = lax.axis_index("replica")
    me = lax.axis_index("tensor")
    lanes = out_refs[0].shape[-1]
    starts = [
        pl.multiple_of(((me + shift) % tensor_count) * lanes, lanes) for shift in range(tensor_count)
    ]
    for distance in range(first, last + 1):
        reader = (holder + distance) % replicas
        chosen = [jnp.int32(0)] * slot_cap
        count = jnp.int32(0)
        for page in range(page_count):
            matched = off_ref[reader, page] == distance
            place = slot_ref[reader, page]
            chosen = [
                jnp.where(matched & (count == slot), place, chosen[slot]) for slot in range(slot_cap)
            ]
            count = count + matched.astype(jnp.int32)
        for slot in range(slot_cap):
            for shift in range(tensor_count):
                out_refs[(distance - first) * tensor_count + shift][slot] = pool_ref[
                    chosen[slot], :, :, pl.ds(starts[shift], lanes)
                ]


def pack_pages(pool_part, offsets, slots, first, last, slot_cap, tensor_count):
    pages, kv, rows, width = pool_part.shape
    lanes = width // tensor_count
    piece = (slot_cap, kv, rows, lanes)
    span_count = last - first + 1
    count = span_count * tensor_count
    grid_spec = pltpu.PrefetchScalarGridSpec(
        num_scalar_prefetch=2,
        grid=(1,),
        in_specs=[pl.BlockSpec((pages, kv, rows, width), lambda i, o, s: (0, 0, 0, 0))],
        out_specs=[pl.BlockSpec(piece, lambda i, o, s: (0, 0, 0, 0)) for _ in range(count)],
    )
    nbytes = 2 * (pool_part.size + span_count * slot_cap * kv * rows * width)
    return pl.pallas_call(
        functools.partial(gather_kernel, first, last, slot_cap, tensor_count),
        grid_spec=grid_spec,
        out_shape=[jax.ShapeDtypeStruct(piece, pool_part.dtype) for _ in range(count)],
        cost_estimate=pl.CostEstimate(flops=0, transcendentals=0, bytes_accessed=nbytes),
    )(offsets, slots, pool_part)


def on_device(queries, suffix_kv, page_pool, offsets, slots, prefix_len):
    replicas = lax.axis_size("replica")
    tensor_count = lax.axis_size("tensor")
    reader = lax.axis_index("replica")
    me = lax.axis_index("tensor")
    span_count = min(8, replicas - 1)
    page_count = offsets.shape[1]
    slot_cap = (page_count + span_count - 1) // span_count + 1
    distances = jnp.arange(1, span_count + 1, dtype=jnp.int32)

    payload = pack_pages(page_pool, offsets, slots, 1, 1, slot_cap, tensor_count)
    if span_count > 1:
        payload = payload + pack_pages(page_pool, offsets, slots, 2, span_count, slot_cap, tensor_count)

    arrivals = []
    for distance in range(1, span_count + 1):
        for shift in range(tensor_count):
            pairs = []
            for source in range(replicas):
                for peer in range(tensor_count):
                    target = ((source + distance) % replicas) * tensor_count + (peer + shift) % tensor_count
                    pairs.append((source * tensor_count + peer, target))
            arrivals.append(lax.ppermute(payload[(distance - 1) * tensor_count + shift], ("replica", "tensor"), pairs))

    quarter = page_pool.shape[2]
    page_rows = quarter * tensor_count
    suffix_rows = queries.shape[1]
    own_offsets = lax.dynamic_index_in_dim(offsets, reader, 0, keepdims=False)
    own_length = lax.dynamic_index_in_dim(prefix_len, reader, 0, keepdims=False)
    page_ids = jnp.arange(page_count, dtype=jnp.int32)
    earlier = (page_ids[None, :] < page_ids[:, None]).astype(jnp.int32)
    same = (own_offsets[:, None] == own_offsets[None, :]).astype(jnp.int32)
    rank = jnp.sum(same * earlier, axis=1)
    table = jnp.concatenate([own_offsets, rank]).astype(jnp.int32)
    shifts = jnp.arange(tensor_count, dtype=jnp.int32)
    row_ids = jnp.arange(quarter, dtype=jnp.int32)
    position = (
        page_ids[:, None, None] * page_rows
        + ((me - shifts + tensor_count) % tensor_count)[None, :, None] * quarter
        + row_ids[None, None, :]
    )
    visible = (position < own_length).astype(jnp.int32).reshape(page_count, 1, -1)
    result = attend(queries[0], suffix_kv[0], table, visible, arrivals, span_count, tensor_count)
    return result.reshape(1, suffix_rows, result.shape[1])


def attention_kernel(span_count, tensor_count, tab_ref, q_ref, suf_ref, vis_ref, *rest):
    chunk_refs, o_ref = rest[:-1], rest[-1]
    page_count = vis_ref.shape[0]
    rows, width = q_ref.shape
    group = HEADS // KV_HEADS
    kv_local = width // (group * HEAD_DIM)
    scale = HEAD_DIM ** (-0.5)
    dims = (((1,), (1,)), ((), ()))
    row_pos = lax.broadcasted_iota(jnp.int32, (group * rows, rows), 0) % rows
    col_pos = lax.broadcasted_iota(jnp.int32, (group * rows, rows), 1)
    causal = col_pos <= row_pos
    for head in range(kv_local):
        lanes = pl.ds(head * HEAD_DIM, HEAD_DIM)
        q_all = jnp.concatenate(
            [q_ref[:, pl.ds((head * group + g) * HEAD_DIM, HEAD_DIM)] for g in range(group)], axis=0
        )

        def page_part(page, part):
            distance, slot = tab_ref[page], tab_ref[page_count + page]
            pieces = []
            for shift in range(tensor_count):
                piece = chunk_refs[shift][slot, part, :, lanes]
                for d in range(2, span_count + 1):
                    other = chunk_refs[(d - 1) * tensor_count + shift][slot, part, :, lanes]
                    piece = jnp.where(distance == d, other, piece)
                pieces.append(piece)
            return jnp.concatenate(pieces, axis=0)

        keys = [suf_ref[0, :, lanes]]
        vals = [suf_ref[1, :, lanes]]
        masks = [causal]
        join = 2 if page_count % 2 == 0 else 1
        for page in range(0, page_count, join):
            keys.append(jnp.concatenate([page_part(p, 0) for p in range(page, page + join)], axis=0))
            vals.append(jnp.concatenate([page_part(p, 1) for p in range(page, page + join)], axis=0))
            masks.append(
                jnp.concatenate([vis_ref[p] for p in range(page, page + join)], axis=-1) > 0
            )
        scores = []
        for key, mask in zip(keys, masks):
            s = lax.dot_general(q_all, key, dims, preferred_element_type=jnp.float32)
            scores.append(jnp.where(mask, s, NEG_FILL))
        widths = sorted(set(s.shape[-1] for s in scores))
        top = None
        for width_now in widths:
            same = [s for s in scores if s.shape[-1] == width_now]
            part = functools.reduce(jnp.maximum, same)
            part = jnp.max(part, axis=-1, keepdims=True)
            top = part if top is None else jnp.maximum(top, part)
        top = top * scale
        sums = {}
        acc = None
        for s, val in zip(scores, vals):
            w = jnp.exp(s * scale - top)
            width_now = s.shape[-1]
            sums[width_now] = w if width_now not in sums else sums[width_now] + w
            pv = jnp.dot(w.astype(jnp.bfloat16), val, preferred_element_type=jnp.float32)
            acc = pv if acc is None else acc + pv
        total = None
        for width_now in widths:
            part = jnp.sum(sums[width_now], axis=-1, keepdims=True)
            total = part if total is None else total + part
        out = (acc / total).astype(o_ref.dtype)
        for g in range(group):
            o_ref[:, pl.ds((head * group + g) * HEAD_DIM, HEAD_DIM)] = out[g * rows:(g + 1) * rows]


def attend(q, suf, table, visible, chunks, span_count, tensor_count):
    rows, width = q.shape
    keys_total = suf.shape[1] + visible.shape[0] * visible.shape[2]
    flops = 4 * rows * width * keys_total
    nbytes = 2 * (q.size * 2 + suf.size + sum(c.size for c in chunks))

    def whole(a):
        return pl.BlockSpec(a.shape, lambda i, t: (0,) * a.ndim)

    grid_spec = pltpu.PrefetchScalarGridSpec(
        num_scalar_prefetch=1,
        grid=(1,),
        in_specs=[whole(q), whole(suf), whole(visible)] + [whole(c) for c in chunks],
        out_specs=pl.BlockSpec((rows, width), lambda i, t: (0, 0)),
    )
    return pl.pallas_call(
        functools.partial(attention_kernel, span_count, tensor_count),
        grid_spec=grid_spec,
        out_shape=jax.ShapeDtypeStruct((rows, width), jnp.bfloat16),
        cost_estimate=pl.CostEstimate(
            flops=flops, transcendentals=rows * (width // HEAD_DIM) * keys_total, bytes_accessed=nbytes
        ),
    )(table, q, suf, visible, *chunks)


def solution(mesh):
    in_specs = (
        P(("groups", "replica"), None, "tensor"),
        P(("groups", "replica"), None, None, "tensor"),
        P(("groups", "replica"), None, "tensor", None),
        P("groups", None),
        P("groups", None),
        P("groups"),
    )
    out_specs = P(("groups", "replica"), None, "tensor")
    return jax.shard_map(
        on_device, mesh=mesh, in_specs=in_specs, out_specs=out_specs, check_vma=False
    )
```

```python
import functools

import jax
import jax.numpy as jnp
from jax import lax
from jax.experimental import pallas as pl
from jax.experimental.pallas import tpu as pltpu
from jax.sharding import PartitionSpec as P

HEADS = 64
KV_HEADS = 8
HEAD_DIM = 128


NEG_FILL = -1e30


def slot_choice(offsets_rows, distances, slot_cap):
    matched = (offsets_rows == distances[:, None]).astype(jnp.int32)
    page_count = offsets_rows.shape[1]
    page_ids = jnp.arange(page_count, dtype=jnp.int32)
    earlier = (page_ids[None, :] < page_ids[:, None]).astype(jnp.int32)
    ranking = jnp.sum(matched[:, None, :] * earlier[None, :, :], axis=2)
    places = jnp.arange(slot_cap, dtype=jnp.int32)
    return matched[:, None, :] * (ranking[:, None, :] == places[None, :, None]).astype(jnp.int32)


def gather_kernel(first, last, slot_cap, tensor_count, off_ref, slot_ref, pool_hbm, *rest):
    out_refs, buf, sems = rest[:-2], rest[-2], rest[-1]
    replicas, page_count = off_ref.shape
    holder = lax.axis_index("replica")
    me = lax.axis_index("tensor")
    lanes = out_refs[0].shape[-1]
    starts = [
        pl.multiple_of(((me + shift) % tensor_count) * lanes, lanes) for shift in range(tensor_count)
    ]
    copies = []
    for distance in range(first, last + 1):
        reader = (holder + distance) % replicas
        chosen = [jnp.int32(0)] * slot_cap
        count = jnp.int32(0)
        for page in range(page_count):
            matched = off_ref[reader, page] == distance
            place = slot_ref[reader, page]
            chosen = [
                jnp.where(matched & (count == slot), place, chosen[slot]) for slot in range(slot_cap)
            ]
            count = count + matched.astype(jnp.int32)
        for slot in range(slot_cap):
            index = (distance - first) * slot_cap + slot
            copy = pltpu.make_async_copy(pool_hbm.at[chosen[slot]], buf.at[index], sems.at[index])
            copy.start()
            copies.append(copy)
    for copy in copies:
        copy.wait()
    for distance in range(first, last + 1):
        for slot in range(slot_cap):
            index = (distance - first) * slot_cap + slot
            for shift in range(tensor_count):
                out_refs[(distance - first) * tensor_count + shift][slot] = buf[
                    index, :, :, pl.ds(starts[shift], lanes)
                ]


def pack_pages(pool_part, offsets, slots, first, last, slot_cap, tensor_count):
    pages, kv, rows, width = pool_part.shape
    lanes = width // tensor_count
    piece = (slot_cap, kv, rows, lanes)
    span_count = last - first + 1
    count = span_count * tensor_count
    grid_spec = pltpu.PrefetchScalarGridSpec(
        num_scalar_prefetch=2,
        grid=(1,),
        in_specs=[pl.BlockSpec(memory_space=pl.ANY)],
        out_specs=[pl.BlockSpec(piece, lambda i, o, s: (0, 0, 0, 0)) for _ in range(count)],
        scratch_shapes=[
            pltpu.VMEM((span_count * slot_cap, kv, rows, width), pool_part.dtype),
            pltpu.SemaphoreType.DMA((span_count * slot_cap,)),
        ],
    )
    nbytes = 2 * 2 * span_count * slot_cap * kv * rows * width
    return pl.pallas_call(
        functools.partial(gather_kernel, first, last, slot_cap, tensor_count),
        grid_spec=grid_spec,
        out_shape=[jax.ShapeDtypeStruct(piece, pool_part.dtype) for _ in range(count)],
        cost_estimate=pl.CostEstimate(flops=0, transcendentals=0, bytes_accessed=nbytes),
    )(offsets, slots, pool_part)


def on_device(queries, suffix_kv, page_pool, offsets, slots, prefix_len):
    replicas = lax.axis_size("replica")
    tensor_count = lax.axis_size("tensor")
    reader = lax.axis_index("replica")
    me = lax.axis_index("tensor")
    span_count = min(8, replicas - 1)
    page_count = offsets.shape[1]
    slot_cap = (page_count + span_count - 1) // span_count + 1
    distances = jnp.arange(1, span_count + 1, dtype=jnp.int32)

    payload = pack_pages(page_pool, offsets, slots, 1, 1, slot_cap, tensor_count)
    if span_count > 1:
        payload = payload + pack_pages(page_pool, offsets, slots, 2, span_count, slot_cap, tensor_count)

    arrivals = []
    for distance in range(1, span_count + 1):
        for shift in range(tensor_count):
            pairs = []
            for source in range(replicas):
                for peer in range(tensor_count):
                    target = ((source + distance) % replicas) * tensor_count + (peer + shift) % tensor_count
                    pairs.append((source * tensor_count + peer, target))
            arrivals.append(lax.ppermute(payload[(distance - 1) * tensor_count + shift], ("replica", "tensor"), pairs))

    quarter = page_pool.shape[2]
    page_rows = quarter * tensor_count
    suffix_rows = queries.shape[1]
    own_offsets = lax.dynamic_index_in_dim(offsets, reader, 0, keepdims=False)
    own_length = lax.dynamic_index_in_dim(prefix_len, reader, 0, keepdims=False)
    page_ids = jnp.arange(page_count, dtype=jnp.int32)
    earlier = (page_ids[None, :] < page_ids[:, None]).astype(jnp.int32)
    same = (own_offsets[:, None] == own_offsets[None, :]).astype(jnp.int32)
    rank = jnp.sum(same * earlier, axis=1)
    table = jnp.concatenate([own_offsets, rank]).astype(jnp.int32)
    shifts = jnp.arange(tensor_count, dtype=jnp.int32)
    row_ids = jnp.arange(quarter, dtype=jnp.int32)
    position = (
        page_ids[:, None, None] * page_rows
        + ((me - shifts + tensor_count) % tensor_count)[None, :, None] * quarter
        + row_ids[None, None, :]
    )
    visible = (position < own_length).astype(jnp.int32).reshape(page_count, 1, -1)
    result = attend(queries[0], suffix_kv[0], table, visible, arrivals, span_count, tensor_count)
    return result.reshape(1, suffix_rows, result.shape[1])


def attention_kernel(span_count, tensor_count, tab_ref, q_ref, suf_ref, vis_ref, *rest):
    chunk_refs, o_ref = rest[:-1], rest[-1]
    page_count = vis_ref.shape[0]
    rows, width = q_ref.shape
    group = HEADS // KV_HEADS
    kv_local = width // (group * HEAD_DIM)
    scale = HEAD_DIM ** (-0.5)
    dims = (((1,), (1,)), ((), ()))
    row_pos = lax.broadcasted_iota(jnp.int32, (group * rows, rows), 0) % rows
    col_pos = lax.broadcasted_iota(jnp.int32, (group * rows, rows), 1)
    causal = col_pos <= row_pos
    for head in range(kv_local):
        lanes = pl.ds(head * HEAD_DIM, HEAD_DIM)
        q_all = jnp.concatenate(
            [q_ref[:, pl.ds((head * group + g) * HEAD_DIM, HEAD_DIM)] for g in range(group)], axis=0
        )

        def page_part(page, part):
            distance, slot = tab_ref[page], tab_ref[page_count + page]
            pieces = []
            for shift in range(tensor_count):
                piece = chunk_refs[shift][slot, part, :, lanes]
                for d in range(2, span_count + 1):
                    other = chunk_refs[(d - 1) * tensor_count + shift][slot, part, :, lanes]
                    piece = jnp.where(distance == d, other, piece)
                pieces.append(piece)
            return jnp.concatenate(pieces, axis=0)

        keys = [suf_ref[0, :, lanes]]
        vals = [suf_ref[1, :, lanes]]
        masks = [causal]
        join = 2 if page_count % 2 == 0 else 1
        for page in range(0, page_count, join):
            keys.append(jnp.concatenate([page_part(p, 0) for p in range(page, page + join)], axis=0))
            vals.append(jnp.concatenate([page_part(p, 1) for p in range(page, page + join)], axis=0))
            masks.append(
                jnp.concatenate([vis_ref[p] for p in range(page, page + join)], axis=-1) > 0
            )
        scores = []
        for key, mask in zip(keys, masks):
            s = lax.dot_general(q_all, key, dims, preferred_element_type=jnp.float32)
            scores.append(jnp.where(mask, s, NEG_FILL))
        widths = sorted(set(s.shape[-1] for s in scores))
        top = None
        for width_now in widths:
            same = [s for s in scores if s.shape[-1] == width_now]
            part = functools.reduce(jnp.maximum, same)
            part = jnp.max(part, axis=-1, keepdims=True)
            top = part if top is None else jnp.maximum(top, part)
        top = top * scale
        sums = {}
        acc = None
        for s, val in zip(scores, vals):
            w = jnp.exp(s * scale - top)
            width_now = s.shape[-1]
            sums[width_now] = w if width_now not in sums else sums[width_now] + w
            pv = jnp.dot(w.astype(jnp.bfloat16), val, preferred_element_type=jnp.float32)
            acc = pv if acc is None else acc + pv
        total = None
        for width_now in widths:
            part = jnp.sum(sums[width_now], axis=-1, keepdims=True)
            total = part if total is None else total + part
        out = (acc / total).astype(o_ref.dtype)
        for g in range(group):
            o_ref[:, pl.ds((head * group + g) * HEAD_DIM, HEAD_DIM)] = out[g * rows:(g + 1) * rows]


def attend(q, suf, table, visible, chunks, span_count, tensor_count):
    rows, width = q.shape
    keys_total = suf.shape[1] + visible.shape[0] * visible.shape[2]
    flops = 4 * rows * width * keys_total
    nbytes = 2 * (q.size * 2 + suf.size + sum(c.size for c in chunks))

    def whole(a):
        return pl.BlockSpec(a.shape, lambda i, t: (0,) * a.ndim)

    grid_spec = pltpu.PrefetchScalarGridSpec(
        num_scalar_prefetch=1,
        grid=(1,),
        in_specs=[whole(q), whole(suf), whole(visible)] + [whole(c) for c in chunks],
        out_specs=pl.BlockSpec((rows, width), lambda i, t: (0, 0)),
    )
    return pl.pallas_call(
        functools.partial(attention_kernel, span_count, tensor_count),
        grid_spec=grid_spec,
        out_shape=jax.ShapeDtypeStruct((rows, width), jnp.bfloat16),
        cost_estimate=pl.CostEstimate(
            flops=flops, transcendentals=rows * (width // HEAD_DIM) * keys_total, bytes_accessed=nbytes
        ),
    )(table, q, suf, visible, *chunks)


def solution(mesh):
    in_specs = (
        P(("groups", "replica"), None, "tensor"),
        P(("groups", "replica"), None, None, "tensor"),
        P(("groups", "replica"), None, "tensor", None),
        P("groups", None),
        P("groups", None),
        P("groups"),
    )
    out_specs = P(("groups", "replica"), None, "tensor")
    return jax.shard_map(
        on_device, mesh=mesh, in_specs=in_specs, out_specs=out_specs, check_vma=False
    )
```

```python
import functools

import jax
import jax.numpy as jnp
from jax import lax
from jax.experimental import pallas as pl
from jax.experimental.pallas import tpu as pltpu
from jax.sharding import PartitionSpec as P

HEADS = 64
KV_HEADS = 8
HEAD_DIM = 128


NEG_FILL = -1e30


def slot_choice(offsets_rows, distances, slot_cap):
    matched = (offsets_rows == distances[:, None]).astype(jnp.int32)
    page_count = offsets_rows.shape[1]
    page_ids = jnp.arange(page_count, dtype=jnp.int32)
    earlier = (page_ids[None, :] < page_ids[:, None]).astype(jnp.int32)
    ranking = jnp.sum(matched[:, None, :] * earlier[None, :, :], axis=2)
    places = jnp.arange(slot_cap, dtype=jnp.int32)
    return matched[:, None, :] * (ranking[:, None, :] == places[None, :, None]).astype(jnp.int32)


def gather_kernel(first, last, slot_cap, tensor_count, off_ref, slot_ref, pool_hbm, *rest):
    out_refs, sems = rest[:-1], rest[-1]
    replicas, page_count = off_ref.shape
    holder = lax.axis_index("replica")
    me = lax.axis_index("tensor")
    lanes = out_refs[0].shape[-1]
    starts = [
        pl.multiple_of(((me + shift) % tensor_count) * lanes, lanes) for shift in range(tensor_count)
    ]
    copies = []
    for distance in range(first, last + 1):
        reader = (holder + distance) % replicas
        chosen = [jnp.int32(0)] * slot_cap
        count = jnp.int32(0)
        for page in range(page_count):
            matched = off_ref[reader, page] == distance
            place = slot_ref[reader, page]
            chosen = [
                jnp.where(matched & (count == slot), place, chosen[slot]) for slot in range(slot_cap)
            ]
            count = count + matched.astype(jnp.int32)
        for slot in range(slot_cap):
            for shift in range(tensor_count):
                index = ((distance - first) * slot_cap + slot) * tensor_count + shift
                copy = pltpu.make_async_copy(
                    pool_hbm.at[chosen[slot], :, :, pl.ds(starts[shift], lanes)],
                    out_refs[(distance - first) * tensor_count + shift].at[slot],
                    sems.at[index],
                )
                copy.start()
                copies.append(copy)
    for copy in copies:
        copy.wait()


def pack_pages(pool_part, offsets, slots, first, last, slot_cap, tensor_count):
    pages, kv, rows, width = pool_part.shape
    lanes = width // tensor_count
    piece = (slot_cap, kv, rows, lanes)
    span_count = last - first + 1
    count = span_count * tensor_count
    grid_spec = pltpu.PrefetchScalarGridSpec(
        num_scalar_prefetch=2,
        grid=(1,),
        in_specs=[pl.BlockSpec(memory_space=pl.ANY)],
        out_specs=[pl.BlockSpec(piece, lambda i, o, s: (0, 0, 0, 0)) for _ in range(count)],
        scratch_shapes=[pltpu.SemaphoreType.DMA((span_count * slot_cap * tensor_count,))],
    )
    nbytes = 2 * 2 * span_count * slot_cap * kv * rows * width
    return pl.pallas_call(
        functools.partial(gather_kernel, first, last, slot_cap, tensor_count),
        grid_spec=grid_spec,
        out_shape=[jax.ShapeDtypeStruct(piece, pool_part.dtype) for _ in range(count)],
        cost_estimate=pl.CostEstimate(flops=0, transcendentals=0, bytes_accessed=nbytes),
    )(offsets, slots, pool_part)


def on_device(queries, suffix_kv, page_pool, offsets, slots, prefix_len):
    replicas = lax.axis_size("replica")
    tensor_count = lax.axis_size("tensor")
    reader = lax.axis_index("replica")
    me = lax.axis_index("tensor")
    span_count = min(8, replicas - 1)
    page_count = offsets.shape[1]
    slot_cap = (page_count + span_count - 1) // span_count + 1
    distances = jnp.arange(1, span_count + 1, dtype=jnp.int32)

    payload = pack_pages(page_pool, offsets, slots, 1, 1, slot_cap, tensor_count)
    if span_count > 1:
        payload = payload + pack_pages(page_pool, offsets, slots, 2, span_count, slot_cap, tensor_count)

    arrivals = []
    for distance in range(1, span_count + 1):
        for shift in range(tensor_count):
            pairs = []
            for source in range(replicas):
                for peer in range(tensor_count):
                    target = ((source + distance) % replicas) * tensor_count + (peer + shift) % tensor_count
                    pairs.append((source * tensor_count + peer, target))
            arrivals.append(lax.ppermute(payload[(distance - 1) * tensor_count + shift], ("replica", "tensor"), pairs))

    quarter = page_pool.shape[2]
    page_rows = quarter * tensor_count
    suffix_rows = queries.shape[1]
    own_offsets = lax.dynamic_index_in_dim(offsets, reader, 0, keepdims=False)
    own_length = lax.dynamic_index_in_dim(prefix_len, reader, 0, keepdims=False)
    page_ids = jnp.arange(page_count, dtype=jnp.int32)
    earlier = (page_ids[None, :] < page_ids[:, None]).astype(jnp.int32)
    same = (own_offsets[:, None] == own_offsets[None, :]).astype(jnp.int32)
    rank = jnp.sum(same * earlier, axis=1)
    table = jnp.concatenate([own_offsets, rank]).astype(jnp.int32)
    shifts = jnp.arange(tensor_count, dtype=jnp.int32)
    row_ids = jnp.arange(quarter, dtype=jnp.int32)
    position = (
        page_ids[:, None, None] * page_rows
        + ((me - shifts + tensor_count) % tensor_count)[None, :, None] * quarter
        + row_ids[None, None, :]
    )
    visible = (position < own_length).astype(jnp.int32).reshape(page_count, 1, -1)
    result = attend(queries[0], suffix_kv[0], table, visible, arrivals, span_count, tensor_count)
    return result.reshape(1, suffix_rows, result.shape[1])


def attention_kernel(span_count, tensor_count, tab_ref, q_ref, suf_ref, vis_ref, *rest):
    chunk_refs, o_ref = rest[:-1], rest[-1]
    page_count = vis_ref.shape[0]
    rows, width = q_ref.shape
    group = HEADS // KV_HEADS
    kv_local = width // (group * HEAD_DIM)
    scale = HEAD_DIM ** (-0.5)
    dims = (((1,), (1,)), ((), ()))
    row_pos = lax.broadcasted_iota(jnp.int32, (group * rows, rows), 0) % rows
    col_pos = lax.broadcasted_iota(jnp.int32, (group * rows, rows), 1)
    causal = col_pos <= row_pos
    for head in range(kv_local):
        lanes = pl.ds(head * HEAD_DIM, HEAD_DIM)
        q_all = jnp.concatenate(
            [q_ref[:, pl.ds((head * group + g) * HEAD_DIM, HEAD_DIM)] for g in range(group)], axis=0
        )

        def page_part(page, part):
            distance, slot = tab_ref[page], tab_ref[page_count + page]
            pieces = []
            for shift in range(tensor_count):
                piece = chunk_refs[shift][slot, part, :, lanes]
                for d in range(2, span_count + 1):
                    other = chunk_refs[(d - 1) * tensor_count + shift][slot, part, :, lanes]
                    piece = jnp.where(distance == d, other, piece)
                pieces.append(piece)
            return jnp.concatenate(pieces, axis=0)

        keys = [suf_ref[0, :, lanes]]
        vals = [suf_ref[1, :, lanes]]
        masks = [causal]
        join = 2 if page_count % 2 == 0 else 1
        for page in range(0, page_count, join):
            keys.append(jnp.concatenate([page_part(p, 0) for p in range(page, page + join)], axis=0))
            vals.append(jnp.concatenate([page_part(p, 1) for p in range(page, page + join)], axis=0))
            masks.append(
                jnp.concatenate([vis_ref[p] for p in range(page, page + join)], axis=-1) > 0
            )
        scores = []
        for key, mask in zip(keys, masks):
            s = lax.dot_general(q_all, key, dims, preferred_element_type=jnp.float32)
            scores.append(jnp.where(mask, s, NEG_FILL))
        widths = sorted(set(s.shape[-1] for s in scores))
        top = None
        for width_now in widths:
            same = [s for s in scores if s.shape[-1] == width_now]
            part = functools.reduce(jnp.maximum, same)
            part = jnp.max(part, axis=-1, keepdims=True)
            top = part if top is None else jnp.maximum(top, part)
        top = top * scale
        sums = {}
        acc = None
        for s, val in zip(scores, vals):
            w = jnp.exp(s * scale - top)
            width_now = s.shape[-1]
            sums[width_now] = w if width_now not in sums else sums[width_now] + w
            pv = jnp.dot(w.astype(jnp.bfloat16), val, preferred_element_type=jnp.float32)
            acc = pv if acc is None else acc + pv
        total = None
        for width_now in widths:
            part = jnp.sum(sums[width_now], axis=-1, keepdims=True)
            total = part if total is None else total + part
        out = (acc / total).astype(o_ref.dtype)
        for g in range(group):
            o_ref[:, pl.ds((head * group + g) * HEAD_DIM, HEAD_DIM)] = out[g * rows:(g + 1) * rows]


def attend(q, suf, table, visible, chunks, span_count, tensor_count):
    rows, width = q.shape
    keys_total = suf.shape[1] + visible.shape[0] * visible.shape[2]
    flops = 4 * rows * width * keys_total
    nbytes = 2 * (q.size * 2 + suf.size + sum(c.size for c in chunks))

    def whole(a):
        return pl.BlockSpec(a.shape, lambda i, t: (0,) * a.ndim)

    grid_spec = pltpu.PrefetchScalarGridSpec(
        num_scalar_prefetch=1,
        grid=(1,),
        in_specs=[whole(q), whole(suf), whole(visible)] + [whole(c) for c in chunks],
        out_specs=pl.BlockSpec((rows, width), lambda i, t: (0, 0)),
    )
    return pl.pallas_call(
        functools.partial(attention_kernel, span_count, tensor_count),
        grid_spec=grid_spec,
        out_shape=jax.ShapeDtypeStruct((rows, width), jnp.bfloat16),
        cost_estimate=pl.CostEstimate(
            flops=flops, transcendentals=rows * (width // HEAD_DIM) * keys_total, bytes_accessed=nbytes
        ),
    )(table, q, suf, visible, *chunks)


def solution(mesh):
    in_specs = (
        P(("groups", "replica"), None, "tensor"),
        P(("groups", "replica"), None, None, "tensor"),
        P(("groups", "replica"), None, "tensor", None),
        P("groups", None),
        P("groups", None),
        P("groups"),
    )
    out_specs = P(("groups", "replica"), None, "tensor")
    return jax.shard_map(
        on_device, mesh=mesh, in_specs=in_specs, out_specs=out_specs, check_vma=False
    )
```

```python
import functools

import jax
import jax.numpy as jnp
from jax import lax
from jax.experimental import pallas as pl
from jax.experimental.pallas import tpu as pltpu
from jax.sharding import PartitionSpec as P

HEADS = 64
KV_HEADS = 8
HEAD_DIM = 128


NEG_FILL = -1e30


def slot_choice(offsets_rows, distances, slot_cap):
    matched = (offsets_rows == distances[:, None]).astype(jnp.int32)
    page_count = offsets_rows.shape[1]
    page_ids = jnp.arange(page_count, dtype=jnp.int32)
    earlier = (page_ids[None, :] < page_ids[:, None]).astype(jnp.int32)
    ranking = jnp.sum(matched[:, None, :] * earlier[None, :, :], axis=2)
    places = jnp.arange(slot_cap, dtype=jnp.int32)
    return matched[:, None, :] * (ranking[:, None, :] == places[None, :, None]).astype(jnp.int32)


def gather_kernel(first, last, slot_cap, tensor_count, off_ref, slot_ref, pool_hbm, *rest):
    out_refs, sems = rest[:-1], rest[-1]
    replicas, page_count = off_ref.shape
    holder = lax.axis_index("replica")
    me = lax.axis_index("tensor")
    lanes = out_refs[0].shape[-1]
    starts = [
        pl.multiple_of(((me + shift) % tensor_count) * lanes, lanes) for shift in range(tensor_count)
    ]
    copies = []
    for distance in range(first, last + 1):
        reader = (holder + distance) % replicas
        chosen = [jnp.int32(0)] * slot_cap
        count = jnp.int32(0)
        for page in range(page_count):
            matched = off_ref[reader, page] == distance
            place = slot_ref[reader, page]
            chosen = [
                jnp.where(matched & (count == slot), place, chosen[slot]) for slot in range(slot_cap)
            ]
            count = count + matched.astype(jnp.int32)
        for slot in range(slot_cap):
            for shift in range(tensor_count):
                index = ((distance - first) * slot_cap + slot) * tensor_count + shift
                copy = pltpu.make_async_copy(
                    pool_hbm.at[chosen[slot], :, :, pl.ds(starts[shift], lanes)],
                    out_refs[(distance - first) * tensor_count + shift].at[slot],
                    sems.at[index],
                )
                copy.start()
                copies.append(copy)
    for copy in copies:
        copy.wait()


def pack_pages(pool_part, offsets, slots, first, last, slot_cap, tensor_count):
    pages, kv, rows, width = pool_part.shape
    lanes = width // tensor_count
    piece = (slot_cap, kv, rows, lanes)
    span_count = last - first + 1
    count = span_count * tensor_count
    grid_spec = pltpu.PrefetchScalarGridSpec(
        num_scalar_prefetch=2,
        grid=(1,),
        in_specs=[pl.BlockSpec(memory_space=pl.ANY)],
        out_specs=[pl.BlockSpec(piece, lambda i, o, s: (0, 0, 0, 0)) for _ in range(count)],
        scratch_shapes=[pltpu.SemaphoreType.DMA((span_count * slot_cap * tensor_count,))],
    )
    nbytes = 2 * 2 * span_count * slot_cap * kv * rows * width
    return pl.pallas_call(
        functools.partial(gather_kernel, first, last, slot_cap, tensor_count),
        grid_spec=grid_spec,
        out_shape=[jax.ShapeDtypeStruct(piece, pool_part.dtype) for _ in range(count)],
        cost_estimate=pl.CostEstimate(flops=0, transcendentals=0, bytes_accessed=nbytes),
    )(offsets, slots, pool_part)


def on_device(queries, suffix_kv, page_pool, offsets, slots, prefix_len):
    replicas = lax.axis_size("replica")
    tensor_count = lax.axis_size("tensor")
    reader = lax.axis_index("replica")
    me = lax.axis_index("tensor")
    span_count = min(8, replicas - 1)
    page_count = offsets.shape[1]
    slot_cap = (page_count + span_count - 1) // span_count + 1
    distances = jnp.arange(1, span_count + 1, dtype=jnp.int32)

    payload = pack_pages(page_pool, offsets, slots, 1, 1, slot_cap, tensor_count)
    if span_count > 1:
        payload = payload + pack_pages(page_pool, offsets, slots, 2, span_count, slot_cap, tensor_count)

    arrivals = []
    for distance in range(1, span_count + 1):
        for shift in range(tensor_count):
            pairs = []
            for source in range(replicas):
                for peer in range(tensor_count):
                    target = ((source + distance) % replicas) * tensor_count + (peer + shift) % tensor_count
                    pairs.append((source * tensor_count + peer, target))
            arrivals.append(lax.ppermute(payload[(distance - 1) * tensor_count + shift], ("replica", "tensor"), pairs))

    quarter = page_pool.shape[2]
    page_rows = quarter * tensor_count
    suffix_rows = queries.shape[1]
    own_offsets = lax.dynamic_index_in_dim(offsets, reader, 0, keepdims=False)
    own_length = lax.dynamic_index_in_dim(prefix_len, reader, 0, keepdims=False)
    page_ids = jnp.arange(page_count, dtype=jnp.int32)
    earlier = (page_ids[None, :] < page_ids[:, None]).astype(jnp.int32)
    same = (own_offsets[:, None] == own_offsets[None, :]).astype(jnp.int32)
    rank = jnp.sum(same * earlier, axis=1)
    table = jnp.concatenate([own_offsets, rank]).astype(jnp.int32)
    shifts = jnp.arange(tensor_count, dtype=jnp.int32)
    row_ids = jnp.arange(quarter, dtype=jnp.int32)
    position = (
        page_ids[:, None, None] * page_rows
        + ((me - shifts + tensor_count) % tensor_count)[None, :, None] * quarter
        + row_ids[None, None, :]
    )
    visible = (position < own_length).astype(jnp.int32).reshape(page_count, 1, -1)
    result = attend(queries[0], suffix_kv[0], table, visible, arrivals, span_count, tensor_count)
    return result.reshape(1, suffix_rows, result.shape[1])


def attention_kernel(span_count, tensor_count, tab_ref, q_ref, suf_ref, vis_ref, *rest):
    chunk_refs, o_ref, page_buf, sems = rest[:-3], rest[-3], rest[-2], rest[-1]
    page_count = vis_ref.shape[0]
    for page in range(page_count):
        distance, slot = tab_ref[page], tab_ref[page_count + page]
        for shift in range(tensor_count):
            for d in range(1, span_count + 1):

                @pl.when(distance == d)
                def _():
                    pltpu.make_async_copy(
                        chunk_refs[(d - 1) * tensor_count + shift].at[slot],
                        page_buf.at[page, shift],
                        sems.at[page * tensor_count + shift],
                    ).start()

    for page in range(page_count):
        for shift in range(tensor_count):
            pltpu.make_async_copy(
                chunk_refs[shift].at[0], page_buf.at[page, shift], sems.at[page * tensor_count + shift]
            ).wait()
    rows, width = q_ref.shape
    group = HEADS // KV_HEADS
    kv_local = width // (group * HEAD_DIM)
    scale = HEAD_DIM ** (-0.5)
    dims = (((1,), (1,)), ((), ()))
    row_pos = lax.broadcasted_iota(jnp.int32, (group * rows, rows), 0) % rows
    col_pos = lax.broadcasted_iota(jnp.int32, (group * rows, rows), 1)
    causal = col_pos <= row_pos
    for head in range(kv_local):
        lanes = pl.ds(head * HEAD_DIM, HEAD_DIM)
        q_all = jnp.concatenate(
            [q_ref[:, pl.ds((head * group + g) * HEAD_DIM, HEAD_DIM)] for g in range(group)], axis=0
        )

        def page_part(page, part):
            return jnp.concatenate(
                [page_buf[page, shift, part, :, lanes] for shift in range(tensor_count)], axis=0
            )

        keys = [suf_ref[0, :, lanes]]
        vals = [suf_ref[1, :, lanes]]
        masks = [causal]
        join = 2 if page_count % 2 == 0 else 1
        for page in range(0, page_count, join):
            keys.append(jnp.concatenate([page_part(p, 0) for p in range(page, page + join)], axis=0))
            vals.append(jnp.concatenate([page_part(p, 1) for p in range(page, page + join)], axis=0))
            masks.append(
                jnp.concatenate([vis_ref[p] for p in range(page, page + join)], axis=-1) > 0
            )
        scores = []
        for key, mask in zip(keys, masks):
            s = lax.dot_general(q_all, key, dims, preferred_element_type=jnp.float32)
            scores.append(jnp.where(mask, s, NEG_FILL))
        widths = sorted(set(s.shape[-1] for s in scores))
        top = None
        for width_now in widths:
            same = [s for s in scores if s.shape[-1] == width_now]
            part = functools.reduce(jnp.maximum, same)
            part = jnp.max(part, axis=-1, keepdims=True)
            top = part if top is None else jnp.maximum(top, part)
        top = top * scale
        sums = {}
        acc = None
        for s, val in zip(scores, vals):
            w = jnp.exp(s * scale - top)
            width_now = s.shape[-1]
            sums[width_now] = w if width_now not in sums else sums[width_now] + w
            pv = jnp.dot(w.astype(jnp.bfloat16), val, preferred_element_type=jnp.float32)
            acc = pv if acc is None else acc + pv
        total = None
        for width_now in widths:
            part = jnp.sum(sums[width_now], axis=-1, keepdims=True)
            total = part if total is None else total + part
        out = (acc / total).astype(o_ref.dtype)
        for g in range(group):
            o_ref[:, pl.ds((head * group + g) * HEAD_DIM, HEAD_DIM)] = out[g * rows:(g + 1) * rows]


def attend(q, suf, table, visible, chunks, span_count, tensor_count):
    rows, width = q.shape
    keys_total = suf.shape[1] + visible.shape[0] * visible.shape[2]
    flops = 4 * rows * width * keys_total
    nbytes = 2 * (q.size * 2 + suf.size + sum(c.size for c in chunks))

    def whole(a):
        return pl.BlockSpec(a.shape, lambda i, t: (0,) * a.ndim)

    page_count = visible.shape[0]
    slot_cap, kv, quarter, lanes = chunks[0].shape
    grid_spec = pltpu.PrefetchScalarGridSpec(
        num_scalar_prefetch=1,
        grid=(1,),
        in_specs=[whole(q), whole(suf), whole(visible)]
        + [pl.BlockSpec(memory_space=pl.ANY) for _ in chunks],
        out_specs=pl.BlockSpec((rows, width), lambda i, t: (0, 0)),
        scratch_shapes=[
            pltpu.VMEM((page_count, tensor_count, kv, quarter, lanes), chunks[0].dtype),
            pltpu.SemaphoreType.DMA((page_count * tensor_count,)),
        ],
    )
    return pl.pallas_call(
        functools.partial(attention_kernel, span_count, tensor_count),
        grid_spec=grid_spec,
        out_shape=jax.ShapeDtypeStruct((rows, width), jnp.bfloat16),
        cost_estimate=pl.CostEstimate(
            flops=flops, transcendentals=rows * (width // HEAD_DIM) * keys_total, bytes_accessed=nbytes
        ),
    )(table, q, suf, visible, *chunks)


def solution(mesh):
    in_specs = (
        P(("groups", "replica"), None, "tensor"),
        P(("groups", "replica"), None, None, "tensor"),
        P(("groups", "replica"), None, "tensor", None),
        P("groups", None),
        P("groups", None),
        P("groups"),
    )
    out_specs = P(("groups", "replica"), None, "tensor")
    return jax.shard_map(
        on_device, mesh=mesh, in_specs=in_specs, out_specs=out_specs, check_vma=False
    )
```

```python
import functools

import jax
import jax.numpy as jnp
from jax import lax
from jax.experimental import pallas as pl
from jax.experimental.pallas import tpu as pltpu
from jax.sharding import PartitionSpec as P

HEADS = 64
KV_HEADS = 8
HEAD_DIM = 128


NEG_FILL = -1e30


def slot_choice(offsets_rows, distances, slot_cap):
    matched = (offsets_rows == distances[:, None]).astype(jnp.int32)
    page_count = offsets_rows.shape[1]
    page_ids = jnp.arange(page_count, dtype=jnp.int32)
    earlier = (page_ids[None, :] < page_ids[:, None]).astype(jnp.int32)
    ranking = jnp.sum(matched[:, None, :] * earlier[None, :, :], axis=2)
    places = jnp.arange(slot_cap, dtype=jnp.int32)
    return matched[:, None, :] * (ranking[:, None, :] == places[None, :, None]).astype(jnp.int32)


def gather_kernel(first, last, slot_cap, tensor_count, off_ref, slot_ref, pool_hbm, *rest):
    out_refs, sems = rest[:-1], rest[-1]
    replicas, page_count = off_ref.shape
    holder = lax.axis_index("replica")
    me = lax.axis_index("tensor")
    lanes = out_refs[0].shape[-1]
    starts = [
        pl.multiple_of(((me + shift) % tensor_count) * lanes, lanes) for shift in range(tensor_count)
    ]
    copies = []
    for distance in range(first, last + 1):
        reader = (holder + distance) % replicas
        chosen = [jnp.int32(0)] * slot_cap
        count = jnp.int32(0)
        for page in range(page_count):
            matched = off_ref[reader, page] == distance
            place = slot_ref[reader, page]
            chosen = [
                jnp.where(matched & (count == slot), place, chosen[slot]) for slot in range(slot_cap)
            ]
            count = count + matched.astype(jnp.int32)
        for slot in range(slot_cap):
            for shift in range(tensor_count):
                index = ((distance - first) * slot_cap + slot) * tensor_count + shift
                copy = pltpu.make_async_copy(
                    pool_hbm.at[chosen[slot], :, :, pl.ds(starts[shift], lanes)],
                    out_refs[(distance - first) * tensor_count + shift].at[slot],
                    sems.at[index],
                )
                copy.start()
                copies.append(copy)
    for copy in copies:
        copy.wait()


def pack_pages(pool_part, offsets, slots, first, last, slot_cap, tensor_count):
    pages, kv, rows, width = pool_part.shape
    lanes = width // tensor_count
    piece = (slot_cap, kv, rows, lanes)
    span_count = last - first + 1
    count = span_count * tensor_count
    grid_spec = pltpu.PrefetchScalarGridSpec(
        num_scalar_prefetch=2,
        grid=(1,),
        in_specs=[pl.BlockSpec(memory_space=pl.ANY)],
        out_specs=[pl.BlockSpec(piece, lambda i, o, s: (0, 0, 0, 0)) for _ in range(count)],
        scratch_shapes=[pltpu.SemaphoreType.DMA((span_count * slot_cap * tensor_count,))],
    )
    nbytes = 2 * 2 * span_count * slot_cap * kv * rows * width
    return pl.pallas_call(
        functools.partial(gather_kernel, first, last, slot_cap, tensor_count),
        grid_spec=grid_spec,
        out_shape=[jax.ShapeDtypeStruct(piece, pool_part.dtype) for _ in range(count)],
        cost_estimate=pl.CostEstimate(flops=0, transcendentals=0, bytes_accessed=nbytes),
    )(offsets, slots, pool_part)


def on_device(queries, suffix_kv, page_pool, offsets, slots, prefix_len):
    replicas = lax.axis_size("replica")
    tensor_count = lax.axis_size("tensor")
    reader = lax.axis_index("replica")
    me = lax.axis_index("tensor")
    span_count = min(8, replicas - 1)
    page_count = offsets.shape[1]
    slot_cap = (page_count + span_count - 1) // span_count + 1
    distances = jnp.arange(1, span_count + 1, dtype=jnp.int32)

    payload = pack_pages(page_pool, offsets, slots, 1, 1, slot_cap, tensor_count)
    if span_count > 1:
        payload = payload + pack_pages(page_pool, offsets, slots, 2, span_count, slot_cap, tensor_count)

    arrivals = []
    for distance in range(1, span_count + 1):
        for shift in range(tensor_count):
            pairs = []
            for source in range(replicas):
                for peer in range(tensor_count):
                    target = ((source + distance) % replicas) * tensor_count + (peer + shift) % tensor_count
                    pairs.append((source * tensor_count + peer, target))
            arrivals.append(lax.ppermute(payload[(distance - 1) * tensor_count + shift], ("replica", "tensor"), pairs))

    quarter = page_pool.shape[2]
    page_rows = quarter * tensor_count
    suffix_rows = queries.shape[1]
    own_offsets = lax.dynamic_index_in_dim(offsets, reader, 0, keepdims=False)
    own_length = lax.dynamic_index_in_dim(prefix_len, reader, 0, keepdims=False)
    page_ids = jnp.arange(page_count, dtype=jnp.int32)
    earlier = (page_ids[None, :] < page_ids[:, None]).astype(jnp.int32)
    same = (own_offsets[:, None] == own_offsets[None, :]).astype(jnp.int32)
    rank = jnp.sum(same * earlier, axis=1)
    whole_page = ((page_ids + 1) * page_rows <= own_length).astype(jnp.int32)
    table = jnp.concatenate([own_offsets, rank, whole_page]).astype(jnp.int32)
    shifts = jnp.arange(tensor_count, dtype=jnp.int32)
    row_ids = jnp.arange(quarter, dtype=jnp.int32)
    position = (
        page_ids[:, None, None] * page_rows
        + ((me - shifts + tensor_count) % tensor_count)[None, :, None] * quarter
        + row_ids[None, None, :]
    )
    visible = (position < own_length).astype(jnp.int32).reshape(page_count, 1, -1)
    result = attend(queries[0], suffix_kv[0], table, visible, arrivals, span_count, tensor_count)
    return result.reshape(1, suffix_rows, result.shape[1])


def attention_kernel(span_count, tensor_count, tab_ref, q_ref, suf_ref, vis_ref, *rest):
    chunk_refs, o_ref = rest[:-1], rest[-1]
    page_count = vis_ref.shape[0]
    rows, width = q_ref.shape
    group = HEADS // KV_HEADS
    kv_local = width // (group * HEAD_DIM)
    scale = HEAD_DIM ** (-0.5)
    dims = (((1,), (1,)), ((), ()))
    row_pos = lax.broadcasted_iota(jnp.int32, (group * rows, rows), 0) % rows
    col_pos = lax.broadcasted_iota(jnp.int32, (group * rows, rows), 1)
    causal = col_pos <= row_pos
    for head in range(kv_local):
        lanes = pl.ds(head * HEAD_DIM, HEAD_DIM)
        q_all = jnp.concatenate(
            [q_ref[:, pl.ds((head * group + g) * HEAD_DIM, HEAD_DIM)] for g in range(group)], axis=0
        )

        def page_part(page, part):
            distance, slot = tab_ref[page], tab_ref[page_count + page]
            pieces = []
            for shift in range(tensor_count):
                piece = chunk_refs[shift][slot, part, :, lanes]
                for d in range(2, span_count + 1):
                    other = chunk_refs[(d - 1) * tensor_count + shift][slot, part, :, lanes]
                    piece = jnp.where(distance == d, other, piece)
                pieces.append(piece)
            return jnp.concatenate(pieces, axis=0)

        keys = [suf_ref[0, :, lanes]]
        vals = [suf_ref[1, :, lanes]]
        masks = [causal]
        join = 2 if page_count % 2 == 0 else 1
        for page in range(0, page_count, join):
            keys.append(jnp.concatenate([page_part(p, 0) for p in range(page, page + join)], axis=0))
            vals.append(jnp.concatenate([page_part(p, 1) for p in range(page, page + join)], axis=0))
            masks.append(
                jnp.concatenate([vis_ref[p] for p in range(page, page + join)], axis=-1) > 0
            )
        scores = []
        for number, (key, mask) in enumerate(zip(keys, masks)):
            s = lax.dot_general(q_all, key, dims, preferred_element_type=jnp.float32)
            if number == 0:
                scores.append(jnp.where(mask, s, NEG_FILL))
            else:
                first_page = (number - 1) * join
                whole_tile = tab_ref[2 * page_count + first_page + join - 1] > 0
                scores.append(
                    lax.cond(whole_tile, lambda x: x, lambda x: jnp.where(mask, x, NEG_FILL), s)
                )
        widths = sorted(set(s.shape[-1] for s in scores))
        top = None
        for width_now in widths:
            same = [s for s in scores if s.shape[-1] == width_now]
            part = functools.reduce(jnp.maximum, same)
            part = jnp.max(part, axis=-1, keepdims=True)
            top = part if top is None else jnp.maximum(top, part)
        top = top * scale
        sums = {}
        acc = None
        for s, val in zip(scores, vals):
            w = jnp.exp(s * scale - top)
            width_now = s.shape[-1]
            sums[width_now] = w if width_now not in sums else sums[width_now] + w
            pv = jnp.dot(w.astype(jnp.bfloat16), val, preferred_element_type=jnp.float32)
            acc = pv if acc is None else acc + pv
        total = None
        for width_now in widths:
            part = jnp.sum(sums[width_now], axis=-1, keepdims=True)
            total = part if total is None else total + part
        out = (acc / total).astype(o_ref.dtype)
        for g in range(group):
            o_ref[:, pl.ds((head * group + g) * HEAD_DIM, HEAD_DIM)] = out[g * rows:(g + 1) * rows]


def attend(q, suf, table, visible, chunks, span_count, tensor_count):
    rows, width = q.shape
    keys_total = suf.shape[1] + visible.shape[0] * visible.shape[2]
    flops = 4 * rows * width * keys_total
    nbytes = 2 * (q.size * 2 + suf.size + sum(c.size for c in chunks))

    def whole(a):
        return pl.BlockSpec(a.shape, lambda i, t: (0,) * a.ndim)

    grid_spec = pltpu.PrefetchScalarGridSpec(
        num_scalar_prefetch=1,
        grid=(1,),
        in_specs=[whole(q), whole(suf), whole(visible)] + [whole(c) for c in chunks],
        out_specs=pl.BlockSpec((rows, width), lambda i, t: (0, 0)),
    )
    return pl.pallas_call(
        functools.partial(attention_kernel, span_count, tensor_count),
        grid_spec=grid_spec,
        out_shape=jax.ShapeDtypeStruct((rows, width), jnp.bfloat16),
        cost_estimate=pl.CostEstimate(
            flops=flops, transcendentals=rows * (width // HEAD_DIM) * keys_total, bytes_accessed=nbytes
        ),
    )(table, q, suf, visible, *chunks)


def solution(mesh):
    in_specs = (
        P(("groups", "replica"), None, "tensor"),
        P(("groups", "replica"), None, None, "tensor"),
        P(("groups", "replica"), None, "tensor", None),
        P("groups", None),
        P("groups", None),
        P("groups"),
    )
    out_specs = P(("groups", "replica"), None, "tensor")
    return jax.shard_map(
        on_device, mesh=mesh, in_specs=in_specs, out_specs=out_specs, check_vma=False
    )
```

```python
import functools

import jax
import jax.numpy as jnp
from jax import lax
from jax.experimental import pallas as pl
from jax.experimental.pallas import tpu as pltpu
from jax.sharding import PartitionSpec as P

HEADS = 64
KV_HEADS = 8
HEAD_DIM = 128


NEG_FILL = -1e30


def slot_choice(offsets_rows, distances, slot_cap):
    matched = (offsets_rows == distances[:, None]).astype(jnp.int32)
    page_count = offsets_rows.shape[1]
    page_ids = jnp.arange(page_count, dtype=jnp.int32)
    earlier = (page_ids[None, :] < page_ids[:, None]).astype(jnp.int32)
    ranking = jnp.sum(matched[:, None, :] * earlier[None, :, :], axis=2)
    places = jnp.arange(slot_cap, dtype=jnp.int32)
    return matched[:, None, :] * (ranking[:, None, :] == places[None, :, None]).astype(jnp.int32)


def gather_kernel(chosen_distances, slot_cap, tensor_count, off_ref, slot_ref, pool_hbm, *rest):
    out_refs, buf, sems = rest[:-2], rest[-2], rest[-1]
    replicas, page_count = off_ref.shape
    holder = lax.axis_index("replica")
    me = lax.axis_index("tensor")
    lanes = out_refs[0].shape[-1]
    starts = [
        pl.multiple_of(((me + shift) % tensor_count) * lanes, lanes) for shift in range(tensor_count)
    ]
    copies = []
    for number, distance in enumerate(chosen_distances):
        reader = (holder + distance) % replicas
        chosen = [jnp.int32(0)] * slot_cap
        count = jnp.int32(0)
        for page in range(page_count):
            matched = off_ref[reader, page] == distance
            place = slot_ref[reader, page]
            chosen = [
                jnp.where(matched & (count == slot), place, chosen[slot]) for slot in range(slot_cap)
            ]
            count = count + matched.astype(jnp.int32)
        for slot in range(slot_cap):
            index = number * slot_cap + slot
            copy = pltpu.make_async_copy(pool_hbm.at[chosen[slot]], buf.at[index], sems.at[index])
            copy.start()
            copies.append(copy)
    for copy in copies:
        copy.wait()
    for number in range(len(chosen_distances)):
        for slot in range(slot_cap):
            index = number * slot_cap + slot
            for shift in range(tensor_count):
                out_refs[number * tensor_count + shift][slot] = buf[
                    index, :, :, pl.ds(starts[shift], lanes)
                ]


def pack_pages(pool_part, offsets, slots, chosen_distances, slot_cap, tensor_count):
    pages, kv, rows, width = pool_part.shape
    lanes = width // tensor_count
    piece = (slot_cap, kv, rows, lanes)
    span_count = len(chosen_distances)
    count = span_count * tensor_count
    grid_spec = pltpu.PrefetchScalarGridSpec(
        num_scalar_prefetch=2,
        grid=(1,),
        in_specs=[pl.BlockSpec(memory_space=pl.ANY)],
        out_specs=[pl.BlockSpec(piece, lambda i, o, s: (0, 0, 0, 0)) for _ in range(count)],
        scratch_shapes=[
            pltpu.VMEM((span_count * slot_cap, kv, rows, width), pool_part.dtype),
            pltpu.SemaphoreType.DMA((span_count * slot_cap,)),
        ],
    )
    nbytes = 2 * 2 * span_count * slot_cap * kv * rows * width
    return pl.pallas_call(
        functools.partial(gather_kernel, tuple(chosen_distances), slot_cap, tensor_count),
        grid_spec=grid_spec,
        out_shape=[jax.ShapeDtypeStruct(piece, pool_part.dtype) for _ in range(count)],
        cost_estimate=pl.CostEstimate(flops=0, transcendentals=0, bytes_accessed=nbytes),
    )(offsets, slots, pool_part)


def on_device(queries, suffix_kv, page_pool, offsets, slots, prefix_len):
    replicas = lax.axis_size("replica")
    tensor_count = lax.axis_size("tensor")
    reader = lax.axis_index("replica")
    me = lax.axis_index("tensor")
    span_count = min(8, replicas - 1)
    page_count = offsets.shape[1]
    slot_cap = (page_count + span_count - 1) // span_count + 1
    distances = jnp.arange(1, span_count + 1, dtype=jnp.int32)

    lead = max(range(1, span_count + 1), key=lambda d: min(d, replicas - d))
    rest = [d for d in range(1, span_count + 1) if d != lead]
    packed = pack_pages(page_pool, offsets, slots, [lead], slot_cap, tensor_count)
    if rest:
        packed = packed + pack_pages(page_pool, offsets, slots, rest, slot_cap, tensor_count)
    order = [lead] + rest
    payload = [None] * (span_count * tensor_count)
    for number, distance in enumerate(order):
        for shift in range(tensor_count):
            payload[(distance - 1) * tensor_count + shift] = packed[number * tensor_count + shift]

    arrivals = []
    for distance in range(1, span_count + 1):
        for shift in range(tensor_count):
            pairs = []
            for source in range(replicas):
                for peer in range(tensor_count):
                    target = ((source + distance) % replicas) * tensor_count + (peer + shift) % tensor_count
                    pairs.append((source * tensor_count + peer, target))
            arrivals.append(lax.ppermute(payload[(distance - 1) * tensor_count + shift], ("replica", "tensor"), pairs))

    quarter = page_pool.shape[2]
    page_rows = quarter * tensor_count
    suffix_rows = queries.shape[1]
    own_offsets = lax.dynamic_index_in_dim(offsets, reader, 0, keepdims=False)
    own_length = lax.dynamic_index_in_dim(prefix_len, reader, 0, keepdims=False)
    page_ids = jnp.arange(page_count, dtype=jnp.int32)
    earlier = (page_ids[None, :] < page_ids[:, None]).astype(jnp.int32)
    same = (own_offsets[:, None] == own_offsets[None, :]).astype(jnp.int32)
    rank = jnp.sum(same * earlier, axis=1)
    table = jnp.concatenate([own_offsets, rank]).astype(jnp.int32)
    shifts = jnp.arange(tensor_count, dtype=jnp.int32)
    row_ids = jnp.arange(quarter, dtype=jnp.int32)
    position = (
        page_ids[:, None, None] * page_rows
        + ((me - shifts + tensor_count) % tensor_count)[None, :, None] * quarter
        + row_ids[None, None, :]
    )
    visible = (position < own_length).astype(jnp.int32).reshape(page_count, 1, -1)
    result = attend(queries[0], suffix_kv[0], table, visible, arrivals, span_count, tensor_count)
    return result.reshape(1, suffix_rows, result.shape[1])


def attention_kernel(span_count, tensor_count, tab_ref, q_ref, suf_ref, vis_ref, *rest):
    chunk_refs, o_ref = rest[:-1], rest[-1]
    page_count = vis_ref.shape[0]
    rows, width = q_ref.shape
    group = HEADS // KV_HEADS
    kv_local = width // (group * HEAD_DIM)
    scale = HEAD_DIM ** (-0.5)
    dims = (((1,), (1,)), ((), ()))
    row_pos = lax.broadcasted_iota(jnp.int32, (group * rows, rows), 0) % rows
    col_pos = lax.broadcasted_iota(jnp.int32, (group * rows, rows), 1)
    causal = col_pos <= row_pos
    for head in range(kv_local):
        lanes = pl.ds(head * HEAD_DIM, HEAD_DIM)
        q_all = jnp.concatenate(
            [q_ref[:, pl.ds((head * group + g) * HEAD_DIM, HEAD_DIM)] for g in range(group)], axis=0
        )

        def page_part(page, part):
            distance, slot = tab_ref[page], tab_ref[page_count + page]
            pieces = []
            for shift in range(tensor_count):
                piece = chunk_refs[shift][slot, part, :, lanes]
                for d in range(2, span_count + 1):
                    other = chunk_refs[(d - 1) * tensor_count + shift][slot, part, :, lanes]
                    piece = jnp.where(distance == d, other, piece)
                pieces.append(piece)
            return jnp.concatenate(pieces, axis=0)

        keys = [suf_ref[0, :, lanes]]
        vals = [suf_ref[1, :, lanes]]
        masks = [causal]
        join = 2 if page_count % 2 == 0 else 1
        for page in range(0, page_count, join):
            keys.append(jnp.concatenate([page_part(p, 0) for p in range(page, page + join)], axis=0))
            vals.append(jnp.concatenate([page_part(p, 1) for p in range(page, page + join)], axis=0))
            masks.append(
                jnp.concatenate([vis_ref[p] for p in range(page, page + join)], axis=-1) > 0
            )
        scores = []
        for key, mask in zip(keys, masks):
            s = lax.dot_general(q_all, key, dims, preferred_element_type=jnp.float32)
            scores.append(jnp.where(mask, s, NEG_FILL))
        widths = sorted(set(s.shape[-1] for s in scores))
        top = None
        for width_now in widths:
            same = [s for s in scores if s.shape[-1] == width_now]
            part = functools.reduce(jnp.maximum, same)
            part = jnp.max(part, axis=-1, keepdims=True)
            top = part if top is None else jnp.maximum(top, part)
        top = top * scale
        sums = {}
        acc = None
        for s, val in zip(scores, vals):
            w = jnp.exp(s * scale - top)
            width_now = s.shape[-1]
            sums[width_now] = w if width_now not in sums else sums[width_now] + w
            pv = jnp.dot(w.astype(jnp.bfloat16), val, preferred_element_type=jnp.float32)
            acc = pv if acc is None else acc + pv
        total = None
        for width_now in widths:
            part = jnp.sum(sums[width_now], axis=-1, keepdims=True)
            total = part if total is None else total + part
        out = (acc / total).astype(o_ref.dtype)
        for g in range(group):
            o_ref[:, pl.ds((head * group + g) * HEAD_DIM, HEAD_DIM)] = out[g * rows:(g + 1) * rows]


def attend(q, suf, table, visible, chunks, span_count, tensor_count):
    rows, width = q.shape
    keys_total = suf.shape[1] + visible.shape[0] * visible.shape[2]
    flops = 4 * rows * width * keys_total
    nbytes = 2 * (q.size * 2 + suf.size + sum(c.size for c in chunks))

    def whole(a):
        return pl.BlockSpec(a.shape, lambda i, t: (0,) * a.ndim)

    grid_spec = pltpu.PrefetchScalarGridSpec(
        num_scalar_prefetch=1,
        grid=(1,),
        in_specs=[whole(q), whole(suf), whole(visible)] + [whole(c) for c in chunks],
        out_specs=pl.BlockSpec((rows, width), lambda i, t: (0, 0)),
    )
    return pl.pallas_call(
        functools.partial(attention_kernel, span_count, tensor_count),
        grid_spec=grid_spec,
        out_shape=jax.ShapeDtypeStruct((rows, width), jnp.bfloat16),
        cost_estimate=pl.CostEstimate(
            flops=flops, transcendentals=rows * (width // HEAD_DIM) * keys_total, bytes_accessed=nbytes
        ),
    )(table, q, suf, visible, *chunks)


def solution(mesh):
    in_specs = (
        P(("groups", "replica"), None, "tensor"),
        P(("groups", "replica"), None, None, "tensor"),
        P(("groups", "replica"), None, "tensor", None),
        P("groups", None),
        P("groups", None),
        P("groups"),
    )
    out_specs = P(("groups", "replica"), None, "tensor")
    return jax.shard_map(
        on_device, mesh=mesh, in_specs=in_specs, out_specs=out_specs, check_vma=False
    )
```

```python
import functools

import jax
import jax.numpy as jnp
from jax import lax
from jax.experimental import pallas as pl
from jax.experimental.pallas import tpu as pltpu
from jax.sharding import PartitionSpec as P

HEADS = 64
KV_HEADS = 8
HEAD_DIM = 128


NEG_FILL = -1e30


def slot_choice(offsets_rows, distances, slot_cap):
    matched = (offsets_rows == distances[:, None]).astype(jnp.int32)
    page_count = offsets_rows.shape[1]
    page_ids = jnp.arange(page_count, dtype=jnp.int32)
    earlier = (page_ids[None, :] < page_ids[:, None]).astype(jnp.int32)
    ranking = jnp.sum(matched[:, None, :] * earlier[None, :, :], axis=2)
    places = jnp.arange(slot_cap, dtype=jnp.int32)
    return matched[:, None, :] * (ranking[:, None, :] == places[None, :, None]).astype(jnp.int32)


def gather_kernel(first, last, slot_cap, tensor_count, off_ref, slot_ref, pool_hbm, *rest):
    out_refs, buf, sems = rest[:-2], rest[-2], rest[-1]
    replicas, page_count = off_ref.shape
    holder = lax.axis_index("replica")
    me = lax.axis_index("tensor")
    lanes = out_refs[0].shape[-1]
    starts = [
        pl.multiple_of(((me + shift) % tensor_count) * lanes, lanes) for shift in range(tensor_count)
    ]
    copies = []
    for distance in range(first, last + 1):
        reader = (holder + distance) % replicas
        chosen = [jnp.int32(0)] * slot_cap
        count = jnp.int32(0)
        for page in range(page_count):
            matched = off_ref[reader, page] == distance
            place = slot_ref[reader, page]
            chosen = [
                jnp.where(matched & (count == slot), place, chosen[slot]) for slot in range(slot_cap)
            ]
            count = count + matched.astype(jnp.int32)
        for slot in range(slot_cap):
            index = (distance - first) * slot_cap + slot
            copy = pltpu.make_async_copy(pool_hbm.at[chosen[slot]], buf.at[index], sems.at[index])
            copy.start()
            copies.append(copy)
    for copy in copies:
        copy.wait()
    for distance in range(first, last + 1):
        for slot in range(slot_cap):
            index = (distance - first) * slot_cap + slot
            for shift in range(tensor_count):
                out_refs[(distance - first) * tensor_count + shift][slot] = buf[
                    index, :, :, pl.ds(starts[shift], lanes)
                ]


def pack_pages(pool_part, offsets, slots, first, last, slot_cap, tensor_count):
    pages, kv, rows, width = pool_part.shape
    lanes = width // tensor_count
    piece = (slot_cap, kv, rows, lanes)
    span_count = last - first + 1
    count = span_count * tensor_count
    grid_spec = pltpu.PrefetchScalarGridSpec(
        num_scalar_prefetch=2,
        grid=(1,),
        in_specs=[pl.BlockSpec(memory_space=pl.ANY)],
        out_specs=[pl.BlockSpec(piece, lambda i, o, s: (0, 0, 0, 0)) for _ in range(count)],
        scratch_shapes=[
            pltpu.VMEM((span_count * slot_cap, kv, rows, width), pool_part.dtype),
            pltpu.SemaphoreType.DMA((span_count * slot_cap,)),
        ],
    )
    nbytes = 2 * 2 * span_count * slot_cap * kv * rows * width
    return pl.pallas_call(
        functools.partial(gather_kernel, first, last, slot_cap, tensor_count),
        grid_spec=grid_spec,
        out_shape=[jax.ShapeDtypeStruct(piece, pool_part.dtype) for _ in range(count)],
        cost_estimate=pl.CostEstimate(flops=0, transcendentals=0, bytes_accessed=nbytes),
    )(offsets, slots, pool_part)


def on_device(queries, suffix_kv, page_pool, offsets, slots, prefix_len):
    replicas = lax.axis_size("replica")
    tensor_count = lax.axis_size("tensor")
    reader = lax.axis_index("replica")
    me = lax.axis_index("tensor")
    span_count = min(8, replicas - 1)
    page_count = offsets.shape[1]
    slot_cap = (page_count + span_count - 1) // span_count + 1
    distances = jnp.arange(1, span_count + 1, dtype=jnp.int32)

    payload = pack_pages(page_pool, offsets, slots, 1, 1, slot_cap, tensor_count)
    if span_count > 1:
        payload = payload + pack_pages(page_pool, offsets, slots, 2, span_count, slot_cap, tensor_count)

    arrivals = []
    for distance in range(1, span_count + 1):
        for shift in range(tensor_count):
            pairs = []
            for source in range(replicas):
                for peer in range(tensor_count):
                    target = ((source + distance) % replicas) * tensor_count + (peer + shift) % tensor_count
                    pairs.append((source * tensor_count + peer, target))
            arrivals.append(lax.ppermute(payload[(distance - 1) * tensor_count + shift], ("replica", "tensor"), pairs))

    quarter = page_pool.shape[2]
    page_rows = quarter * tensor_count
    suffix_rows = queries.shape[1]
    result = attend(queries[0], suffix_kv[0], offsets, prefix_len, arrivals, span_count, tensor_count)
    return result.reshape(1, suffix_rows, result.shape[1])


def attention_kernel(span_count, tensor_count, off_ref, len_ref, q_ref, suf_ref, *rest):
    chunk_refs, o_ref = rest[:-1], rest[-1]
    replicas, page_count = off_ref.shape
    reader = lax.axis_index("replica")
    me = lax.axis_index("tensor")
    length = len_ref[reader]
    quarter = chunk_refs[0].shape[2]
    page_rows = quarter * tensor_count
    page_distance = [off_ref[reader, page] for page in range(page_count)]
    page_slot = []
    for page in range(page_count):
        rank = jnp.int32(0)
        for other in range(page):
            rank = rank + (page_distance[other] == page_distance[page]).astype(jnp.int32)
        page_slot.append(rank)
    rows, width = q_ref.shape
    group = HEADS // KV_HEADS
    kv_local = width // (group * HEAD_DIM)
    scale = HEAD_DIM ** (-0.5)
    dims = (((1,), (1,)), ((), ()))
    row_pos = lax.broadcasted_iota(jnp.int32, (group * rows, rows), 0) % rows
    col_pos = lax.broadcasted_iota(jnp.int32, (group * rows, rows), 1)
    causal = col_pos <= row_pos

    def page_mask(first, count):
        col = lax.broadcasted_iota(jnp.int32, (1, count * page_rows), 1)
        page = first + col // page_rows
        shift = (col % page_rows) // quarter
        position = page * page_rows + ((me - shift + tensor_count) % tensor_count) * quarter + col % quarter
        return position < length

    for head in range(kv_local):
        lanes = pl.ds(head * HEAD_DIM, HEAD_DIM)
        q_all = jnp.concatenate(
            [q_ref[:, pl.ds((head * group + g) * HEAD_DIM, HEAD_DIM)] for g in range(group)], axis=0
        )

        def page_part(page, part):
            distance, slot = page_distance[page], page_slot[page]
            pieces = []
            for shift in range(tensor_count):
                piece = chunk_refs[shift][slot, part, :, lanes]
                for d in range(2, span_count + 1):
                    other = chunk_refs[(d - 1) * tensor_count + shift][slot, part, :, lanes]
                    piece = jnp.where(distance == d, other, piece)
                pieces.append(piece)
            return jnp.concatenate(pieces, axis=0)

        keys = [suf_ref[0, :, lanes]]
        vals = [suf_ref[1, :, lanes]]
        masks = [causal]
        join = 2 if page_count % 2 == 0 else 1
        for page in range(0, page_count, join):
            keys.append(jnp.concatenate([page_part(p, 0) for p in range(page, page + join)], axis=0))
            vals.append(jnp.concatenate([page_part(p, 1) for p in range(page, page + join)], axis=0))
            masks.append(page_mask(page, join))
        scores = []
        for key, mask in zip(keys, masks):
            s = lax.dot_general(q_all, key, dims, preferred_element_type=jnp.float32)
            scores.append(jnp.where(mask, s, NEG_FILL))
        widths = sorted(set(s.shape[-1] for s in scores))
        top = None
        for width_now in widths:
            same = [s for s in scores if s.shape[-1] == width_now]
            part = functools.reduce(jnp.maximum, same)
            part = jnp.max(part, axis=-1, keepdims=True)
            top = part if top is None else jnp.maximum(top, part)
        top = top * scale
        sums = {}
        acc = None
        for s, val in zip(scores, vals):
            w = jnp.exp(s * scale - top)
            width_now = s.shape[-1]
            sums[width_now] = w if width_now not in sums else sums[width_now] + w
            pv = jnp.dot(w.astype(jnp.bfloat16), val, preferred_element_type=jnp.float32)
            acc = pv if acc is None else acc + pv
        total = None
        for width_now in widths:
            part = jnp.sum(sums[width_now], axis=-1, keepdims=True)
            total = part if total is None else total + part
        out = (acc / total).astype(o_ref.dtype)
        for g in range(group):
            o_ref[:, pl.ds((head * group + g) * HEAD_DIM, HEAD_DIM)] = out[g * rows:(g + 1) * rows]


def attend(q, suf, offsets, prefix_len, chunks, span_count, tensor_count):
    rows, width = q.shape
    page_count = offsets.shape[1]
    chunk_keys = chunks[0].shape[0] * chunks[0].shape[2] * tensor_count // chunks[0].shape[0]
    keys_total = suf.shape[1] + page_count * chunk_keys
    flops = 4 * rows * width * keys_total
    nbytes = 2 * (q.size * 2 + suf.size + sum(c.size for c in chunks))

    def whole(a):
        return pl.BlockSpec(a.shape, lambda i, o, n: (0,) * a.ndim)

    grid_spec = pltpu.PrefetchScalarGridSpec(
        num_scalar_prefetch=2,
        grid=(1,),
        in_specs=[whole(q), whole(suf)] + [whole(c) for c in chunks],
        out_specs=pl.BlockSpec((rows, width), lambda i, o, n: (0, 0)),
    )
    return pl.pallas_call(
        functools.partial(attention_kernel, span_count, tensor_count),
        grid_spec=grid_spec,
        out_shape=jax.ShapeDtypeStruct((rows, width), jnp.bfloat16),
        cost_estimate=pl.CostEstimate(
            flops=flops, transcendentals=rows * (width // HEAD_DIM) * keys_total, bytes_accessed=nbytes
        ),
    )(offsets, prefix_len, q, suf, *chunks)


def solution(mesh):
    in_specs = (
        P(("groups", "replica"), None, "tensor"),
        P(("groups", "replica"), None, None, "tensor"),
        P(("groups", "replica"), None, "tensor", None),
        P("groups", None),
        P("groups", None),
        P("groups"),
    )
    out_specs = P(("groups", "replica"), None, "tensor")
    return jax.shard_map(
        on_device, mesh=mesh, in_specs=in_specs, out_specs=out_specs, check_vma=False
    )
```

```python
import functools

import jax
import jax.numpy as jnp
from jax import lax
from jax.experimental import pallas as pl
from jax.experimental.pallas import tpu as pltpu
from jax.sharding import PartitionSpec as P

HEADS = 64
KV_HEADS = 8
HEAD_DIM = 128


NEG_FILL = -1e30


def slot_choice(offsets_rows, distances, slot_cap):
    matched = (offsets_rows == distances[:, None]).astype(jnp.int32)
    page_count = offsets_rows.shape[1]
    page_ids = jnp.arange(page_count, dtype=jnp.int32)
    earlier = (page_ids[None, :] < page_ids[:, None]).astype(jnp.int32)
    ranking = jnp.sum(matched[:, None, :] * earlier[None, :, :], axis=2)
    places = jnp.arange(slot_cap, dtype=jnp.int32)
    return matched[:, None, :] * (ranking[:, None, :] == places[None, :, None]).astype(jnp.int32)


def gather_kernel(first, last, slot_cap, tensor_count, off_ref, slot_ref, pool_hbm, *rest):
    out_refs, buf, sems = rest[:-2], rest[-2], rest[-1]
    replicas, page_count = off_ref.shape
    holder = lax.axis_index("replica")
    me = lax.axis_index("tensor")
    lanes = out_refs[0].shape[-1]
    pair_count = tensor_count // 2
    starts = [
        pl.multiple_of(((me // 2 + shift) % pair_count) * lanes, lanes) for shift in range(pair_count)
    ]
    copies = []
    for distance in range(first, last + 1):
        reader = (holder + distance) % replicas
        chosen = [jnp.int32(0)] * slot_cap
        count = jnp.int32(0)
        for page in range(page_count):
            matched = off_ref[reader, page] == distance
            place = slot_ref[reader, page]
            chosen = [
                jnp.where(matched & (count == slot), place, chosen[slot]) for slot in range(slot_cap)
            ]
            count = count + matched.astype(jnp.int32)
        for slot in range(slot_cap):
            index = (distance - first) * slot_cap + slot
            copy = pltpu.make_async_copy(pool_hbm.at[chosen[slot]], buf.at[index], sems.at[index])
            copy.start()
            copies.append(copy)
    for copy in copies:
        copy.wait()
    for distance in range(first, last + 1):
        for slot in range(slot_cap):
            index = (distance - first) * slot_cap + slot
            for shift in range(pair_count):
                out_refs[(distance - first) * pair_count + shift][slot] = buf[
                    index, :, :, pl.ds(starts[shift], lanes)
                ]


def pack_pages(pool_part, offsets, slots, first, last, slot_cap, tensor_count):
    pages, kv, rows, width = pool_part.shape
    lanes = 2 * width // tensor_count
    piece = (slot_cap, kv, rows, lanes)
    span_count = last - first + 1
    count = span_count * (tensor_count // 2)
    grid_spec = pltpu.PrefetchScalarGridSpec(
        num_scalar_prefetch=2,
        grid=(1,),
        in_specs=[pl.BlockSpec(memory_space=pl.ANY)],
        out_specs=[pl.BlockSpec(piece, lambda i, o, s: (0, 0, 0, 0)) for _ in range(count)],
        scratch_shapes=[
            pltpu.VMEM((span_count * slot_cap, kv, rows, width), pool_part.dtype),
            pltpu.SemaphoreType.DMA((span_count * slot_cap,)),
        ],
    )
    nbytes = 2 * 2 * span_count * slot_cap * kv * rows * width
    return pl.pallas_call(
        functools.partial(gather_kernel, first, last, slot_cap, tensor_count),
        grid_spec=grid_spec,
        out_shape=[jax.ShapeDtypeStruct(piece, pool_part.dtype) for _ in range(count)],
        cost_estimate=pl.CostEstimate(flops=0, transcendentals=0, bytes_accessed=nbytes),
    )(offsets, slots, pool_part)


def on_device(queries, suffix_kv, page_pool, offsets, slots, prefix_len):
    replicas = lax.axis_size("replica")
    tensor_count = lax.axis_size("tensor")
    reader = lax.axis_index("replica")
    me = lax.axis_index("tensor")
    span_count = min(8, replicas - 1)
    page_count = offsets.shape[1]
    slot_cap = (page_count + span_count - 1) // span_count + 1
    distances = jnp.arange(1, span_count + 1, dtype=jnp.int32)

    payload = pack_pages(page_pool, offsets, slots, 1, 1, slot_cap, tensor_count)
    if span_count > 1:
        payload = payload + pack_pages(page_pool, offsets, slots, 2, span_count, slot_cap, tensor_count)

    pair_count = tensor_count // 2
    arrivals = []
    for distance in range(1, span_count + 1):
        for shift in range(pair_count):
            pairs = []
            for source in range(replicas):
                for peer in range(tensor_count):
                    lead = ((peer // 2 + shift) % pair_count) * 2 + peer % 2
                    target = ((source + distance) % replicas) * tensor_count + lead
                    pairs.append((source * tensor_count + peer, target))
            arrivals.append(lax.ppermute(payload[(distance - 1) * pair_count + shift], ("replica", "tensor"), pairs))
    swap = [(peer, peer ^ 1) for peer in range(tensor_count)]
    arrivals = arrivals + [lax.ppermute(a, "tensor", swap) for a in arrivals]

    suffix_rows = queries.shape[1]
    result = attend(queries[0], suffix_kv[0], offsets, prefix_len, arrivals, span_count, tensor_count)
    return result.reshape(1, suffix_rows, result.shape[1])


def attention_kernel(span_count, tensor_count, off_ref, len_ref, q_ref, suf_ref, *rest):
    chunk_refs, o_ref = rest[:-1], rest[-1]
    replicas, page_count = off_ref.shape
    reader = lax.axis_index("replica")
    me = lax.axis_index("tensor")
    length = len_ref[reader]
    quarter = chunk_refs[0].shape[2]
    page_rows = quarter * tensor_count
    page_distance = [off_ref[reader, page] for page in range(page_count)]
    page_slot = []
    for page in range(page_count):
        rank = jnp.int32(0)
        for other in range(page):
            rank = rank + (page_distance[other] == page_distance[page]).astype(jnp.int32)
        page_slot.append(rank)
    rows, width = q_ref.shape
    group = HEADS // KV_HEADS
    kv_local = width // (group * HEAD_DIM)
    scale = HEAD_DIM ** (-0.5)
    dims = (((1,), (1,)), ((), ()))
    row_pos = lax.broadcasted_iota(jnp.int32, (group * rows, rows), 0) % rows
    col_pos = lax.broadcasted_iota(jnp.int32, (group * rows, rows), 1)
    causal = col_pos <= row_pos

    pair_count = tensor_count // 2
    pair, side = me // 2, me % 2
    piece_quarter = []
    for shift in range(pair_count):
        source_pair = (pair - shift + pair_count) % pair_count
        piece_quarter += [source_pair * 2 + side, source_pair * 2 + 1 - side]

    def page_mask(first, count):
        col = lax.broadcasted_iota(jnp.int32, (1, count * page_rows), 1)
        page = first + col // page_rows
        piece = (col % page_rows) // quarter
        own_quarter = jnp.zeros_like(col)
        for number, value in enumerate(piece_quarter):
            own_quarter = jnp.where(piece == number, value, own_quarter)
        position = page * page_rows + own_quarter * quarter + col % quarter
        return position < length

    half = span_count * pair_count
    for head in range(kv_local):
        lanes = pl.ds(pl.multiple_of(side * kv_local * HEAD_DIM + head * HEAD_DIM, HEAD_DIM), HEAD_DIM)
        q_all = jnp.concatenate(
            [q_ref[:, pl.ds((head * group + g) * HEAD_DIM, HEAD_DIM)] for g in range(group)], axis=0
        )

        def page_part(page, part):
            distance, slot = page_distance[page], page_slot[page]
            pieces = []
            for shift in range(pair_count):
                for origin in (0, half):
                    piece = chunk_refs[origin + shift][slot, part, :, lanes]
                    for d in range(2, span_count + 1):
                        other = chunk_refs[origin + (d - 1) * pair_count + shift][slot, part, :, lanes]
                        piece = jnp.where(distance == d, other, piece)
                    pieces.append(piece)
            return jnp.concatenate(pieces, axis=0)

        suffix_lanes = pl.ds(head * HEAD_DIM, HEAD_DIM)
        keys = [suf_ref[0, :, suffix_lanes]]
        vals = [suf_ref[1, :, suffix_lanes]]
        masks = [causal]
        join = 2 if page_count % 2 == 0 else 1
        for page in range(0, page_count, join):
            keys.append(jnp.concatenate([page_part(p, 0) for p in range(page, page + join)], axis=0))
            vals.append(jnp.concatenate([page_part(p, 1) for p in range(page, page + join)], axis=0))
            masks.append(page_mask(page, join))
        scores = []
        for key, mask in zip(keys, masks):
            s = lax.dot_general(q_all, key, dims, preferred_element_type=jnp.float32)
            scores.append(jnp.where(mask, s, NEG_FILL))
        widths = sorted(set(s.shape[-1] for s in scores))
        top = None
        for width_now in widths:
            same = [s for s in scores if s.shape[-1] == width_now]
            part = functools.reduce(jnp.maximum, same)
            part = jnp.max(part, axis=-1, keepdims=True)
            top = part if top is None else jnp.maximum(top, part)
        top = top * scale
        sums = {}
        acc = None
        for s, val in zip(scores, vals):
            w = jnp.exp(s * scale - top)
            width_now = s.shape[-1]
            sums[width_now] = w if width_now not in sums else sums[width_now] + w
            pv = jnp.dot(w.astype(jnp.bfloat16), val, preferred_element_type=jnp.float32)
            acc = pv if acc is None else acc + pv
        total = None
        for width_now in widths:
            part = jnp.sum(sums[width_now], axis=-1, keepdims=True)
            total = part if total is None else total + part
        out = (acc / total).astype(o_ref.dtype)
        for g in range(group):
            o_ref[:, pl.ds((head * group + g) * HEAD_DIM, HEAD_DIM)] = out[g * rows:(g + 1) * rows]


def attend(q, suf, offsets, prefix_len, chunks, span_count, tensor_count):
    rows, width = q.shape
    page_count = offsets.shape[1]
    chunk_keys = chunks[0].shape[2] * tensor_count
    keys_total = suf.shape[1] + page_count * chunk_keys
    flops = 4 * rows * width * keys_total
    nbytes = 2 * (q.size * 2 + suf.size + sum(c.size for c in chunks))

    def whole(a):
        return pl.BlockSpec(a.shape, lambda i, o, n: (0,) * a.ndim)

    grid_spec = pltpu.PrefetchScalarGridSpec(
        num_scalar_prefetch=2,
        grid=(1,),
        in_specs=[whole(q), whole(suf)] + [whole(c) for c in chunks],
        out_specs=pl.BlockSpec((rows, width), lambda i, o, n: (0, 0)),
    )
    return pl.pallas_call(
        functools.partial(attention_kernel, span_count, tensor_count),
        grid_spec=grid_spec,
        out_shape=jax.ShapeDtypeStruct((rows, width), jnp.bfloat16),
        cost_estimate=pl.CostEstimate(
            flops=flops, transcendentals=rows * (width // HEAD_DIM) * keys_total, bytes_accessed=nbytes
        ),
    )(offsets, prefix_len, q, suf, *chunks)


def solution(mesh):
    in_specs = (
        P(("groups", "replica"), None, "tensor"),
        P(("groups", "replica"), None, None, "tensor"),
        P(("groups", "replica"), None, "tensor", None),
        P("groups", None),
        P("groups", None),
        P("groups"),
    )
    out_specs = P(("groups", "replica"), None, "tensor")
    return jax.shard_map(
        on_device, mesh=mesh, in_specs=in_specs, out_specs=out_specs, check_vma=False
    )
```

```python
import functools

import jax
import jax.numpy as jnp
from jax import lax
from jax.experimental import pallas as pl
from jax.experimental.pallas import tpu as pltpu
from jax.sharding import PartitionSpec as P

HEADS = 64
KV_HEADS = 8
HEAD_DIM = 128


NEG_FILL = -1e30


def slot_choice(offsets_rows, distances, slot_cap):
    matched = (offsets_rows == distances[:, None]).astype(jnp.int32)
    page_count = offsets_rows.shape[1]
    page_ids = jnp.arange(page_count, dtype=jnp.int32)
    earlier = (page_ids[None, :] < page_ids[:, None]).astype(jnp.int32)
    ranking = jnp.sum(matched[:, None, :] * earlier[None, :, :], axis=2)
    places = jnp.arange(slot_cap, dtype=jnp.int32)
    return matched[:, None, :] * (ranking[:, None, :] == places[None, :, None]).astype(jnp.int32)


def gather_kernel(first, last, slot_cap, tensor_count, off_ref, slot_ref, pool_hbm, *rest):
    out_refs, buf, sems = rest[:-2], rest[-2], rest[-1]
    replicas, page_count = off_ref.shape
    holder = lax.axis_index("replica")
    me = lax.axis_index("tensor")
    lanes = out_refs[0].shape[-1]
    starts = [
        pl.multiple_of(((me + shift) % tensor_count) * lanes, lanes) for shift in range(tensor_count)
    ]
    copies = []
    for distance in range(first, last + 1):
        reader = (holder + distance) % replicas
        chosen = [jnp.int32(0)] * slot_cap
        count = jnp.int32(0)
        for page in range(page_count):
            matched = off_ref[reader, page] == distance
            place = slot_ref[reader, page]
            chosen = [
                jnp.where(matched & (count == slot), place, chosen[slot]) for slot in range(slot_cap)
            ]
            count = count + matched.astype(jnp.int32)
        for slot in range(slot_cap):
            index = (distance - first) * slot_cap + slot
            copy = pltpu.make_async_copy(pool_hbm.at[chosen[slot]], buf.at[index], sems.at[index])
            copy.start()
            copies.append(copy)
    for copy in copies:
        copy.wait()
    for distance in range(first, last + 1):
        for slot in range(slot_cap):
            index = (distance - first) * slot_cap + slot
            for shift in range(tensor_count):
                out_refs[(distance - first) * tensor_count + shift][slot] = buf[
                    index, :, :, pl.ds(starts[shift], lanes)
                ]


def pack_pages(pool_part, offsets, slots, first, last, slot_cap, tensor_count):
    pages, kv, rows, width = pool_part.shape
    lanes = width // tensor_count
    piece = (slot_cap, kv, rows, lanes)
    span_count = last - first + 1
    count = span_count * tensor_count
    grid_spec = pltpu.PrefetchScalarGridSpec(
        num_scalar_prefetch=2,
        grid=(1,),
        in_specs=[pl.BlockSpec(memory_space=pl.ANY)],
        out_specs=[pl.BlockSpec(piece, lambda i, o, s: (0, 0, 0, 0)) for _ in range(count)],
        scratch_shapes=[
            pltpu.VMEM((span_count * slot_cap, kv, rows, width), pool_part.dtype),
            pltpu.SemaphoreType.DMA((span_count * slot_cap,)),
        ],
    )
    nbytes = 2 * 2 * span_count * slot_cap * kv * rows * width
    return pl.pallas_call(
        functools.partial(gather_kernel, first, last, slot_cap, tensor_count),
        grid_spec=grid_spec,
        out_shape=[jax.ShapeDtypeStruct(piece, pool_part.dtype) for _ in range(count)],
        cost_estimate=pl.CostEstimate(flops=0, transcendentals=0, bytes_accessed=nbytes),
    )(offsets, slots, pool_part)


def on_device(queries, suffix_kv, page_pool, offsets, slots, prefix_len):
    replicas = lax.axis_size("replica")
    tensor_count = lax.axis_size("tensor")
    reader = lax.axis_index("replica")
    me = lax.axis_index("tensor")
    span_count = min(8, replicas - 1)
    page_count = offsets.shape[1]
    slot_cap = (page_count + span_count - 1) // span_count + 1
    distances = jnp.arange(1, span_count + 1, dtype=jnp.int32)

    payload = pack_pages(page_pool, offsets, slots, 1, 1, slot_cap, tensor_count)
    if span_count > 1:
        payload = payload + pack_pages(page_pool, offsets, slots, 2, span_count, slot_cap, tensor_count)

    arrivals = []
    for distance in range(1, span_count + 1):
        for shift in range(tensor_count):
            pairs = []
            for source in range(replicas):
                for peer in range(tensor_count):
                    target = ((source + distance) % replicas) * tensor_count + (peer + shift) % tensor_count
                    pairs.append((source * tensor_count + peer, target))
            arrivals.append(lax.ppermute(payload[(distance - 1) * tensor_count + shift], ("replica", "tensor"), pairs))

    quarter = page_pool.shape[2]
    page_rows = quarter * tensor_count
    suffix_rows = queries.shape[1]
    result = attend(queries[0], suffix_kv[0], offsets, prefix_len, arrivals, span_count, tensor_count)
    return result.reshape(1, suffix_rows, result.shape[1])


def attention_kernel(span_count, tensor_count, off_ref, len_ref, q_ref, suf_ref, *rest):
    chunk_refs, o_ref = rest[:-1], rest[-1]
    replicas, page_count = off_ref.shape
    reader = lax.axis_index("replica")
    me = lax.axis_index("tensor")
    length = len_ref[reader]
    quarter = chunk_refs[0].shape[2]
    page_rows = quarter * tensor_count
    page_distance = [off_ref[reader, page] for page in range(page_count)]
    page_slot = []
    for page in range(page_count):
        rank = jnp.int32(0)
        for other in range(page):
            rank = rank + (page_distance[other] == page_distance[page]).astype(jnp.int32)
        page_slot.append(rank)
    rows, width = q_ref.shape
    group = HEADS // KV_HEADS
    kv_local = width // (group * HEAD_DIM)
    scale = HEAD_DIM ** (-0.5)
    dims = (((1,), (1,)), ((), ()))
    row_pos = lax.broadcasted_iota(jnp.int32, (group * rows, rows), 0) % rows
    col_pos = lax.broadcasted_iota(jnp.int32, (group * rows, rows), 1)
    causal = col_pos <= row_pos

    def page_mask(first, count):
        col = lax.broadcasted_iota(jnp.int32, (1, count * page_rows), 1)
        page = first + col // page_rows
        shift = (col % page_rows) // quarter
        position = page * page_rows + ((me - shift + tensor_count) % tensor_count) * quarter + col % quarter
        return position < length

    for head in range(kv_local):
        lanes = pl.ds(head * HEAD_DIM, HEAD_DIM)
        q_all = jnp.concatenate(
            [q_ref[:, pl.ds((head * group + g) * HEAD_DIM, HEAD_DIM)] for g in range(group)], axis=0
        )

        def page_part(page, part):
            distance, slot = page_distance[page], page_slot[page]
            pieces = []
            for shift in range(tensor_count):
                piece = chunk_refs[shift][slot, part, :, lanes]
                for d in range(2, span_count + 1):
                    other = chunk_refs[(d - 1) * tensor_count + shift][slot, part, :, lanes]
                    piece = jnp.where(distance == d, other, piece)
                pieces.append(piece)
            return jnp.concatenate(pieces, axis=0)

        keys = [suf_ref[0, :, lanes]]
        vals = [suf_ref[1, :, lanes]]
        masks = [causal]
        join = 4 if page_count % 4 == 0 else (2 if page_count % 2 == 0 else 1)
        for page in range(0, page_count, join):
            keys.append(jnp.concatenate([page_part(p, 0) for p in range(page, page + join)], axis=0))
            vals.append(jnp.concatenate([page_part(p, 1) for p in range(page, page + join)], axis=0))
            masks.append(page_mask(page, join))
        scores = []
        for key, mask in zip(keys, masks):
            s = lax.dot_general(q_all, key, dims, preferred_element_type=jnp.float32)
            scores.append(jnp.where(mask, s, NEG_FILL))
        widths = sorted(set(s.shape[-1] for s in scores))
        top = None
        for width_now in widths:
            same = [s for s in scores if s.shape[-1] == width_now]
            part = functools.reduce(jnp.maximum, same)
            part = jnp.max(part, axis=-1, keepdims=True)
            top = part if top is None else jnp.maximum(top, part)
        top = top * scale
        sums = {}
        acc = None
        for s, val in zip(scores, vals):
            w = jnp.exp(s * scale - top)
            width_now = s.shape[-1]
            sums[width_now] = w if width_now not in sums else sums[width_now] + w
            pv = jnp.dot(w.astype(jnp.bfloat16), val, preferred_element_type=jnp.float32)
            acc = pv if acc is None else acc + pv
        total = None
        for width_now in widths:
            part = jnp.sum(sums[width_now], axis=-1, keepdims=True)
            total = part if total is None else total + part
        out = (acc / total).astype(o_ref.dtype)
        for g in range(group):
            o_ref[:, pl.ds((head * group + g) * HEAD_DIM, HEAD_DIM)] = out[g * rows:(g + 1) * rows]


def attend(q, suf, offsets, prefix_len, chunks, span_count, tensor_count):
    rows, width = q.shape
    page_count = offsets.shape[1]
    chunk_keys = chunks[0].shape[0] * chunks[0].shape[2] * tensor_count // chunks[0].shape[0]
    keys_total = suf.shape[1] + page_count * chunk_keys
    flops = 4 * rows * width * keys_total
    nbytes = 2 * (q.size * 2 + suf.size + sum(c.size for c in chunks))

    def whole(a):
        return pl.BlockSpec(a.shape, lambda i, o, n: (0,) * a.ndim)

    grid_spec = pltpu.PrefetchScalarGridSpec(
        num_scalar_prefetch=2,
        grid=(1,),
        in_specs=[whole(q), whole(suf)] + [whole(c) for c in chunks],
        out_specs=pl.BlockSpec((rows, width), lambda i, o, n: (0, 0)),
    )
    return pl.pallas_call(
        functools.partial(attention_kernel, span_count, tensor_count),
        grid_spec=grid_spec,
        out_shape=jax.ShapeDtypeStruct((rows, width), jnp.bfloat16),
        cost_estimate=pl.CostEstimate(
            flops=flops, transcendentals=rows * (width // HEAD_DIM) * keys_total, bytes_accessed=nbytes
        ),
    )(offsets, prefix_len, q, suf, *chunks)


def solution(mesh):
    in_specs = (
        P(("groups", "replica"), None, "tensor"),
        P(("groups", "replica"), None, None, "tensor"),
        P(("groups", "replica"), None, "tensor", None),
        P("groups", None),
        P("groups", None),
        P("groups"),
    )
    out_specs = P(("groups", "replica"), None, "tensor")
    return jax.shard_map(
        on_device, mesh=mesh, in_specs=in_specs, out_specs=out_specs, check_vma=False
    )
```

```python
import functools

import jax
import jax.numpy as jnp
from jax import lax
from jax.experimental import pallas as pl
from jax.experimental.pallas import tpu as pltpu
from jax.sharding import PartitionSpec as P

HEADS = 64
KV_HEADS = 8
HEAD_DIM = 128


NEG_FILL = -1e30


def slot_choice(offsets_rows, distances, slot_cap):
    matched = (offsets_rows == distances[:, None]).astype(jnp.int32)
    page_count = offsets_rows.shape[1]
    page_ids = jnp.arange(page_count, dtype=jnp.int32)
    earlier = (page_ids[None, :] < page_ids[:, None]).astype(jnp.int32)
    ranking = jnp.sum(matched[:, None, :] * earlier[None, :, :], axis=2)
    places = jnp.arange(slot_cap, dtype=jnp.int32)
    return matched[:, None, :] * (ranking[:, None, :] == places[None, :, None]).astype(jnp.int32)


def gather_kernel(first, last, slot_cap, tensor_count, off_ref, slot_ref, pool_hbm, *rest):
    out_refs, buf, sems = rest[:-2], rest[-2], rest[-1]
    replicas, page_count = off_ref.shape
    holder = lax.axis_index("replica")
    me = lax.axis_index("tensor")
    lanes = out_refs[0].shape[-1]
    starts = [
        pl.multiple_of(((me + shift) % tensor_count) * lanes, lanes) for shift in range(tensor_count)
    ]
    copies = []
    for distance in range(first, last + 1):
        reader = (holder + distance) % replicas
        chosen = [jnp.int32(0)] * slot_cap
        count = jnp.int32(0)
        for page in range(page_count):
            matched = off_ref[reader, page] == distance
            place = slot_ref[reader, page]
            chosen = [
                jnp.where(matched & (count == slot), place, chosen[slot]) for slot in range(slot_cap)
            ]
            count = count + matched.astype(jnp.int32)
        for slot in range(slot_cap):
            index = (distance - first) * slot_cap + slot
            copy = pltpu.make_async_copy(pool_hbm.at[chosen[slot]], buf.at[index], sems.at[index])
            copy.start()
            copies.append(copy)
    for copy in copies:
        copy.wait()
    for distance in range(first, last + 1):
        for slot in range(slot_cap):
            index = (distance - first) * slot_cap + slot
            for shift in range(tensor_count):
                out_refs[(distance - first) * tensor_count + shift][slot] = buf[
                    index, :, :, pl.ds(starts[shift], lanes)
                ]


def pack_pages(pool_part, offsets, slots, first, last, slot_cap, tensor_count):
    pages, kv, rows, width = pool_part.shape
    lanes = width // tensor_count
    piece = (slot_cap, kv, rows, lanes)
    span_count = last - first + 1
    count = span_count * tensor_count
    grid_spec = pltpu.PrefetchScalarGridSpec(
        num_scalar_prefetch=2,
        grid=(1,),
        in_specs=[pl.BlockSpec(memory_space=pl.ANY)],
        out_specs=[pl.BlockSpec(piece, lambda i, o, s: (0, 0, 0, 0)) for _ in range(count)],
        scratch_shapes=[
            pltpu.VMEM((span_count * slot_cap, kv, rows, width), pool_part.dtype),
            pltpu.SemaphoreType.DMA((span_count * slot_cap,)),
        ],
    )
    nbytes = 2 * 2 * span_count * slot_cap * kv * rows * width
    return pl.pallas_call(
        functools.partial(gather_kernel, first, last, slot_cap, tensor_count),
        grid_spec=grid_spec,
        out_shape=[jax.ShapeDtypeStruct(piece, pool_part.dtype) for _ in range(count)],
        cost_estimate=pl.CostEstimate(flops=0, transcendentals=0, bytes_accessed=nbytes),
    )(offsets, slots, pool_part)


def on_device(queries, suffix_kv, page_pool, offsets, slots, prefix_len):
    replicas = lax.axis_size("replica")
    tensor_count = lax.axis_size("tensor")
    reader = lax.axis_index("replica")
    me = lax.axis_index("tensor")
    span_count = min(8, replicas - 1)
    page_count = offsets.shape[1]
    slot_cap = (page_count + span_count - 1) // span_count + 1
    distances = jnp.arange(1, span_count + 1, dtype=jnp.int32)

    payload = pack_pages(page_pool, offsets, slots, 1, 1, slot_cap, tensor_count)
    if span_count > 1:
        payload = payload + pack_pages(page_pool, offsets, slots, 2, span_count, slot_cap, tensor_count)

    arrivals = []
    for distance in range(1, span_count + 1):
        for shift in range(tensor_count):
            pairs = []
            for source in range(replicas):
                for peer in range(tensor_count):
                    target = ((source + distance) % replicas) * tensor_count + (peer + shift) % tensor_count
                    pairs.append((source * tensor_count + peer, target))
            arrivals.append(lax.ppermute(payload[(distance - 1) * tensor_count + shift], ("replica", "tensor"), pairs))

    quarter = page_pool.shape[2]
    page_rows = quarter * tensor_count
    suffix_rows = queries.shape[1]
    result = attend(queries[0], suffix_kv[0], offsets, prefix_len, arrivals, span_count, tensor_count)
    return result.reshape(1, suffix_rows, result.shape[1])


def attention_kernel(span_count, tensor_count, off_ref, len_ref, q_ref, suf_ref, *rest):
    chunk_refs, o_ref = rest[:-1], rest[-1]
    replicas, page_count = off_ref.shape
    reader = lax.axis_index("replica")
    me = lax.axis_index("tensor")
    length = len_ref[reader]
    quarter = chunk_refs[0].shape[2]
    page_rows = quarter * tensor_count
    page_distance = [off_ref[reader, page] for page in range(page_count)]
    page_slot = []
    for page in range(page_count):
        rank = jnp.int32(0)
        for other in range(page):
            rank = rank + (page_distance[other] == page_distance[page]).astype(jnp.int32)
        page_slot.append(rank)
    rows, width = q_ref.shape
    group = HEADS // KV_HEADS
    kv_local = width // (group * HEAD_DIM)
    scale = HEAD_DIM ** (-0.5)
    dims = (((1,), (1,)), ((), ()))
    row_pos = lax.broadcasted_iota(jnp.int32, (group * rows, rows), 0) % rows
    col_pos = lax.broadcasted_iota(jnp.int32, (group * rows, rows), 1)
    causal = col_pos <= row_pos

    def page_mask(first, count):
        col = lax.broadcasted_iota(jnp.int32, (1, count * page_rows), 1)
        page = first + col // page_rows
        shift = (col % page_rows) // quarter
        position = page * page_rows + ((me - shift + tensor_count) % tensor_count) * quarter + col % quarter
        return position < length

    for head in range(kv_local):
        lanes = pl.ds(head * HEAD_DIM, HEAD_DIM)
        q_all = jnp.concatenate(
            [q_ref[:, pl.ds((head * group + g) * HEAD_DIM, HEAD_DIM)] for g in range(group)], axis=0
        )

        def page_part(page, part):
            distance, slot = page_distance[page], page_slot[page]
            pieces = []
            for shift in range(tensor_count):
                piece = chunk_refs[shift][slot, part, :, lanes]
                for d in range(2, span_count + 1):
                    other = chunk_refs[(d - 1) * tensor_count + shift][slot, part, :, lanes]
                    piece = jnp.where(distance == d, other, piece)
                pieces.append(piece)
            return jnp.concatenate(pieces, axis=0)

        keys = [suf_ref[0, :, lanes]]
        vals = [suf_ref[1, :, lanes]]
        masks = [causal]
        join = page_count
        for page in range(0, page_count, join):
            keys.append(jnp.concatenate([page_part(p, 0) for p in range(page, page + join)], axis=0))
            vals.append(jnp.concatenate([page_part(p, 1) for p in range(page, page + join)], axis=0))
            masks.append(page_mask(page, join))
        scores = []
        for key, mask in zip(keys, masks):
            s = lax.dot_general(q_all, key, dims, preferred_element_type=jnp.float32)
            scores.append(jnp.where(mask, s, NEG_FILL))
        widths = sorted(set(s.shape[-1] for s in scores))
        top = None
        for width_now in widths:
            same = [s for s in scores if s.shape[-1] == width_now]
            part = functools.reduce(jnp.maximum, same)
            part = jnp.max(part, axis=-1, keepdims=True)
            top = part if top is None else jnp.maximum(top, part)
        top = top * scale
        sums = {}
        acc = None
        for s, val in zip(scores, vals):
            w = jnp.exp(s * scale - top)
            width_now = s.shape[-1]
            sums[width_now] = w if width_now not in sums else sums[width_now] + w
            pv = jnp.dot(w.astype(jnp.bfloat16), val, preferred_element_type=jnp.float32)
            acc = pv if acc is None else acc + pv
        total = None
        for width_now in widths:
            part = jnp.sum(sums[width_now], axis=-1, keepdims=True)
            total = part if total is None else total + part
        out = (acc / total).astype(o_ref.dtype)
        for g in range(group):
            o_ref[:, pl.ds((head * group + g) * HEAD_DIM, HEAD_DIM)] = out[g * rows:(g + 1) * rows]


def attend(q, suf, offsets, prefix_len, chunks, span_count, tensor_count):
    rows, width = q.shape
    page_count = offsets.shape[1]
    chunk_keys = chunks[0].shape[0] * chunks[0].shape[2] * tensor_count // chunks[0].shape[0]
    keys_total = suf.shape[1] + page_count * chunk_keys
    flops = 4 * rows * width * keys_total
    nbytes = 2 * (q.size * 2 + suf.size + sum(c.size for c in chunks))

    def whole(a):
        return pl.BlockSpec(a.shape, lambda i, o, n: (0,) * a.ndim)

    grid_spec = pltpu.PrefetchScalarGridSpec(
        num_scalar_prefetch=2,
        grid=(1,),
        in_specs=[whole(q), whole(suf)] + [whole(c) for c in chunks],
        out_specs=pl.BlockSpec((rows, width), lambda i, o, n: (0, 0)),
    )
    return pl.pallas_call(
        functools.partial(attention_kernel, span_count, tensor_count),
        grid_spec=grid_spec,
        out_shape=jax.ShapeDtypeStruct((rows, width), jnp.bfloat16),
        cost_estimate=pl.CostEstimate(
            flops=flops, transcendentals=rows * (width // HEAD_DIM) * keys_total, bytes_accessed=nbytes
        ),
    )(offsets, prefix_len, q, suf, *chunks)


def solution(mesh):
    in_specs = (
        P(("groups", "replica"), None, "tensor"),
        P(("groups", "replica"), None, None, "tensor"),
        P(("groups", "replica"), None, "tensor", None),
        P("groups", None),
        P("groups", None),
        P("groups"),
    )
    out_specs = P(("groups", "replica"), None, "tensor")
    return jax.shard_map(
        on_device, mesh=mesh, in_specs=in_specs, out_specs=out_specs, check_vma=False
    )
```

```python
import functools

import jax
import jax.numpy as jnp
from jax import lax
from jax.experimental import pallas as pl
from jax.experimental.pallas import tpu as pltpu
from jax.sharding import PartitionSpec as P

HEADS = 64
KV_HEADS = 8
HEAD_DIM = 128


NEG_FILL = -1e30


def slot_choice(offsets_rows, distances, slot_cap):
    matched = (offsets_rows == distances[:, None]).astype(jnp.int32)
    page_count = offsets_rows.shape[1]
    page_ids = jnp.arange(page_count, dtype=jnp.int32)
    earlier = (page_ids[None, :] < page_ids[:, None]).astype(jnp.int32)
    ranking = jnp.sum(matched[:, None, :] * earlier[None, :, :], axis=2)
    places = jnp.arange(slot_cap, dtype=jnp.int32)
    return matched[:, None, :] * (ranking[:, None, :] == places[None, :, None]).astype(jnp.int32)


def gather_kernel(first, last, slot_cap, tensor_count, off_ref, slot_ref, pool_hbm, *rest):
    out_refs, buf, sems = rest[:-2], rest[-2], rest[-1]
    replicas, page_count = off_ref.shape
    holder = lax.axis_index("replica")
    me = lax.axis_index("tensor")
    lanes = out_refs[0].shape[-1]
    starts = [
        pl.multiple_of(((me + shift) % tensor_count) * lanes, lanes) for shift in range(tensor_count)
    ]
    copies = []
    for distance in range(first, last + 1):
        reader = (holder + distance) % replicas
        chosen = [jnp.int32(0)] * slot_cap
        count = jnp.int32(0)
        for page in range(page_count):
            matched = off_ref[reader, page] == distance
            place = slot_ref[reader, page]
            chosen = [
                jnp.where(matched & (count == slot), place, chosen[slot]) for slot in range(slot_cap)
            ]
            count = count + matched.astype(jnp.int32)
        for slot in range(slot_cap):
            index = (distance - first) * slot_cap + slot
            copy = pltpu.make_async_copy(pool_hbm.at[chosen[slot]], buf.at[index], sems.at[index])
            copy.start()
            copies.append(copy)
    for copy in copies:
        copy.wait()
    for distance in range(first, last + 1):
        for slot in range(slot_cap):
            index = (distance - first) * slot_cap + slot
            for shift in range(tensor_count):
                out_refs[(distance - first) * tensor_count + shift][slot] = buf[
                    index, :, :, pl.ds(starts[shift], lanes)
                ]


def pack_pages(pool_part, offsets, slots, first, last, slot_cap, tensor_count):
    pages, kv, rows, width = pool_part.shape
    lanes = width // tensor_count
    piece = (slot_cap, kv, rows, lanes)
    span_count = last - first + 1
    count = span_count * tensor_count
    grid_spec = pltpu.PrefetchScalarGridSpec(
        num_scalar_prefetch=2,
        grid=(1,),
        in_specs=[pl.BlockSpec(memory_space=pl.ANY)],
        out_specs=[pl.BlockSpec(piece, lambda i, o, s: (0, 0, 0, 0)) for _ in range(count)],
        scratch_shapes=[
            pltpu.VMEM((span_count * slot_cap, kv, rows, width), pool_part.dtype),
            pltpu.SemaphoreType.DMA((span_count * slot_cap,)),
        ],
    )
    nbytes = 2 * 2 * span_count * slot_cap * kv * rows * width
    return pl.pallas_call(
        functools.partial(gather_kernel, first, last, slot_cap, tensor_count),
        grid_spec=grid_spec,
        out_shape=[jax.ShapeDtypeStruct(piece, pool_part.dtype) for _ in range(count)],
        cost_estimate=pl.CostEstimate(flops=0, transcendentals=0, bytes_accessed=nbytes),
    )(offsets, slots, pool_part)


def on_device(queries, suffix_kv, page_pool, offsets, slots, prefix_len):
    replicas = lax.axis_size("replica")
    tensor_count = lax.axis_size("tensor")
    reader = lax.axis_index("replica")
    me = lax.axis_index("tensor")
    span_count = min(8, replicas - 1)
    page_count = offsets.shape[1]
    slot_cap = (page_count + span_count - 1) // span_count + 1
    distances = jnp.arange(1, span_count + 1, dtype=jnp.int32)

    payload = pack_pages(page_pool, offsets, slots, 1, 1, slot_cap, tensor_count)
    if span_count > 1:
        payload = payload + pack_pages(page_pool, offsets, slots, 2, span_count, slot_cap, tensor_count)

    arrivals = []
    for distance in range(1, span_count + 1):
        for shift in range(tensor_count):
            pairs = []
            for source in range(replicas):
                for peer in range(tensor_count):
                    target = ((source + distance) % replicas) * tensor_count + (peer + shift) % tensor_count
                    pairs.append((source * tensor_count + peer, target))
            arrivals.append(lax.ppermute(payload[(distance - 1) * tensor_count + shift], ("replica", "tensor"), pairs))

    quarter = page_pool.shape[2]
    page_rows = quarter * tensor_count
    suffix_rows = queries.shape[1]
    result = attend(queries[0], suffix_kv[0], offsets, prefix_len, arrivals, span_count, tensor_count)
    return result.reshape(1, suffix_rows, result.shape[1])


def attention_kernel(span_count, tensor_count, off_ref, len_ref, q_ref, suf_ref, *rest):
    chunk_refs, o_ref = rest[:-1], rest[-1]
    replicas, page_count = off_ref.shape
    reader = lax.axis_index("replica")
    me = lax.axis_index("tensor")
    length = len_ref[reader]
    quarter = chunk_refs[0].shape[2]
    page_rows = quarter * tensor_count
    page_distance = [off_ref[reader, page] for page in range(page_count)]
    page_slot = []
    for page in range(page_count):
        rank = jnp.int32(0)
        for other in range(page):
            rank = rank + (page_distance[other] == page_distance[page]).astype(jnp.int32)
        page_slot.append(rank)
    rows, width = q_ref.shape
    group = HEADS // KV_HEADS
    kv_local = width // (group * HEAD_DIM)
    scale = HEAD_DIM ** (-0.5)
    dims = (((1,), (1,)), ((), ()))
    row_pos = lax.broadcasted_iota(jnp.int32, (group * rows, rows), 0) % rows
    col_pos = lax.broadcasted_iota(jnp.int32, (group * rows, rows), 1)
    causal = col_pos <= row_pos

    def page_mask(first, count):
        col = lax.broadcasted_iota(jnp.int32, (1, count * page_rows), 1)
        page = first + col // page_rows
        shift = (col % page_rows) // quarter
        position = page * page_rows + ((me - shift + tensor_count) % tensor_count) * quarter + col % quarter
        return position < length

    for head in range(kv_local):
        lanes = pl.ds(head * HEAD_DIM, HEAD_DIM)
        q_all = jnp.concatenate(
            [q_ref[:, pl.ds((head * group + g) * HEAD_DIM, HEAD_DIM)] for g in range(group)], axis=0
        )

        def page_part(page, part):
            distance, slot = page_distance[page], page_slot[page]
            pieces = []
            for shift in range(tensor_count):
                piece = chunk_refs[shift][slot, part, :, lanes]
                for d in range(2, span_count + 1):
                    other = chunk_refs[(d - 1) * tensor_count + shift][slot, part, :, lanes]
                    piece = jnp.where(distance == d, other, piece)
                pieces.append(piece)
            return jnp.concatenate(pieces, axis=0)

        keys = [suf_ref[0, :, lanes]]
        vals = [suf_ref[1, :, lanes]]
        masks = [causal]
        join = 4 if page_count % 4 == 0 else (2 if page_count % 2 == 0 else 1)
        for page in range(0, page_count, join):
            keys.append(jnp.concatenate([page_part(p, 0) for p in range(page, page + join)], axis=0))
            vals.append(jnp.concatenate([page_part(p, 1) for p in range(page, page + join)], axis=0))
            masks.append(page_mask(page, join))
        keys = keys[1:-1] + [jnp.concatenate([keys[-1], keys[0]], axis=0)]
        vals = vals[1:-1] + [jnp.concatenate([vals[-1], vals[0]], axis=0)]
        last_mask = jnp.broadcast_to(masks[-1], (causal.shape[0], masks[-1].shape[1]))
        masks = masks[1:-1] + [jnp.concatenate([last_mask, causal], axis=1)]
        scores = []
        for key, mask in zip(keys, masks):
            s = lax.dot_general(q_all, key, dims, preferred_element_type=jnp.float32)
            scores.append(jnp.where(mask, s, NEG_FILL))
        widths = sorted(set(s.shape[-1] for s in scores))
        top = None
        for width_now in widths:
            same = [s for s in scores if s.shape[-1] == width_now]
            part = functools.reduce(jnp.maximum, same)
            part = jnp.max(part, axis=-1, keepdims=True)
            top = part if top is None else jnp.maximum(top, part)
        top = top * scale
        sums = {}
        acc = None
        for s, val in zip(scores, vals):
            w = jnp.exp(s * scale - top)
            width_now = s.shape[-1]
            sums[width_now] = w if width_now not in sums else sums[width_now] + w
            pv = jnp.dot(w.astype(jnp.bfloat16), val, preferred_element_type=jnp.float32)
            acc = pv if acc is None else acc + pv
        total = None
        for width_now in widths:
            part = jnp.sum(sums[width_now], axis=-1, keepdims=True)
            total = part if total is None else total + part
        out = (acc / total).astype(o_ref.dtype)
        for g in range(group):
            o_ref[:, pl.ds((head * group + g) * HEAD_DIM, HEAD_DIM)] = out[g * rows:(g + 1) * rows]


def attend(q, suf, offsets, prefix_len, chunks, span_count, tensor_count):
    rows, width = q.shape
    page_count = offsets.shape[1]
    chunk_keys = chunks[0].shape[0] * chunks[0].shape[2] * tensor_count // chunks[0].shape[0]
    keys_total = suf.shape[1] + page_count * chunk_keys
    flops = 4 * rows * width * keys_total
    nbytes = 2 * (q.size * 2 + suf.size + sum(c.size for c in chunks))

    def whole(a):
        return pl.BlockSpec(a.shape, lambda i, o, n: (0,) * a.ndim)

    grid_spec = pltpu.PrefetchScalarGridSpec(
        num_scalar_prefetch=2,
        grid=(1,),
        in_specs=[whole(q), whole(suf)] + [whole(c) for c in chunks],
        out_specs=pl.BlockSpec((rows, width), lambda i, o, n: (0, 0)),
    )
    return pl.pallas_call(
        functools.partial(attention_kernel, span_count, tensor_count),
        grid_spec=grid_spec,
        out_shape=jax.ShapeDtypeStruct((rows, width), jnp.bfloat16),
        cost_estimate=pl.CostEstimate(
            flops=flops, transcendentals=rows * (width // HEAD_DIM) * keys_total, bytes_accessed=nbytes
        ),
    )(offsets, prefix_len, q, suf, *chunks)


def solution(mesh):
    in_specs = (
        P(("groups", "replica"), None, "tensor"),
        P(("groups", "replica"), None, None, "tensor"),
        P(("groups", "replica"), None, "tensor", None),
        P("groups", None),
        P("groups", None),
        P("groups"),
    )
    out_specs = P(("groups", "replica"), None, "tensor")
    return jax.shard_map(
        on_device, mesh=mesh, in_specs=in_specs, out_specs=out_specs, check_vma=False
    )
```

```python
import functools

import jax
import jax.numpy as jnp
from jax import lax
from jax.experimental import pallas as pl
from jax.experimental.pallas import tpu as pltpu
from jax.sharding import PartitionSpec as P

HEADS = 64
KV_HEADS = 8
HEAD_DIM = 128


NEG_FILL = -1e30


def slot_choice(offsets_rows, distances, slot_cap):
    matched = (offsets_rows == distances[:, None]).astype(jnp.int32)
    page_count = offsets_rows.shape[1]
    page_ids = jnp.arange(page_count, dtype=jnp.int32)
    earlier = (page_ids[None, :] < page_ids[:, None]).astype(jnp.int32)
    ranking = jnp.sum(matched[:, None, :] * earlier[None, :, :], axis=2)
    places = jnp.arange(slot_cap, dtype=jnp.int32)
    return matched[:, None, :] * (ranking[:, None, :] == places[None, :, None]).astype(jnp.int32)


def gather_kernel(first, last, slot_cap, tensor_count, off_ref, slot_ref, pool_hbm, *rest):
    out_refs, buf, sems = rest[:-2], rest[-2], rest[-1]
    replicas, page_count = off_ref.shape
    holder = lax.axis_index("replica")
    me = lax.axis_index("tensor")
    lanes = out_refs[0].shape[-1]
    starts = [
        pl.multiple_of(((me + shift) % tensor_count) * lanes, lanes) for shift in range(tensor_count)
    ]
    copies = []
    for distance in range(first, last + 1):
        reader = (holder + distance) % replicas
        chosen = [jnp.int32(0)] * slot_cap
        count = jnp.int32(0)
        for page in range(page_count):
            matched = off_ref[reader, page] == distance
            place = slot_ref[reader, page]
            chosen = [
                jnp.where(matched & (count == slot), place, chosen[slot]) for slot in range(slot_cap)
            ]
            count = count + matched.astype(jnp.int32)
        for slot in range(slot_cap):
            index = (distance - first) * slot_cap + slot
            copy = pltpu.make_async_copy(pool_hbm.at[chosen[slot]], buf.at[index], sems.at[index])
            copy.start()
            copies.append(copy)
    for copy in copies:
        copy.wait()
    for distance in range(first, last + 1):
        for slot in range(slot_cap):
            index = (distance - first) * slot_cap + slot
            for shift in range(tensor_count):
                out_refs[(distance - first) * tensor_count + shift][slot] = buf[
                    index, :, :, pl.ds(starts[shift], lanes)
                ]


def pack_pages(pool_part, offsets, slots, first, last, slot_cap, tensor_count):
    pages, kv, rows, width = pool_part.shape
    lanes = width // tensor_count
    piece = (slot_cap, kv, rows, lanes)
    span_count = last - first + 1
    count = span_count * tensor_count
    grid_spec = pltpu.PrefetchScalarGridSpec(
        num_scalar_prefetch=2,
        grid=(1,),
        in_specs=[pl.BlockSpec(memory_space=pl.ANY)],
        out_specs=[pl.BlockSpec(piece, lambda i, o, s: (0, 0, 0, 0)) for _ in range(count)],
        scratch_shapes=[
            pltpu.VMEM((span_count * slot_cap, kv, rows, width), pool_part.dtype),
            pltpu.SemaphoreType.DMA((span_count * slot_cap,)),
        ],
    )
    nbytes = 2 * 2 * span_count * slot_cap * kv * rows * width
    return pl.pallas_call(
        functools.partial(gather_kernel, first, last, slot_cap, tensor_count),
        grid_spec=grid_spec,
        out_shape=[jax.ShapeDtypeStruct(piece, pool_part.dtype) for _ in range(count)],
        cost_estimate=pl.CostEstimate(flops=0, transcendentals=0, bytes_accessed=nbytes),
    )(offsets, slots, pool_part)


def on_device(queries, suffix_kv, page_pool, offsets, slots, prefix_len):
    replicas = lax.axis_size("replica")
    tensor_count = lax.axis_size("tensor")
    reader = lax.axis_index("replica")
    me = lax.axis_index("tensor")
    span_count = min(8, replicas - 1)
    page_count = offsets.shape[1]
    slot_cap = (page_count + span_count - 1) // span_count + 1
    distances = jnp.arange(1, span_count + 1, dtype=jnp.int32)

    lead = min(2, span_count)
    payload = pack_pages(page_pool, offsets, slots, 1, lead, slot_cap, tensor_count)
    if span_count > lead:
        payload = payload + pack_pages(page_pool, offsets, slots, lead + 1, span_count, slot_cap, tensor_count)

    arrivals = []
    for distance in range(1, span_count + 1):
        for shift in range(tensor_count):
            pairs = []
            for source in range(replicas):
                for peer in range(tensor_count):
                    target = ((source + distance) % replicas) * tensor_count + (peer + shift) % tensor_count
                    pairs.append((source * tensor_count + peer, target))
            arrivals.append(lax.ppermute(payload[(distance - 1) * tensor_count + shift], ("replica", "tensor"), pairs))

    quarter = page_pool.shape[2]
    page_rows = quarter * tensor_count
    suffix_rows = queries.shape[1]
    result = attend(queries[0], suffix_kv[0], offsets, prefix_len, arrivals, span_count, tensor_count)
    return result.reshape(1, suffix_rows, result.shape[1])


def attention_kernel(span_count, tensor_count, off_ref, len_ref, q_ref, suf_ref, *rest):
    chunk_refs, o_ref = rest[:-1], rest[-1]
    replicas, page_count = off_ref.shape
    reader = lax.axis_index("replica")
    me = lax.axis_index("tensor")
    length = len_ref[reader]
    quarter = chunk_refs[0].shape[2]
    page_rows = quarter * tensor_count
    page_distance = [off_ref[reader, page] for page in range(page_count)]
    page_slot = []
    for page in range(page_count):
        rank = jnp.int32(0)
        for other in range(page):
            rank = rank + (page_distance[other] == page_distance[page]).astype(jnp.int32)
        page_slot.append(rank)
    rows, width = q_ref.shape
    group = HEADS // KV_HEADS
    kv_local = width // (group * HEAD_DIM)
    scale = HEAD_DIM ** (-0.5)
    dims = (((1,), (1,)), ((), ()))
    row_pos = lax.broadcasted_iota(jnp.int32, (group * rows, rows), 0) % rows
    col_pos = lax.broadcasted_iota(jnp.int32, (group * rows, rows), 1)
    causal = col_pos <= row_pos

    def page_mask(first, count):
        col = lax.broadcasted_iota(jnp.int32, (1, count * page_rows), 1)
        page = first + col // page_rows
        shift = (col % page_rows) // quarter
        position = page * page_rows + ((me - shift + tensor_count) % tensor_count) * quarter + col % quarter
        return position < length

    for head in range(kv_local):
        lanes = pl.ds(head * HEAD_DIM, HEAD_DIM)
        q_all = jnp.concatenate(
            [q_ref[:, pl.ds((head * group + g) * HEAD_DIM, HEAD_DIM)] for g in range(group)], axis=0
        )

        def page_part(page, part):
            distance, slot = page_distance[page], page_slot[page]
            pieces = []
            for shift in range(tensor_count):
                piece = chunk_refs[shift][slot, part, :, lanes]
                for d in range(2, span_count + 1):
                    other = chunk_refs[(d - 1) * tensor_count + shift][slot, part, :, lanes]
                    piece = jnp.where(distance == d, other, piece)
                pieces.append(piece)
            return jnp.concatenate(pieces, axis=0)

        keys = [suf_ref[0, :, lanes]]
        vals = [suf_ref[1, :, lanes]]
        masks = [causal]
        join = 4 if page_count % 4 == 0 else (2 if page_count % 2 == 0 else 1)
        for page in range(0, page_count, join):
            keys.append(jnp.concatenate([page_part(p, 0) for p in range(page, page + join)], axis=0))
            vals.append(jnp.concatenate([page_part(p, 1) for p in range(page, page + join)], axis=0))
            masks.append(page_mask(page, join))
        keys = keys[1:-1] + [jnp.concatenate([keys[-1], keys[0]], axis=0)]
        vals = vals[1:-1] + [jnp.concatenate([vals[-1], vals[0]], axis=0)]
        last_mask = jnp.broadcast_to(masks[-1], (causal.shape[0], masks[-1].shape[1]))
        masks = masks[1:-1] + [jnp.concatenate([last_mask, causal], axis=1)]
        scores = []
        for key, mask in zip(keys, masks):
            s = lax.dot_general(q_all, key, dims, preferred_element_type=jnp.float32)
            scores.append(jnp.where(mask, s, NEG_FILL))
        widths = sorted(set(s.shape[-1] for s in scores))
        top = None
        for width_now in widths:
            same = [s for s in scores if s.shape[-1] == width_now]
            part = functools.reduce(jnp.maximum, same)
            part = jnp.max(part, axis=-1, keepdims=True)
            top = part if top is None else jnp.maximum(top, part)
        top = top * scale
        sums = {}
        acc = None
        for s, val in zip(scores, vals):
            w = jnp.exp(s * scale - top)
            width_now = s.shape[-1]
            sums[width_now] = w if width_now not in sums else sums[width_now] + w
            pv = jnp.dot(w.astype(jnp.bfloat16), val, preferred_element_type=jnp.float32)
            acc = pv if acc is None else acc + pv
        total = None
        for width_now in widths:
            part = jnp.sum(sums[width_now], axis=-1, keepdims=True)
            total = part if total is None else total + part
        out = (acc / total).astype(o_ref.dtype)
        for g in range(group):
            o_ref[:, pl.ds((head * group + g) * HEAD_DIM, HEAD_DIM)] = out[g * rows:(g + 1) * rows]


def attend(q, suf, offsets, prefix_len, chunks, span_count, tensor_count):
    rows, width = q.shape
    page_count = offsets.shape[1]
    chunk_keys = chunks[0].shape[0] * chunks[0].shape[2] * tensor_count // chunks[0].shape[0]
    keys_total = suf.shape[1] + page_count * chunk_keys
    flops = 4 * rows * width * keys_total
    nbytes = 2 * (q.size * 2 + suf.size + sum(c.size for c in chunks))

    def whole(a):
        return pl.BlockSpec(a.shape, lambda i, o, n: (0,) * a.ndim)

    grid_spec = pltpu.PrefetchScalarGridSpec(
        num_scalar_prefetch=2,
        grid=(1,),
        in_specs=[whole(q), whole(suf)] + [whole(c) for c in chunks],
        out_specs=pl.BlockSpec((rows, width), lambda i, o, n: (0, 0)),
    )
    return pl.pallas_call(
        functools.partial(attention_kernel, span_count, tensor_count),
        grid_spec=grid_spec,
        out_shape=jax.ShapeDtypeStruct((rows, width), jnp.bfloat16),
        cost_estimate=pl.CostEstimate(
            flops=flops, transcendentals=rows * (width // HEAD_DIM) * keys_total, bytes_accessed=nbytes
        ),
    )(offsets, prefix_len, q, suf, *chunks)


def solution(mesh):
    in_specs = (
        P(("groups", "replica"), None, "tensor"),
        P(("groups", "replica"), None, None, "tensor"),
        P(("groups", "replica"), None, "tensor", None),
        P("groups", None),
        P("groups", None),
        P("groups"),
    )
    out_specs = P(("groups", "replica"), None, "tensor")
    return jax.shard_map(
        on_device, mesh=mesh, in_specs=in_specs, out_specs=out_specs, check_vma=False
    )
```
